32 devices in a mesh: fsdp: 4 (over y, x), seq: 8 (over z, core).
Axes of the slice: x: 2, y: 2, z: 4, core: 2. Of those that a mesh axis runs over, the one named last changes fastest.
Arguments:
- events: bfloat16 [4, 1024, 2048], P('fsdp', 'seq'), may hold values from -6 to 6
- type_ids: int32 [4, 1024], P('fsdp', 'seq'), may hold values from 0 to 255
- type_table: bfloat16 [256, 2048], P('fsdp'), may hold values from -6 to 6
- norm_gain: float32 [2048], replicated, may hold values from 0.25 to 1.75
- kernel: bfloat16 [2048, 1152], P('fsdp'), may hold values from -0.1875 to 0.1875
- upstream: bfloat16 [4, 1024, 2048], P('fsdp', 'seq'), may hold values from -6 to 6
Outputs:
- input_grad: bfloat16 [4, 1024, 2048], P('fsdp', 'seq')
- table_grad: float32 [256, 2048], P(('fsdp', 'seq'))
- gain_grad: float32 [2048], P(('fsdp', 'seq'))
- kernel_grad: float32 [2048, 1152], P('seq')
The draws below stay inside these ranges and needn't reach their ends.
All inputs are finite; a program needn't handle non-finite values.
Results may differ from the reference program's by a relative error of at most 0.0053.
Values may be sent and summed in bfloat16 or wider, within the bound.
No kernel may reach another device: no remote copies, remote signals or barrier semaphores. Data moves between devices by JAX's collectives and lax.ppermute only.
A program may use at most 128 MiB of HBM per device.

```python
import math
import jax
import jax.numpy as jnp
import numpy as np
from jax import lax

D = 2048
GROUPS = 16
CG = 128
KERNEL = 9
TYPES = 256
STREAMS = 4
LENGTH = 1024


def place_ends(values, own_key, least, largest):
    extent = values.shape
    spot = [jax.random.randint(jax.random.fold_in(own_key, axis), (), 0, extent[axis]) for axis in range(len(extent))]
    values = values.at[tuple(spot)].set(least)
    longest = extent.index(max(extent))
    spot[longest] = (spot[longest] + 1) % extent[longest]
    return values.at[tuple(spot)].set(largest)


def with_spikes(drawn, key, source, target, blocks, factor):
    def block_of(dim):
        return (jnp.arange(drawn.shape[dim]) // (drawn.shape[dim] // blocks)).reshape((-1,) + (1,) * (drawn.ndim - 1 - dim))

    first = jax.random.permutation(key, blocks)[block_of(target)]
    other_side = (block_of(target) + blocks // 2) % blocks
    return jnp.where((block_of(source) == first) | (block_of(source) == other_side), factor * drawn, drawn)


def levels(stream_key, dims, split, least, largest):
    gain = 1.0
    for dim, shards_of in split:
        steps = jax.random.uniform(jax.random.fold_in(jax.random.fold_in(stream_key, 6), dim), (shards_of,), jnp.float32, least / len(split), largest / len(split))
        gain = gain * jnp.repeat(jnp.exp(steps), dims[dim] // shards_of).reshape((-1,) + (1,) * (len(dims) - 1 - dim))
    return gain


def rank_table(amount, skew):
    weights = [(1 << 20) // math.isqrt(grade ** skew) + 1 for grade in range(1, amount + 1)]
    spread = 1 + sum(weights) // (1 << 30)
    return np.cumsum(np.array([max(1, weight // spread) for weight in weights]))


def ranked(stream_key, shape, count, slope):
    grid = rank_table(count, slope)
    ticket = jax.random.randint(jax.random.fold_in(stream_key, 1), shape, 0, int(grid[count - 1]))
    rank = jnp.searchsorted(jnp.asarray(grid, jnp.int32), ticket, side="right")
    return jax.random.permutation(jax.random.fold_in(stream_key, 2), count)[rank].astype(jnp.int32)


def centred(key, shape, scale, most, shards=(), kind=jnp.bfloat16):
    values = scale * jax.random.normal(key, shape, jnp.float32)
    if shards:
        values = values * levels(key, shape, shards, -0.22, 0.18)
    return jnp.clip(values, -most, most).astype(kind)


def bell_draw_with(own_key, shape, spread, limit, cuts, heavy, dtype=jnp.bfloat16):
    entries = spread * jax.random.normal(own_key, shape, jnp.float32)
    if cuts:
        entries = entries * levels(own_key, shape, cuts, -0.22, 0.18)
    return jnp.clip(with_spikes(entries, jax.random.fold_in(own_key, 3), *heavy), -limit, limit).astype(dtype)


def setup_inputs(seed: int = 0) -> dict:
    splits = jax.random.split(jax.random.key(seed), 7)
    return {
        "events": centred(splits[0], (STREAMS, LENGTH, D), 1.0, 6.0, ((0, 4), (1, 8))),
        "type_ids": place_ends(ranked(splits[1], (STREAMS, LENGTH), TYPES, 2), jax.random.fold_in(splits[1], 3), 0, TYPES - 1).astype(jnp.int32),
        "type_table": centred(splits[2], (TYPES, D), 1.0, 6.0, ((0, 4),)),
        "norm_gain": jnp.clip(1.0 + 0.15 * jax.random.normal(splits[3], (D,), jnp.float32), 0.25, 1.75),
        "kernel": centred(splits[4], (D, KERNEL * CG), (KERNEL * CG) ** -0.5, 0.1875, ((0, 4),)),
        "upstream": bell_draw_with(splits[5], (STREAMS, LENGTH, D), 1.0, 6.0, ((0, 4), (1, 8)), (1, 2, 8, 2.0)),
    }


def stream_terms(events_row, ids_row, type_table, norm_gain, kernel, upstream_row):
    length = events_row.shape[0]
    width = events_row.shape[1]
    chans = width // GROUPS
    half = KERNEL // 2
    mixed = events_row.astype(jnp.float32) + type_table[ids_row].astype(jnp.float32)
    inv = lax.rsqrt(lax.optimization_barrier(jnp.mean(mixed * mixed, axis=-1, keepdims=True)) + 1e-06)
    normed = (mixed * inv * norm_gain).astype(jnp.bfloat16)
    padded = jnp.pad(normed, ((half, half), (0, 0))).astype(jnp.float32).reshape(length + 2 * half, GROUPS, chans)
    weights = kernel.astype(jnp.float32).reshape(GROUPS, chans, KERNEL, chans)
    conv = jnp.zeros((length, GROUPS, chans), jnp.float32)
    for k in range(KERNEL):
        conv = conv + jnp.einsum('tgc,goc->tgo', padded[k:k + length], weights[:, :, k, :], precision=lax.Precision.HIGHEST)
    up = upstream_row.astype(jnp.float32).reshape(length, GROUPS, chans)
    sig = jax.nn.sigmoid(conv)
    dconv = (up * sig * (1.0 + conv * (1.0 - sig))).astype(jnp.bfloat16).astype(jnp.float32)
    dpad = jnp.pad(dconv, ((half, half), (0, 0), (0, 0)))
    dnormed = jnp.zeros((length, GROUPS, chans), jnp.float32)
    kterms = []
    for k in range(KERNEL):
        dnormed = dnormed + jnp.einsum('tgo,goc->tgc', dpad[2 * half - k:2 * half - k + length], weights[:, :, k, :], precision=lax.Precision.HIGHEST)
        kterms.append(jnp.einsum('tgo,tgc->goc', dconv, padded[k:k + length], precision=lax.Precision.HIGHEST))
    kernel_term = jnp.stack(kterms, axis=2).reshape(width, KERNEL * chans)
    dnormed = dnormed.reshape(length, width)
    gain_term = lax.optimization_barrier(jnp.sum(dnormed * mixed * inv, axis=0))
    scaled = norm_gain * dnormed
    dmixed = inv * scaled - mixed * inv * inv * inv * lax.optimization_barrier(jnp.mean(scaled * mixed, axis=-1, keepdims=True))
    input_grad = (upstream_row.astype(jnp.float32) + dmixed).astype(jnp.bfloat16)
    table_term = jax.ops.segment_sum(input_grad.astype(jnp.float32), ids_row, num_segments=TYPES)
    return (input_grad, kernel_term, gain_term, table_term)

def reference(events, type_ids, type_table, norm_gain, kernel, upstream):
    width = events.shape[2]
    scale = 1.0 / jnp.sqrt(jnp.float32(STREAMS * LENGTH))

    def step(carry, inputs):
        grad_rows, kernel_term, gain_term, table_term = stream_terms(inputs[0], inputs[1], type_table, norm_gain, kernel, inputs[2])
        return ((carry[0] + kernel_term, carry[1] + table_term, carry[2] + gain_term), grad_rows)
    start = (jnp.zeros(kernel.shape, jnp.float32), jnp.zeros((TYPES, width), jnp.float32), jnp.zeros((width,), jnp.float32))
    sums, input_grad = lax.scan(step, start, (events, type_ids, upstream))
    return (input_grad, sums[1] * scale, sums[2] * scale, sums[0] * scale)
```

```python
import jax
import jax.numpy as jnp
from jax import lax
from jax.sharding import PartitionSpec as P

GROUPS = 16
KERNEL = 9


def with_halo(cells, sides, width):
    for axis, dim in sides:
        count = lax.axis_size(axis)
        ends = count - 1
        head = lax.slice_in_dim(cells, 0, width, axis=dim)
        tail = lax.slice_in_dim(cells, cells.shape[dim] - width, cells.shape[dim], axis=dim)
        cells = jnp.concatenate(
            [
                lax.ppermute(tail, axis, [(i, (i + 1) % count) for i in range(ends)]),
                cells,
                lax.ppermute(head, axis, [((i + 1) % count, i) for i in range(ends)]),
            ],
            axis=dim,
        )
    return cells


def from_partner(value, axis, apart):
    mask = 2**apart
    pairs = [(source, source ^ mask) for source in range(lax.axis_size(axis))]
    return lax.ppermute(value, axis, pairs)


def gather_rows(block, axis):
    count = lax.axis_size(axis)
    return lax.all_to_all(jnp.tile(block, (count, 1)), axis, 0, 0, tiled=True)


def sum_rows(block, axis):
    count = lax.axis_size(axis)
    parts = block.reshape(count, block.shape[0] // count, *block.shape[1:])
    return lax.all_to_all(parts, axis, 0, 0, tiled=True).sum(axis=0)


def psum_rows(block, axis):
    return gather_rows(sum_rows(block, axis), axis)


def scatter_terms(table_term, gain_term):
    fsdp = lax.axis_size("fsdp")
    seq = lax.axis_size("seq")
    types, width = table_term.shape
    wide = width // fsdp
    gain_rows = jnp.zeros((fsdp, 1, width), jnp.float32).at[:, 0, :wide].set(gain_term.reshape(fsdp, wide))
    first = jnp.concatenate([table_term.reshape(fsdp, types // fsdp, width), gain_rows], axis=1)
    first = lax.all_to_all(first, "fsdp", 0, 0, tiled=True).sum(axis=0)
    rows = types // fsdp
    narrow = wide // seq
    gain_rows = jnp.zeros((seq, 1, width), jnp.float32).at[:, 0, :narrow].set(first[rows, :wide].reshape(seq, narrow))
    second = jnp.concatenate([first[:rows].reshape(seq, rows // seq, width), gain_rows], axis=1)
    second = lax.all_to_all(second, "seq", 0, 0, tiled=True).sum(axis=0)
    return second[: rows // seq], second[rows // seq, :narrow]


def body(events, type_ids, type_table, norm_gain, kernel, upstream):
    length = events.shape[1]
    width = events.shape[2]
    chans = width // GROUPS
    half = KERNEL // 2
    seq_count = lax.axis_size("seq")
    total = length * seq_count * lax.axis_size("fsdp")
    scale = 1.0 / jnp.sqrt(jnp.float32(total))
    table = gather_rows(type_table, "fsdp")
    onehot = (type_ids[0][:, None] == jnp.arange(table.shape[0], dtype=jnp.int32)[None, :]).astype(
        jnp.bfloat16
    )
    mixed = events[0].astype(jnp.float32) + jnp.dot(
        onehot, table, preferred_element_type=jnp.float32
    )
    inv = lax.rsqrt(jnp.mean(mixed * mixed, axis=-1, keepdims=True) + 1e-06)
    normed = (mixed * inv * norm_gain).astype(jnp.bfloat16)
    padded = with_halo(normed, (("seq", 0),), half)
    padded = padded.reshape(length + 2 * half, GROUPS, chans)
    weights = lax.all_gather(kernel, "fsdp", axis=0, tiled=True).reshape(
        GROUPS, chans, KERNEL, chans
    )
    conv = jnp.zeros((length, GROUPS, chans), jnp.float32)
    for k in range(KERNEL):
        conv = conv + jnp.einsum(
            "tgc,goc->tgo",
            padded[k : k + length],
            weights[:, :, k, :],
            preferred_element_type=jnp.float32,
        )
    up_float = upstream[0].astype(jnp.float32)
    sig = jax.nn.sigmoid(conv)
    dconv = (up_float.reshape(length, GROUPS, chans) * sig * (1.0 + conv * (1.0 - sig))).astype(
        jnp.bfloat16
    )
    dflat = dconv.reshape(length, width)
    dpad = with_halo(dflat, (("seq", 0),), half)
    dpad = dpad.reshape(length + 2 * half, GROUPS, chans)
    dnormed = jnp.zeros((length, GROUPS, chans), jnp.float32)
    for k in range(KERNEL):
        dnormed = dnormed + jnp.einsum(
            "tgo,goc->tgc",
            dpad[2 * half - k : 2 * half - k + length],
            weights[:, :, k, :],
            preferred_element_type=jnp.float32,
        )
    slice_width = width // seq_count
    normed_slice, dconv_slice = (
        lax.all_to_all(normed, "seq", split_axis=1, concat_axis=0, tiled=True),
        lax.all_to_all(dflat, "seq", split_axis=1, concat_axis=0, tiled=True),
    )
    whole = normed_slice.shape[0]
    if slice_width < chans:
        spread = chans // slice_width
        position = lax.axis_index("seq")
        group_rows = normed_slice
        for bit in range(spread.bit_length() - 1):
            partner = from_partner(group_rows, "seq", bit)
            lower = position >> bit & 1 == 0
            group_rows = jnp.where(
                lower,
                jnp.concatenate([group_rows, partner], axis=1),
                jnp.concatenate([partner, group_rows], axis=1),
            )
        group_in = group_rows.reshape(whole, 1, chans)
        group_out = dconv_slice.reshape(whole, 1, slice_width)
    else:
        local_groups = slice_width // chans
        group_in = normed_slice.reshape(whole, local_groups, chans)
        group_out = dconv_slice.reshape(whole, local_groups, chans)
    group_pad = jnp.pad(group_in, ((half, half), (0, 0), (0, 0)))
    kterms = []
    for k in range(KERNEL):
        kterms.append(
            jnp.einsum(
                "tgo,tgc->goc",
                group_out,
                group_pad[k : k + whole],
                preferred_element_type=jnp.float32,
            )
        )
    kernel_part = jnp.stack(kterms, axis=2).reshape(slice_width, KERNEL * chans) * scale
    kernel_grad = psum_rows(kernel_part, "fsdp")
    dnormed = dnormed.reshape(length, width)
    gain_term = jnp.sum(dnormed * mixed * inv, axis=0) * scale
    scaled = norm_gain * dnormed
    dmixed = inv * scaled - mixed * inv * inv * inv * jnp.mean(
        scaled * mixed, axis=-1, keepdims=True
    )
    input_grad = (up_float + dmixed).astype(jnp.bfloat16)
    table_term = (
        lax.dot_general(
            onehot, input_grad, (((0,), (0,)), ((), ())), preferred_element_type=jnp.float32
        )
        * scale
    )
    table_grad, gain_grad = scatter_terms(table_term, gain_term)
    return (input_grad[None], table_grad, gain_grad, kernel_grad)


def solution(mesh):
    return jax.shard_map(
        body,
        mesh=mesh,
        in_specs=(
            P("fsdp", "seq", None),
            P("fsdp", "seq"),
            P("fsdp", None),
            P(),
            P("fsdp", None),
            P("fsdp", "seq", None),
        ),
        out_specs=(
            P("fsdp", "seq", None),
            P(("fsdp", "seq"), None),
            P(("fsdp", "seq")),
            P("seq", None),
        ),
        check_vma=False,
    )
```

```python
import jax
import jax.numpy as jnp
from jax import lax
from jax.sharding import PartitionSpec as P

GROUPS = 16
KERNEL = 9


def with_halo(cells, axis, dim, width):
    count = lax.axis_size(axis)
    ends = count - 1
    head = lax.slice_in_dim(cells, 0, width, axis=dim)
    tail = lax.slice_in_dim(cells, cells.shape[dim] - width, cells.shape[dim], axis=dim)
    return jnp.concatenate(
        [
            lax.ppermute(tail, axis, [(i, (i + 1) % count) for i in range(ends)]),
            cells,
            lax.ppermute(head, axis, [((i + 1) % count, i) for i in range(ends)]),
        ],
        axis=dim,
    )


def from_partner(value, axis, apart):
    mask = 2**apart
    pairs = [(source, source ^ mask) for source in range(lax.axis_size(axis))]
    return lax.ppermute(value, axis, pairs)


def gather_rows(block, axis):
    count = lax.axis_size(axis)
    return lax.all_to_all(jnp.tile(block, (count,) + (1,) * (block.ndim - 1)), axis, 0, 0, tiled=True)


def conv_forward(padded, weights, length):
    chans = padded.shape[-1]
    total = None
    for k in range(KERNEL):
        term = jnp.einsum(
            "gtc,goc->gto",
            padded[:, k : k + length],
            weights[:, :, k * chans : (k + 1) * chans],
            preferred_element_type=jnp.float32,
        )
        total = term if total is None else total + term
    return total


def conv_backward(dpad, weights, length):
    chans = weights.shape[-1] // KERNEL
    half = KERNEL // 2
    total = None
    for k in range(KERNEL):
        term = jnp.einsum(
            "gto,goc->gtc",
            dpad[:, 2 * half - k : 2 * half - k + length],
            weights[:, :, k * chans : (k + 1) * chans],
            preferred_element_type=jnp.float32,
        )
        total = term if total is None else total + term
    return total


def spread_groups(normed, dflat, chans):
    normed_slice = lax.all_to_all(normed, "seq", 1, 0, tiled=True)
    dconv_slice = lax.all_to_all(dflat, "seq", 1, 0, tiled=True)
    whole, slice_width = normed_slice.shape
    spread = chans // slice_width
    position = lax.axis_index("seq")
    group_rows = normed_slice
    for bit in range(spread.bit_length() - 1):
        partner = from_partner(group_rows, "seq", bit)
        lower = position >> bit & 1 == 0
        group_rows = jnp.where(
            lower,
            jnp.concatenate([group_rows, partner], axis=1),
            jnp.concatenate([partner, group_rows], axis=1),
        )
    return group_rows.reshape(1, whole, chans), dconv_slice.reshape(1, whole, slice_width)


def body(events, type_ids, type_table, norm_gain, kernel, upstream):
    length = events.shape[1]
    width = events.shape[2]
    chans = width // GROUPS
    half = KERNEL // 2
    fsdp = lax.axis_size("fsdp")
    seq_count = lax.axis_size("seq")
    total = length * seq_count * fsdp
    scale = 1.0 / jnp.sqrt(jnp.float32(total))
    table = gather_rows(type_table, "fsdp")
    types = table.shape[0]
    onehot = (type_ids[0][:, None] == jnp.arange(types, dtype=jnp.int32)[None, :]).astype(jnp.bfloat16)
    mixed = events[0].astype(jnp.float32) + jnp.dot(onehot, table, preferred_element_type=jnp.float32)
    inv = lax.rsqrt(jnp.mean(mixed * mixed, axis=-1, keepdims=True) + 1e-06)
    normed = (mixed * inv * norm_gain).astype(jnp.bfloat16)
    normed_g = normed.reshape(length, GROUPS, chans).transpose(1, 0, 2)
    padded = with_halo(normed_g, "seq", 1, half)
    weights = lax.all_gather(kernel, "fsdp", axis=0, tiled=True).reshape(GROUPS, chans, KERNEL * chans)
    conv = conv_forward(padded, weights, length)
    up_float = upstream[0].astype(jnp.float32)
    up_g = up_float.reshape(length, GROUPS, chans).transpose(1, 0, 2)
    sig = jax.nn.sigmoid(conv)
    dconv = (up_g * sig * (1.0 + conv * (1.0 - sig))).astype(jnp.bfloat16)
    dpad = with_halo(dconv, "seq", 1, half)
    dnormed = conv_backward(dpad, weights, length)
    if seq_count <= GROUPS:
        group_in = lax.all_to_all(normed_g, "seq", 0, 1, tiled=True)
        group_out = lax.all_to_all(dconv, "seq", 0, 1, tiled=True)
    else:
        group_in, group_out = spread_groups(normed, dconv.transpose(1, 0, 2).reshape(length, width), chans)
    local_groups = group_in.shape[0]
    whole = group_in.shape[1]
    group_pad = jnp.pad(group_in, ((0, 0), (half, half), (0, 0)))
    kterms = [
        jnp.einsum("gto,gtc->goc", group_out, group_pad[:, k : k + whole], preferred_element_type=jnp.float32)
        for k in range(KERNEL)
    ]
    kernel_part = jnp.concatenate(kterms, axis=-1).reshape(-1, KERNEL * chans) * scale
    dnormed = dnormed.transpose(1, 0, 2).reshape(length, width)
    gain_term = jnp.sum(dnormed * mixed * inv, axis=0) * scale
    scaled = norm_gain * dnormed
    dmixed = inv * scaled - mixed * inv * inv * inv * jnp.mean(scaled * mixed, axis=-1, keepdims=True)
    input_grad = (up_float + dmixed).astype(jnp.bfloat16)
    table_term = (
        lax.dot_general(onehot, input_grad, (((0,), (0,)), ((), ())), preferred_element_type=jnp.float32)
        * scale
    )
    wide = width // fsdp
    rows = types // fsdp
    kg_rows = kernel_part.shape[0] // fsdp
    gain_rows = jnp.zeros((fsdp, 1, width), jnp.float32).at[:, 0, :wide].set(gain_term.reshape(fsdp, wide))
    first_table = jnp.concatenate([table_term.reshape(fsdp, rows, width), gain_rows], axis=1)
    first_kg = jnp.zeros((fsdp, rows + 1, kernel_part.shape[1]), jnp.float32)
    first_kg = first_kg.at[:, :kg_rows].set(kernel_part.reshape(fsdp, kg_rows, kernel_part.shape[1]))
    first = jnp.concatenate([first_table, first_kg], axis=2)
    first = lax.all_to_all(first, "fsdp", 0, 0, tiled=True).sum(axis=0)
    kg_sum = first[:kg_rows, width:]
    kernel_grad = gather_rows(kg_sum, "fsdp")
    narrow = wide // seq_count
    gain_rows = jnp.zeros((seq_count, 1, width), jnp.float32).at[:, 0, :narrow].set(
        first[rows, :wide].reshape(seq_count, narrow)
    )
    second = jnp.concatenate([first[:rows, :width].reshape(seq_count, rows // seq_count, width), gain_rows], axis=1)
    second = lax.all_to_all(second, "seq", 0, 0, tiled=True).sum(axis=0)
    table_grad = second[: rows // seq_count]
    gain_grad = second[rows // seq_count, :narrow]
    return (input_grad[None], table_grad, gain_grad, kernel_grad)


def solution(mesh):
    return jax.shard_map(
        body,
        mesh=mesh,
        in_specs=(
            P("fsdp", "seq", None),
            P("fsdp", "seq"),
            P("fsdp", None),
            P(),
            P("fsdp", None),
            P("fsdp", "seq", None),
        ),
        out_specs=(
            P("fsdp", "seq", None),
            P(("fsdp", "seq"), None),
            P(("fsdp", "seq")),
            P("seq", None),
        ),
        check_vma=False,
    )
```

```python
import jax
import jax.numpy as jnp
from jax import lax
from jax.sharding import PartitionSpec as P

GROUPS = 16
KERNEL = 9


def with_halo(cells, axis, dim, width):
    count = lax.axis_size(axis)
    ends = count - 1
    head = lax.slice_in_dim(cells, 0, width, axis=dim)
    tail = lax.slice_in_dim(cells, cells.shape[dim] - width, cells.shape[dim], axis=dim)
    return jnp.concatenate(
        [
            lax.ppermute(tail, axis, [(i, (i + 1) % count) for i in range(ends)]),
            cells,
            lax.ppermute(head, axis, [((i + 1) % count, i) for i in range(ends)]),
        ],
        axis=dim,
    )


def from_partner(value, axis, apart):
    mask = 2**apart
    pairs = [(source, source ^ mask) for source in range(lax.axis_size(axis))]
    return lax.ppermute(value, axis, pairs)


def gather_rows(block, axis):
    count = lax.axis_size(axis)
    return lax.all_to_all(jnp.tile(block, (count,) + (1,) * (block.ndim - 1)), axis, 0, 0, tiled=True)


def conv_forward(padded, weights, length):
    chans = padded.shape[-1]
    total = None
    for k in range(KERNEL):
        term = jnp.einsum(
            "gtc,goc->gto",
            padded[:, k : k + length],
            weights[:, :, k * chans : (k + 1) * chans],
            preferred_element_type=jnp.float32,
        )
        total = term if total is None else total + term
    return total


def conv_backward(dpad, weights, length):
    chans = weights.shape[-1] // KERNEL
    half = KERNEL // 2
    total = None
    for k in range(KERNEL):
        term = jnp.einsum(
            "gto,goc->gtc",
            dpad[:, 2 * half - k : 2 * half - k + length],
            weights[:, :, k * chans : (k + 1) * chans],
            preferred_element_type=jnp.float32,
        )
        total = term if total is None else total + term
    return total


def spread_groups(normed, dflat, chans):
    normed_slice = lax.all_to_all(normed, "seq", 1, 0, tiled=True)
    dconv_slice = lax.all_to_all(dflat, "seq", 1, 0, tiled=True)
    whole, slice_width = normed_slice.shape
    spread = chans // slice_width
    position = lax.axis_index("seq")
    group_rows = normed_slice
    for bit in range(spread.bit_length() - 1):
        partner = from_partner(group_rows, "seq", bit)
        lower = position >> bit & 1 == 0
        group_rows = jnp.where(
            lower,
            jnp.concatenate([group_rows, partner], axis=1),
            jnp.concatenate([partner, group_rows], axis=1),
        )
    return group_rows.reshape(1, whole, chans), dconv_slice.reshape(1, whole, slice_width)


def sum_rows(block, axis):
    count = lax.axis_size(axis)
    parts = block.reshape(count, block.shape[0] // count, *block.shape[1:])
    return lax.all_to_all(parts, axis, 0, 0, tiled=True).sum(axis=0)


def psum_rows(block, axis):
    return gather_rows(sum_rows(block, axis), axis)


def table_and_gain(input_grad, ids, gain_term, types, scale):
    every = ("fsdp", "seq")
    count = lax.axis_size("fsdp") * lax.axis_size("seq")
    length, width = input_grad.shape
    narrow = width // count
    id_rows = -(-length // narrow)
    ids_wide = jnp.zeros((id_rows * narrow,), jnp.bfloat16).at[:length].set(ids.astype(jnp.bfloat16))
    send = jnp.concatenate(
        [
            input_grad.reshape(length, count, narrow).transpose(1, 0, 2),
            jnp.broadcast_to(ids_wide.reshape(1, id_rows, narrow), (count, id_rows, narrow)),
        ],
        axis=1,
    )
    got = lax.all_to_all(send, every, 0, 0, tiled=True)
    rows_all = got[:, :length].reshape(count * length, narrow)
    ids_all = got[:, length:].reshape(count, id_rows * narrow)[:, :length].reshape(-1).astype(jnp.int32)
    onehot = (ids_all[:, None] == jnp.arange(types, dtype=jnp.int32)[None, :]).astype(jnp.bfloat16)
    columns = lax.dot_general(onehot, rows_all, (((0,), (0,)), ((), ())), preferred_element_type=jnp.float32)
    columns = columns * scale
    per = types // count
    back = jnp.concatenate(
        [columns.reshape(count, per, narrow), gain_term.reshape(count, 1, narrow)], axis=1
    )
    back = lax.all_to_all(back, every, 0, 0, tiled=True)
    table_grad = back[:, :per].transpose(1, 0, 2).reshape(per, width)
    gain_grad = back[:, per].sum(axis=0)
    return table_grad, gain_grad


def body(events, type_ids, type_table, norm_gain, kernel, upstream):
    length = events.shape[1]
    width = events.shape[2]
    chans = width // GROUPS
    half = KERNEL // 2
    fsdp = lax.axis_size("fsdp")
    seq_count = lax.axis_size("seq")
    total = length * seq_count * fsdp
    scale = 1.0 / jnp.sqrt(jnp.float32(total))
    table = gather_rows(type_table, "fsdp")
    types = table.shape[0]
    onehot = (type_ids[0][:, None] == jnp.arange(types, dtype=jnp.int32)[None, :]).astype(jnp.bfloat16)
    mixed = events[0].astype(jnp.float32) + jnp.dot(onehot, table, preferred_element_type=jnp.float32)
    inv = lax.rsqrt(jnp.mean(mixed * mixed, axis=-1, keepdims=True) + 1e-06)
    normed = (mixed * inv * norm_gain).astype(jnp.bfloat16)
    normed_g = normed.reshape(length, GROUPS, chans).transpose(1, 0, 2)
    padded = with_halo(normed_g, "seq", 1, half)
    weights = lax.all_gather(kernel, "fsdp", axis=0, tiled=True).reshape(GROUPS, chans, KERNEL * chans)
    conv = conv_forward(padded, weights, length)
    up_float = upstream[0].astype(jnp.float32)
    up_g = up_float.reshape(length, GROUPS, chans).transpose(1, 0, 2)
    sig = jax.nn.sigmoid(conv)
    dconv = (up_g * sig * (1.0 + conv * (1.0 - sig))).astype(jnp.bfloat16)
    dpad = with_halo(dconv, "seq", 1, half)
    dnormed = conv_backward(dpad, weights, length)
    if seq_count <= GROUPS:
        group_in = lax.all_to_all(normed_g, "seq", 0, 1, tiled=True)
        group_out = lax.all_to_all(dconv, "seq", 0, 1, tiled=True)
    else:
        group_in, group_out = spread_groups(normed, dconv.transpose(1, 0, 2).reshape(length, width), chans)
    local_groups = group_in.shape[0]
    whole = group_in.shape[1]
    group_pad = jnp.pad(group_in, ((0, 0), (half, half), (0, 0)))
    kterms = [
        jnp.einsum("gto,gtc->goc", group_out, group_pad[:, k : k + whole], preferred_element_type=jnp.float32)
        for k in range(KERNEL)
    ]
    kernel_part = jnp.concatenate(kterms, axis=-1).reshape(-1, KERNEL * chans) * scale
    dnormed = dnormed.transpose(1, 0, 2).reshape(length, width)
    gain_term = jnp.sum(dnormed * mixed * inv, axis=0) * scale
    scaled = norm_gain * dnormed
    dmixed = inv * scaled - mixed * inv * inv * inv * jnp.mean(scaled * mixed, axis=-1, keepdims=True)
    input_grad = (up_float + dmixed).astype(jnp.bfloat16)
    kernel_grad = psum_rows(kernel_part, "fsdp")
    table_grad, gain_grad = table_and_gain(input_grad, type_ids[0], gain_term, types, scale)
    return (input_grad[None], table_grad, gain_grad, kernel_grad)


def solution(mesh):
    return jax.shard_map(
        body,
        mesh=mesh,
        in_specs=(
            P("fsdp", "seq", None),
            P("fsdp", "seq"),
            P("fsdp", None),
            P(),
            P("fsdp", None),
            P("fsdp", "seq", None),
        ),
        out_specs=(
            P("fsdp", "seq", None),
            P(("fsdp", "seq"), None),
            P(("fsdp", "seq")),
            P("seq", None),
        ),
        check_vma=False,
    )
```

```python
import jax
import jax.numpy as jnp
from jax import lax
from jax.sharding import PartitionSpec as P

GROUPS = 16
KERNEL = 9


def with_halo(cells, axis, dim, width):
    count = lax.axis_size(axis)
    ends = count - 1
    head = lax.slice_in_dim(cells, 0, width, axis=dim)
    tail = lax.slice_in_dim(cells, cells.shape[dim] - width, cells.shape[dim], axis=dim)
    return jnp.concatenate(
        [
            lax.ppermute(tail, axis, [(i, (i + 1) % count) for i in range(ends)]),
            cells,
            lax.ppermute(head, axis, [((i + 1) % count, i) for i in range(ends)]),
        ],
        axis=dim,
    )


def from_partner(value, axis, apart):
    mask = 2**apart
    pairs = [(source, source ^ mask) for source in range(lax.axis_size(axis))]
    return lax.ppermute(value, axis, pairs)


def gather_rows(block, axis):
    count = lax.axis_size(axis)
    return lax.all_to_all(jnp.tile(block, (count,) + (1,) * (block.ndim - 1)), axis, 0, 0, tiled=True)


def conv_forward(padded, weights, length):
    chans = padded.shape[-1]
    total = None
    for k in range(KERNEL):
        term = jnp.einsum(
            "gtc,goc->gto",
            padded[:, k : k + length],
            weights[:, :, k * chans : (k + 1) * chans],
            preferred_element_type=jnp.float32,
        )
        total = term if total is None else total + term
    return total


def conv_backward(dpad, weights, length):
    chans = weights.shape[-1] // KERNEL
    half = KERNEL // 2
    total = None
    for k in range(KERNEL):
        term = jnp.einsum(
            "gto,goc->gtc",
            dpad[:, 2 * half - k : 2 * half - k + length],
            weights[:, :, k * chans : (k + 1) * chans],
            preferred_element_type=jnp.float32,
        )
        total = term if total is None else total + term
    return total


def spread_groups(normed, dflat, chans):
    normed_slice = lax.all_to_all(normed, "seq", 1, 0, tiled=True)
    dconv_slice = lax.all_to_all(dflat, "seq", 1, 0, tiled=True)
    whole, slice_width = normed_slice.shape
    spread = chans // slice_width
    position = lax.axis_index("seq")
    group_rows = normed_slice
    for bit in range(spread.bit_length() - 1):
        partner = from_partner(group_rows, "seq", bit)
        lower = position >> bit & 1 == 0
        group_rows = jnp.where(
            lower,
            jnp.concatenate([group_rows, partner], axis=1),
            jnp.concatenate([partner, group_rows], axis=1),
        )
    return group_rows.reshape(1, whole, chans), dconv_slice.reshape(1, whole, slice_width)


def sum_rows(block, axis):
    count = lax.axis_size(axis)
    parts = block.reshape(count, block.shape[0] // count, *block.shape[1:])
    return lax.all_to_all(parts, axis, 0, 0, tiled=True).sum(axis=0)


def psum_rows(block, axis):
    return gather_rows(sum_rows(block, axis), axis)


def table_and_gain(input_grad, ids, gain_term, types, scale):
    every = ("fsdp", "seq")
    count = lax.axis_size("fsdp") * lax.axis_size("seq")
    length, width = input_grad.shape
    narrow = width // count
    id_rows = -(-length // narrow)
    ids_wide = jnp.zeros((id_rows * narrow,), jnp.bfloat16).at[:length].set(ids.astype(jnp.bfloat16))
    send = jnp.concatenate(
        [
            input_grad.reshape(length, count, narrow).transpose(1, 0, 2),
            jnp.broadcast_to(ids_wide.reshape(1, id_rows, narrow), (count, id_rows, narrow)),
        ],
        axis=1,
    )
    got = lax.all_to_all(send, every, 0, 0, tiled=True)
    rows_all = got[:, :length].reshape(count * length, narrow)
    ids_all = got[:, length:].reshape(count, id_rows * narrow)[:, :length].reshape(-1).astype(jnp.int32)
    onehot = (ids_all[:, None] == jnp.arange(types, dtype=jnp.int32)[None, :]).astype(jnp.bfloat16)
    columns = lax.dot_general(onehot, rows_all, (((0,), (0,)), ((), ())), preferred_element_type=jnp.float32)
    columns = columns * scale
    per = types // count
    back = jnp.concatenate(
        [columns.reshape(count, per, narrow), gain_term.reshape(count, 1, narrow)], axis=1
    )
    back = lax.all_to_all(back, every, 0, 0, tiled=True)
    table_grad = back[:, :per].transpose(1, 0, 2).reshape(per, width)
    gain_grad = back[:, per].sum(axis=0)
    return table_grad, gain_grad


def body(events, type_ids, type_table, norm_gain, kernel, upstream):
    length = events.shape[1]
    width = events.shape[2]
    chans = width // GROUPS
    half = KERNEL // 2
    fsdp = lax.axis_size("fsdp")
    seq_count = lax.axis_size("seq")
    total = length * seq_count * fsdp
    scale = 1.0 / jnp.sqrt(jnp.float32(total))
    table = gather_rows(type_table, "fsdp")
    types = table.shape[0]
    onehot = (type_ids[0][:, None] == jnp.arange(types, dtype=jnp.int32)[None, :]).astype(jnp.bfloat16)
    mixed = events[0].astype(jnp.float32) + jnp.dot(onehot, table, preferred_element_type=jnp.float32)
    inv = lax.rsqrt(jnp.mean(mixed * mixed, axis=-1, keepdims=True) + 1e-06)
    normed = (mixed * inv * norm_gain).astype(jnp.bfloat16)
    normed_g = normed.reshape(length, GROUPS, chans).transpose(1, 0, 2)
    padded = with_halo(normed_g, "seq", 1, half)
    weights = lax.all_gather(kernel, "fsdp", axis=0, tiled=True).reshape(GROUPS, chans, KERNEL * chans)
    conv = conv_forward(padded, weights, length)
    up_float = upstream[0].astype(jnp.float32)
    up_g = up_float.reshape(length, GROUPS, chans).transpose(1, 0, 2)
    sig = jax.nn.sigmoid(conv)
    dconv = (up_g * sig * (1.0 + conv * (1.0 - sig))).astype(jnp.bfloat16)
    dpad = with_halo(dconv, "seq", 1, half)
    dnormed = conv_backward(dpad, weights, length)
    if seq_count <= GROUPS:
        group_in = lax.all_to_all(normed_g, "seq", 0, 1, tiled=True)
        group_out = lax.all_to_all(dconv, "seq", 0, 1, tiled=True)
    else:
        group_in, group_out = spread_groups(normed, dconv.transpose(1, 0, 2).reshape(length, width), chans)
    local_groups = group_in.shape[0]
    whole = group_in.shape[1]
    group_pad = jnp.pad(group_in, ((0, 0), (half, half), (0, 0)))
    kterms = [
        jnp.einsum("gto,gtc->goc", group_out, group_pad[:, k : k + whole], preferred_element_type=jnp.float32)
        for k in range(KERNEL)
    ]
    kernel_part = jnp.concatenate(kterms, axis=-1).reshape(-1, KERNEL * chans) * scale
    dnormed = dnormed.transpose(1, 0, 2).reshape(length, width)
    gain_term = jnp.sum(dnormed * mixed * inv, axis=0) * scale
    scaled = norm_gain * dnormed
    dmixed = inv * scaled - mixed * inv * inv * inv * jnp.mean(scaled * mixed, axis=-1, keepdims=True)
    input_grad = (up_float + dmixed).astype(jnp.bfloat16)
    kernel_grad = lax.psum(kernel_part, "fsdp")
    table_grad, gain_grad = table_and_gain(input_grad, type_ids[0], gain_term, types, scale)
    return (input_grad[None], table_grad, gain_grad, kernel_grad)


def solution(mesh):
    return jax.shard_map(
        body,
        mesh=mesh,
        in_specs=(
            P("fsdp", "seq", None),
            P("fsdp", "seq"),
            P("fsdp", None),
            P(),
            P("fsdp", None),
            P("fsdp", "seq", None),
        ),
        out_specs=(
            P("fsdp", "seq", None),
            P(("fsdp", "seq"), None),
            P(("fsdp", "seq")),
            P("seq", None),
        ),
        check_vma=False,
    )
```

```python
import jax
import jax.numpy as jnp
from jax import lax
from jax.experimental import pallas as pl
from jax.experimental.pallas import tpu as pltpu
from jax.sharding import PartitionSpec as P

GROUPS = 16
KERNEL = 9


def with_halo(cells, axis, dim, width):
    count = lax.axis_size(axis)
    ends = count - 1
    head = lax.slice_in_dim(cells, 0, width, axis=dim)
    tail = lax.slice_in_dim(cells, cells.shape[dim] - width, cells.shape[dim], axis=dim)
    return jnp.concatenate(
        [
            lax.ppermute(tail, axis, [(i, (i + 1) % count) for i in range(ends)]),
            cells,
            lax.ppermute(head, axis, [((i + 1) % count, i) for i in range(ends)]),
        ],
        axis=dim,
    )


def from_partner(value, axis, apart):
    mask = 2**apart
    pairs = [(source, source ^ mask) for source in range(lax.axis_size(axis))]
    return lax.ppermute(value, axis, pairs)


def gather_rows(block, axis):
    count = lax.axis_size(axis)
    return lax.all_to_all(jnp.tile(block, (count,) + (1,) * (block.ndim - 1)), axis, 0, 0, tiled=True)


STEP_GROUPS = 4


def forward_kernel(pad_ref, w_ref, up_ref, out_ref):
    length = out_ref.shape[1]
    chans = pad_ref.shape[2]
    for g in range(out_ref.shape[0]):
        acc = None
        for k in range(KERNEL):
            x = pad_ref[g, k : k + length, :].astype(jnp.bfloat16)
            w = w_ref[g, :, k * chans : (k + 1) * chans]
            term = lax.dot_general(x, w, (((1,), (1,)), ((), ())), preferred_element_type=jnp.float32)
            acc = term if acc is None else acc + term
        sig = 1.0 / (1.0 + jnp.exp(-acc))
        out_ref[g] = (up_ref[g] * sig * (1.0 + acc * (1.0 - sig))).astype(out_ref.dtype)


def backward_kernel(pad_ref, w_ref, out_ref):
    length = out_ref.shape[1]
    chans = out_ref.shape[2]
    half = KERNEL // 2
    for g in range(out_ref.shape[0]):
        acc = None
        for k in range(KERNEL):
            x = pad_ref[g, 2 * half - k : 2 * half - k + length, :].astype(jnp.bfloat16)
            w = w_ref[g, :, k * chans : (k + 1) * chans]
            term = jnp.dot(x, w, preferred_element_type=jnp.float32)
            acc = term if acc is None else acc + term
        out_ref[g] = acc


def conv_dconv(padded, weights, up):
    groups, rows, chans = padded.shape
    length = up.shape[1]
    step = STEP_GROUPS if groups % STEP_GROUPS == 0 else 1
    flops = 2 * groups * length * chans * weights.shape[1] * KERNEL
    return pl.pallas_call(
        forward_kernel,
        grid=(groups // step,),
        in_specs=[
            pl.BlockSpec((step, rows, chans), lambda i: (i, 0, 0)),
            pl.BlockSpec((step, weights.shape[1], weights.shape[2]), lambda i: (i, 0, 0)),
            pl.BlockSpec((step, length, up.shape[2]), lambda i: (i, 0, 0)),
        ],
        out_specs=pl.BlockSpec((step, length, up.shape[2]), lambda i: (i, 0, 0)),
        out_shape=jax.ShapeDtypeStruct(up.shape, jnp.bfloat16),
        cost_estimate=pl.CostEstimate(
            flops=flops,
            transcendentals=up.size,
            bytes_accessed=padded.size * 4 + weights.size * 2 + up.size * 6,
        ),
    )(padded, weights, up)


def conv_transpose(dpad, weights, length):
    groups, rows, outs = dpad.shape
    chans = weights.shape[2] // KERNEL
    step = STEP_GROUPS if groups % STEP_GROUPS == 0 else 1
    return pl.pallas_call(
        backward_kernel,
        grid=(groups // step,),
        in_specs=[
            pl.BlockSpec((step, rows, outs), lambda i: (i, 0, 0)),
            pl.BlockSpec((step, weights.shape[1], weights.shape[2]), lambda i: (i, 0, 0)),
        ],
        out_specs=pl.BlockSpec((step, length, chans), lambda i: (i, 0, 0)),
        out_shape=jax.ShapeDtypeStruct((groups, length, chans), jnp.float32),
        cost_estimate=pl.CostEstimate(
            flops=2 * groups * length * chans * outs * KERNEL,
            transcendentals=0,
            bytes_accessed=dpad.size * 4 + weights.size * 2 + groups * length * chans * 4,
        ),
    )(dpad, weights)


def spread_groups(normed, dflat, chans):
    normed_slice = lax.all_to_all(normed, "seq", 1, 0, tiled=True)
    dconv_slice = lax.all_to_all(dflat, "seq", 1, 0, tiled=True)
    whole, slice_width = normed_slice.shape
    spread = chans // slice_width
    position = lax.axis_index("seq")
    group_rows = normed_slice
    for bit in range(spread.bit_length() - 1):
        partner = from_partner(group_rows, "seq", bit)
        lower = position >> bit & 1 == 0
        group_rows = jnp.where(
            lower,
            jnp.concatenate([group_rows, partner], axis=1),
            jnp.concatenate([partner, group_rows], axis=1),
        )
    return group_rows.reshape(1, whole, chans), dconv_slice.reshape(1, whole, slice_width)


def sum_rows(block, axis):
    count = lax.axis_size(axis)
    parts = block.reshape(count, block.shape[0] // count, *block.shape[1:])
    return lax.all_to_all(parts, axis, 0, 0, tiled=True).sum(axis=0)


def psum_rows(block, axis):
    return gather_rows(sum_rows(block, axis), axis)


def table_and_gain(input_grad, ids, gain_term, types, scale):
    every = ("fsdp", "seq")
    count = lax.axis_size("fsdp") * lax.axis_size("seq")
    length, width = input_grad.shape
    narrow = width // count
    id_rows = -(-length // narrow)
    ids_wide = jnp.zeros((id_rows * narrow,), jnp.bfloat16).at[:length].set(ids.astype(jnp.bfloat16))
    send = jnp.concatenate(
        [
            input_grad.reshape(length, count, narrow).transpose(1, 0, 2),
            jnp.broadcast_to(ids_wide.reshape(1, id_rows, narrow), (count, id_rows, narrow)),
        ],
        axis=1,
    )
    got = lax.all_to_all(send, every, 0, 0, tiled=True)
    rows_all = got[:, :length].reshape(count * length, narrow)
    ids_all = got[:, length:].reshape(count, id_rows * narrow)[:, :length].reshape(-1).astype(jnp.int32)
    onehot = (ids_all[:, None] == jnp.arange(types, dtype=jnp.int32)[None, :]).astype(jnp.bfloat16)
    columns = lax.dot_general(onehot, rows_all, (((0,), (0,)), ((), ())), preferred_element_type=jnp.float32)
    columns = columns * scale
    per = types // count
    back = jnp.concatenate(
        [columns.reshape(count, per, narrow), gain_term.reshape(count, 1, narrow)], axis=1
    )
    back = lax.all_to_all(back, every, 0, 0, tiled=True)
    table_grad = back[:, :per].transpose(1, 0, 2).reshape(per, width)
    gain_grad = back[:, per].sum(axis=0)
    return table_grad, gain_grad


def body(events, type_ids, type_table, norm_gain, kernel, upstream):
    length = events.shape[1]
    width = events.shape[2]
    chans = width // GROUPS
    half = KERNEL // 2
    fsdp = lax.axis_size("fsdp")
    seq_count = lax.axis_size("seq")
    total = length * seq_count * fsdp
    scale = 1.0 / jnp.sqrt(jnp.float32(total))
    table = gather_rows(type_table, "fsdp")
    types = table.shape[0]
    onehot = (type_ids[0][:, None] == jnp.arange(types, dtype=jnp.int32)[None, :]).astype(jnp.bfloat16)
    mixed = events[0].astype(jnp.float32) + jnp.dot(onehot, table, preferred_element_type=jnp.float32)
    inv = lax.rsqrt(jnp.mean(mixed * mixed, axis=-1, keepdims=True) + 1e-06)
    normed = (mixed * inv * norm_gain).astype(jnp.bfloat16)
    normed_g = normed.reshape(length, GROUPS, chans).transpose(1, 0, 2)
    padded = with_halo(normed_g, "seq", 1, half)
    weights = lax.all_gather(kernel, "fsdp", axis=0, tiled=True).reshape(GROUPS, chans, KERNEL * chans)
    up_float = upstream[0].astype(jnp.float32)
    up_g = up_float.reshape(length, GROUPS, chans).transpose(1, 0, 2)
    dconv = conv_dconv(padded.astype(jnp.float32), weights, up_g)
    dpad = with_halo(dconv, "seq", 1, half)
    dnormed = conv_transpose(dpad.astype(jnp.float32), weights, length)
    if seq_count <= GROUPS:
        group_in = lax.all_to_all(normed_g, "seq", 0, 1, tiled=True)
        group_out = lax.all_to_all(dconv, "seq", 0, 1, tiled=True)
    else:
        group_in, group_out = spread_groups(normed, dconv.transpose(1, 0, 2).reshape(length, width), chans)
    local_groups = group_in.shape[0]
    whole = group_in.shape[1]
    group_pad = jnp.pad(group_in, ((0, 0), (half, half), (0, 0)))
    kterms = [
        jnp.einsum("gto,gtc->goc", group_out, group_pad[:, k : k + whole], preferred_element_type=jnp.float32)
        for k in range(KERNEL)
    ]
    kernel_part = jnp.concatenate(kterms, axis=-1).reshape(-1, KERNEL * chans) * scale
    dnormed = dnormed.transpose(1, 0, 2).reshape(length, width)
    gain_term = jnp.sum(dnormed * mixed * inv, axis=0) * scale
    scaled = norm_gain * dnormed
    dmixed = inv * scaled - mixed * inv * inv * inv * jnp.mean(scaled * mixed, axis=-1, keepdims=True)
    input_grad = (up_float + dmixed).astype(jnp.bfloat16)
    kernel_grad = lax.psum(kernel_part, "fsdp")
    table_grad, gain_grad = table_and_gain(input_grad, type_ids[0], gain_term, types, scale)
    return (input_grad[None], table_grad, gain_grad, kernel_grad)


def solution(mesh):
    return jax.shard_map(
        body,
        mesh=mesh,
        in_specs=(
            P("fsdp", "seq", None),
            P("fsdp", "seq"),
            P("fsdp", None),
            P(),
            P("fsdp", None),
            P("fsdp", "seq", None),
        ),
        out_specs=(
            P("fsdp", "seq", None),
            P(("fsdp", "seq"), None),
            P(("fsdp", "seq")),
            P("seq", None),
        ),
        check_vma=False,
    )
```

```python
import jax
import jax.numpy as jnp
from jax import lax
from jax.experimental import pallas as pl
from jax.experimental.pallas import tpu as pltpu
from jax.sharding import PartitionSpec as P

GROUPS = 16
KERNEL = 9


def with_halo(cells, axis, dim, width):
    count = lax.axis_size(axis)
    ends = count - 1
    head = lax.slice_in_dim(cells, 0, width, axis=dim)
    tail = lax.slice_in_dim(cells, cells.shape[dim] - width, cells.shape[dim], axis=dim)
    return jnp.concatenate(
        [
            lax.ppermute(tail, axis, [(i, (i + 1) % count) for i in range(ends)]),
            cells,
            lax.ppermute(head, axis, [((i + 1) % count, i) for i in range(ends)]),
        ],
        axis=dim,
    )


def from_partner(value, axis, apart):
    mask = 2**apart
    pairs = [(source, source ^ mask) for source in range(lax.axis_size(axis))]
    return lax.ppermute(value, axis, pairs)


def gather_rows(block, axis):
    count = lax.axis_size(axis)
    return lax.all_to_all(jnp.tile(block, (count,) + (1,) * (block.ndim - 1)), axis, 0, 0, tiled=True)


STEP_GROUPS = 4


def forward_kernel(pad_ref, w_ref, up_ref, out_ref):
    length = out_ref.shape[1]
    chans = pad_ref.shape[2]
    for g in range(out_ref.shape[0]):
        acc = None
        for k in range(KERNEL):
            x = pad_ref[g, k : k + length, :].astype(jnp.bfloat16)
            w = w_ref[g, :, k * chans : (k + 1) * chans]
            term = lax.dot_general(x, w, (((1,), (1,)), ((), ())), preferred_element_type=jnp.float32)
            acc = term if acc is None else acc + term
        sig = 1.0 / (1.0 + jnp.exp(-acc))
        out_ref[g] = (up_ref[g] * sig * (1.0 + acc * (1.0 - sig))).astype(out_ref.dtype)


def backward_kernel(pad_ref, w_ref, out_ref):
    length = out_ref.shape[1]
    chans = out_ref.shape[2]
    half = KERNEL // 2
    for g in range(out_ref.shape[0]):
        acc = None
        for k in range(KERNEL):
            x = pad_ref[g, 2 * half - k : 2 * half - k + length, :].astype(jnp.bfloat16)
            w = w_ref[g, :, k * chans : (k + 1) * chans]
            term = jnp.dot(x, w, preferred_element_type=jnp.float32)
            acc = term if acc is None else acc + term
        out_ref[g] = acc


def conv_dconv(padded, weights, up):
    groups, rows, chans = padded.shape
    length = up.shape[1]
    step = STEP_GROUPS if groups % STEP_GROUPS == 0 else 1
    flops = 2 * groups * length * chans * weights.shape[1] * KERNEL
    return pl.pallas_call(
        forward_kernel,
        grid=(groups // step,),
        in_specs=[
            pl.BlockSpec((step, rows, chans), lambda i: (i, 0, 0)),
            pl.BlockSpec((step, weights.shape[1], weights.shape[2]), lambda i: (i, 0, 0)),
            pl.BlockSpec((step, length, up.shape[2]), lambda i: (i, 0, 0)),
        ],
        out_specs=pl.BlockSpec((step, length, up.shape[2]), lambda i: (i, 0, 0)),
        out_shape=jax.ShapeDtypeStruct(up.shape, jnp.bfloat16),
        cost_estimate=pl.CostEstimate(
            flops=flops,
            transcendentals=up.size,
            bytes_accessed=padded.size * 4 + weights.size * 2 + up.size * 6,
        ),
    )(padded, weights, up)


def conv_transpose(dpad, weights, length):
    groups, rows, outs = dpad.shape
    chans = weights.shape[2] // KERNEL
    step = STEP_GROUPS if groups % STEP_GROUPS == 0 else 1
    return pl.pallas_call(
        backward_kernel,
        grid=(groups // step,),
        in_specs=[
            pl.BlockSpec((step, rows, outs), lambda i: (i, 0, 0)),
            pl.BlockSpec((step, weights.shape[1], weights.shape[2]), lambda i: (i, 0, 0)),
        ],
        out_specs=pl.BlockSpec((step, length, chans), lambda i: (i, 0, 0)),
        out_shape=jax.ShapeDtypeStruct((groups, length, chans), jnp.float32),
        cost_estimate=pl.CostEstimate(
            flops=2 * groups * length * chans * outs * KERNEL,
            transcendentals=0,
            bytes_accessed=dpad.size * 4 + weights.size * 2 + groups * length * chans * 4,
        ),
    )(dpad, weights)


def spread_groups(normed, dflat, chans):
    normed_slice = lax.all_to_all(normed, "seq", 1, 0, tiled=True)
    dconv_slice = lax.all_to_all(dflat, "seq", 1, 0, tiled=True)
    whole, slice_width = normed_slice.shape
    spread = chans // slice_width
    position = lax.axis_index("seq")
    group_rows = normed_slice
    for bit in range(spread.bit_length() - 1):
        partner = from_partner(group_rows, "seq", bit)
        lower = position >> bit & 1 == 0
        group_rows = jnp.where(
            lower,
            jnp.concatenate([group_rows, partner], axis=1),
            jnp.concatenate([partner, group_rows], axis=1),
        )
    return group_rows.reshape(1, whole, chans), dconv_slice.reshape(1, whole, slice_width)


def sum_rows(block, axis):
    count = lax.axis_size(axis)
    parts = block.reshape(count, block.shape[0] // count, *block.shape[1:])
    return lax.all_to_all(parts, axis, 0, 0, tiled=True).sum(axis=0)


def psum_rows(block, axis):
    return gather_rows(sum_rows(block, axis), axis)


def table_and_gain(input_grad, ids, gain_term, types, scale):
    every = ("fsdp", "seq")
    count = lax.axis_size("fsdp") * lax.axis_size("seq")
    length, width = input_grad.shape
    narrow = width // count
    id_rows = -(-length // narrow)
    ids_wide = jnp.zeros((id_rows * narrow,), jnp.bfloat16).at[:length].set(ids.astype(jnp.bfloat16))
    send = jnp.concatenate(
        [
            input_grad.reshape(length, count, narrow).transpose(1, 0, 2),
            jnp.broadcast_to(ids_wide.reshape(1, id_rows, narrow), (count, id_rows, narrow)),
        ],
        axis=1,
    )
    got = lax.all_to_all(send, every, 0, 0, tiled=True)
    rows_all = got[:, :length].reshape(count * length, narrow)
    ids_all = got[:, length:].reshape(count, id_rows * narrow)[:, :length].reshape(-1).astype(jnp.int32)
    onehot = (ids_all[:, None] == jnp.arange(types, dtype=jnp.int32)[None, :]).astype(jnp.bfloat16)
    columns = lax.dot_general(onehot, rows_all, (((0,), (0,)), ((), ())), preferred_element_type=jnp.float32)
    columns = columns * scale
    per = types // count
    back = jnp.concatenate(
        [columns.reshape(count, per, narrow), gain_term.reshape(count, 1, narrow)], axis=1
    )
    back = lax.all_to_all(back, every, 0, 0, tiled=True)
    table_grad = back[:, :per].transpose(1, 0, 2).reshape(per, width)
    gain_grad = back[:, per].sum(axis=0)
    return table_grad, gain_grad


def body(events, type_ids, type_table, norm_gain, kernel, upstream):
    length = events.shape[1]
    width = events.shape[2]
    chans = width // GROUPS
    half = KERNEL // 2
    fsdp = lax.axis_size("fsdp")
    seq_count = lax.axis_size("seq")
    total = length * seq_count * fsdp
    scale = 1.0 / jnp.sqrt(jnp.float32(total))
    table = gather_rows(type_table, "fsdp")
    types = table.shape[0]
    onehot = (type_ids[0][:, None] == jnp.arange(types, dtype=jnp.int32)[None, :]).astype(jnp.bfloat16)
    mixed = events[0].astype(jnp.float32) + jnp.dot(onehot, table, preferred_element_type=jnp.float32)
    inv = lax.rsqrt(jnp.mean(mixed * mixed, axis=-1, keepdims=True) + 1e-06)
    normed = (mixed * inv * norm_gain).astype(jnp.bfloat16)
    normed_g = normed.reshape(length, GROUPS, chans).transpose(1, 0, 2)
    padded = with_halo(normed_g, "seq", 1, 2 * half)
    up_g = upstream[0].reshape(length, GROUPS, chans).transpose(1, 0, 2)
    up_pad = with_halo(up_g, "seq", 1, half)
    weights = lax.all_gather(kernel, "fsdp", axis=0, tiled=True).reshape(GROUPS, chans, KERNEL * chans)
    up_float = upstream[0].astype(jnp.float32)
    dpad = conv_dconv(padded.astype(jnp.float32), weights, up_pad.astype(jnp.float32))
    dconv = dpad[:, half : half + length]
    dnormed = conv_transpose(dpad.astype(jnp.float32), weights, length)
    if seq_count <= GROUPS:
        group_in = lax.all_to_all(normed_g, "seq", 0, 1, tiled=True)
        group_out = lax.all_to_all(dconv, "seq", 0, 1, tiled=True)
    else:
        group_in, group_out = spread_groups(normed, dconv.transpose(1, 0, 2).reshape(length, width), chans)
    local_groups = group_in.shape[0]
    whole = group_in.shape[1]
    group_pad = jnp.pad(group_in, ((0, 0), (half, half), (0, 0)))
    kterms = [
        jnp.einsum("gto,gtc->goc", group_out, group_pad[:, k : k + whole], preferred_element_type=jnp.float32)
        for k in range(KERNEL)
    ]
    kernel_part = jnp.concatenate(kterms, axis=-1).reshape(-1, KERNEL * chans) * scale
    dnormed = dnormed.transpose(1, 0, 2).reshape(length, width)
    gain_term = jnp.sum(dnormed * mixed * inv, axis=0) * scale
    scaled = norm_gain * dnormed
    dmixed = inv * scaled - mixed * inv * inv * inv * jnp.mean(scaled * mixed, axis=-1, keepdims=True)
    input_grad = (up_float + dmixed).astype(jnp.bfloat16)
    kernel_grad = lax.psum(kernel_part, "fsdp")
    table_grad, gain_grad = table_and_gain(input_grad, type_ids[0], gain_term, types, scale)
    return (input_grad[None], table_grad, gain_grad, kernel_grad)


def solution(mesh):
    return jax.shard_map(
        body,
        mesh=mesh,
        in_specs=(
            P("fsdp", "seq", None),
            P("fsdp", "seq"),
            P("fsdp", None),
            P(),
            P("fsdp", None),
            P("fsdp", "seq", None),
        ),
        out_specs=(
            P("fsdp", "seq", None),
            P(("fsdp", "seq"), None),
            P(("fsdp", "seq")),
            P("seq", None),
        ),
        check_vma=False,
    )
```

```python
import jax
import jax.numpy as jnp
from jax import lax
from jax.experimental import pallas as pl
from jax.experimental.pallas import tpu as pltpu
from jax.sharding import PartitionSpec as P

GROUPS = 16
KERNEL = 9


def with_halo(cells, axis, dim, width):
    count = lax.axis_size(axis)
    ends = count - 1
    head = lax.slice_in_dim(cells, 0, width, axis=dim)
    tail = lax.slice_in_dim(cells, cells.shape[dim] - width, cells.shape[dim], axis=dim)
    return jnp.concatenate(
        [
            lax.ppermute(tail, axis, [(i, (i + 1) % count) for i in range(ends)]),
            cells,
            lax.ppermute(head, axis, [((i + 1) % count, i) for i in range(ends)]),
        ],
        axis=dim,
    )


def from_partner(value, axis, apart):
    mask = 2**apart
    pairs = [(source, source ^ mask) for source in range(lax.axis_size(axis))]
    return lax.ppermute(value, axis, pairs)


def gather_rows(block, axis):
    count = lax.axis_size(axis)
    return lax.all_to_all(jnp.tile(block, (count,) + (1,) * (block.ndim - 1)), axis, 0, 0, tiled=True)


STEP_GROUPS = 4


def forward_kernel(pad_ref, w_ref, up_ref, out_ref):
    length = out_ref.shape[1]
    chans = pad_ref.shape[2]
    for g in range(out_ref.shape[0]):
        acc = None
        for k in range(KERNEL):
            x = pad_ref[g, k : k + length, :].astype(jnp.bfloat16)
            w = w_ref[g, :, k * chans : (k + 1) * chans]
            term = lax.dot_general(x, w, (((1,), (1,)), ((), ())), preferred_element_type=jnp.float32)
            acc = term if acc is None else acc + term
        sig = 1.0 / (1.0 + jnp.exp(-acc))
        out_ref[g] = (up_ref[g] * sig * (1.0 + acc * (1.0 - sig))).astype(out_ref.dtype)


def backward_kernel(pad_ref, w_ref, out_ref):
    length = out_ref.shape[1]
    chans = out_ref.shape[2]
    half = KERNEL // 2
    for g in range(out_ref.shape[0]):
        acc = None
        for k in range(KERNEL):
            x = pad_ref[g, 2 * half - k : 2 * half - k + length, :].astype(jnp.bfloat16)
            w = w_ref[g, :, k * chans : (k + 1) * chans]
            term = jnp.dot(x, w, preferred_element_type=jnp.float32)
            acc = term if acc is None else acc + term
        out_ref[g] = acc


def conv_dconv(padded, weights, up):
    groups, rows, chans = padded.shape
    length = up.shape[1]
    step = STEP_GROUPS if groups % STEP_GROUPS == 0 else 1
    flops = 2 * groups * length * chans * weights.shape[1] * KERNEL
    return pl.pallas_call(
        forward_kernel,
        grid=(groups // step,),
        in_specs=[
            pl.BlockSpec((step, rows, chans), lambda i: (i, 0, 0)),
            pl.BlockSpec((step, weights.shape[1], weights.shape[2]), lambda i: (i, 0, 0)),
            pl.BlockSpec((step, length, up.shape[2]), lambda i: (i, 0, 0)),
        ],
        out_specs=pl.BlockSpec((step, length, up.shape[2]), lambda i: (i, 0, 0)),
        out_shape=jax.ShapeDtypeStruct(up.shape, jnp.bfloat16),
        cost_estimate=pl.CostEstimate(
            flops=flops,
            transcendentals=up.size,
            bytes_accessed=padded.size * 4 + weights.size * 2 + up.size * 6,
        ),
    )(padded, weights, up)


def conv_transpose(dpad, weights, length):
    groups, rows, outs = dpad.shape
    chans = weights.shape[2] // KERNEL
    step = STEP_GROUPS if groups % STEP_GROUPS == 0 else 1
    return pl.pallas_call(
        backward_kernel,
        grid=(groups // step,),
        in_specs=[
            pl.BlockSpec((step, rows, outs), lambda i: (i, 0, 0)),
            pl.BlockSpec((step, weights.shape[1], weights.shape[2]), lambda i: (i, 0, 0)),
        ],
        out_specs=pl.BlockSpec((step, length, chans), lambda i: (i, 0, 0)),
        out_shape=jax.ShapeDtypeStruct((groups, length, chans), jnp.float32),
        cost_estimate=pl.CostEstimate(
            flops=2 * groups * length * chans * outs * KERNEL,
            transcendentals=0,
            bytes_accessed=dpad.size * 4 + weights.size * 2 + groups * length * chans * 4,
        ),
    )(dpad, weights)


def spread_groups(normed, dflat, chans):
    normed_slice = lax.all_to_all(normed, "seq", 1, 0, tiled=True)
    dconv_slice = lax.all_to_all(dflat, "seq", 1, 0, tiled=True)
    whole, slice_width = normed_slice.shape
    spread = chans // slice_width
    position = lax.axis_index("seq")
    group_rows = normed_slice
    for bit in range(spread.bit_length() - 1):
        partner = from_partner(group_rows, "seq", bit)
        lower = position >> bit & 1 == 0
        group_rows = jnp.where(
            lower,
            jnp.concatenate([group_rows, partner], axis=1),
            jnp.concatenate([partner, group_rows], axis=1),
        )
    return group_rows.reshape(1, whole, chans), dconv_slice.reshape(1, whole, slice_width)


def sum_rows(block, axis):
    count = lax.axis_size(axis)
    parts = block.reshape(count, block.shape[0] // count, *block.shape[1:])
    return lax.all_to_all(parts, axis, 0, 0, tiled=True).sum(axis=0)


def psum_rows(block, axis):
    return gather_rows(sum_rows(block, axis), axis)


def table_and_gain(input_grad, ids, gain_term, types, scale):
    every = ("fsdp", "seq")
    count = lax.axis_size("fsdp") * lax.axis_size("seq")
    length, width = input_grad.shape
    narrow = width // count
    id_rows = -(-length // narrow)
    ids_wide = jnp.zeros((id_rows * narrow,), jnp.bfloat16).at[:length].set(ids.astype(jnp.bfloat16))
    send = jnp.concatenate(
        [
            input_grad.reshape(length, count, narrow).transpose(1, 0, 2),
            jnp.broadcast_to(ids_wide.reshape(1, id_rows, narrow), (count, id_rows, narrow)),
        ],
        axis=1,
    )
    got = lax.all_to_all(send, every, 0, 0, tiled=True)
    rows_all = got[:, :length].reshape(count * length, narrow)
    ids_all = got[:, length:].reshape(count, id_rows * narrow)[:, :length].reshape(-1).astype(jnp.int32)
    onehot = (ids_all[:, None] == jnp.arange(types, dtype=jnp.int32)[None, :]).astype(jnp.bfloat16)
    columns = lax.dot_general(onehot, rows_all, (((0,), (0,)), ((), ())), preferred_element_type=jnp.float32)
    columns = columns * scale
    per = types // count
    back = jnp.concatenate(
        [columns.reshape(count, per, narrow), gain_term.reshape(count, 1, narrow)], axis=1
    )
    back = lax.all_to_all(back, every, 0, 0, tiled=True)
    table_grad = back[:, :per].transpose(1, 0, 2).reshape(per, width)
    gain_grad = back[:, per].sum(axis=0)
    return table_grad, gain_grad


def body(events, type_ids, type_table, norm_gain, kernel, upstream):
    length = events.shape[1]
    width = events.shape[2]
    chans = width // GROUPS
    half = KERNEL // 2
    fsdp = lax.axis_size("fsdp")
    seq_count = lax.axis_size("seq")
    total = length * seq_count * fsdp
    scale = 1.0 / jnp.sqrt(jnp.float32(total))
    table = gather_rows(type_table, "fsdp")
    types = table.shape[0]
    onehot = (type_ids[0][:, None] == jnp.arange(types, dtype=jnp.int32)[None, :]).astype(jnp.bfloat16)
    mixed = events[0].astype(jnp.float32) + jnp.dot(onehot, table, preferred_element_type=jnp.float32)
    inv = lax.rsqrt(jnp.mean(mixed * mixed, axis=-1, keepdims=True) + 1e-06)
    normed = (mixed * inv * norm_gain).astype(jnp.bfloat16)
    normed_g = normed.reshape(length, GROUPS, chans).transpose(1, 0, 2)
    padded = with_halo(normed_g, "seq", 1, 2 * half)
    up_g = upstream[0].reshape(length, GROUPS, chans).transpose(1, 0, 2)
    up_pad = with_halo(up_g, "seq", 1, half)
    weights = lax.all_gather(kernel, "fsdp", axis=0, tiled=True).reshape(GROUPS, chans, KERNEL * chans)
    up_float = upstream[0].astype(jnp.float32)
    dpad = conv_dconv(padded.astype(jnp.float32), weights, up_pad.astype(jnp.float32))
    dconv = dpad[:, half : half + length]
    if seq_count <= GROUPS:
        group_in = lax.all_to_all(normed_g, "seq", 0, 1, tiled=True)
        group_out = lax.all_to_all(dconv, "seq", 0, 1, tiled=True)
    else:
        group_in, group_out = spread_groups(normed, dconv.transpose(1, 0, 2).reshape(length, width), chans)
    local_groups = group_in.shape[0]
    whole = group_in.shape[1]
    group_pad = jnp.pad(group_in, ((0, 0), (half, half), (0, 0)))
    kterms = [
        jnp.einsum("gto,gtc->goc", group_out, group_pad[:, k : k + whole], preferred_element_type=jnp.float32)
        for k in range(KERNEL)
    ]
    kernel_part = jnp.concatenate(kterms, axis=-1).reshape(-1, KERNEL * chans) * scale
    kernel_part, dpad = lax.optimization_barrier((kernel_part, dpad))
    dnormed = conv_transpose(dpad.astype(jnp.float32), weights, length)
    dnormed = dnormed.transpose(1, 0, 2).reshape(length, width)
    gain_term = jnp.sum(dnormed * mixed * inv, axis=0) * scale
    scaled = norm_gain * dnormed
    dmixed = inv * scaled - mixed * inv * inv * inv * jnp.mean(scaled * mixed, axis=-1, keepdims=True)
    input_grad = (up_float + dmixed).astype(jnp.bfloat16)
    kernel_grad = lax.psum(kernel_part, "fsdp")
    table_grad, gain_grad = table_and_gain(input_grad, type_ids[0], gain_term, types, scale)
    return (input_grad[None], table_grad, gain_grad, kernel_grad)


def solution(mesh):
    return jax.shard_map(
        body,
        mesh=mesh,
        in_specs=(
            P("fsdp", "seq", None),
            P("fsdp", "seq"),
            P("fsdp", None),
            P(),
            P("fsdp", None),
            P("fsdp", "seq", None),
        ),
        out_specs=(
            P("fsdp", "seq", None),
            P(("fsdp", "seq"), None),
            P(("fsdp", "seq")),
            P("seq", None),
        ),
        check_vma=False,
    )
```

```python
import jax
import jax.numpy as jnp
from jax import lax
from jax.experimental import pallas as pl
from jax.experimental.pallas import tpu as pltpu
from jax.sharding import PartitionSpec as P

GROUPS = 16
KERNEL = 9


def with_halo(cells, axis, dim, width):
    count = lax.axis_size(axis)
    ends = count - 1
    head = lax.slice_in_dim(cells, 0, width, axis=dim)
    tail = lax.slice_in_dim(cells, cells.shape[dim] - width, cells.shape[dim], axis=dim)
    return jnp.concatenate(
        [
            lax.ppermute(tail, axis, [(i, (i + 1) % count) for i in range(ends)]),
            cells,
            lax.ppermute(head, axis, [((i + 1) % count, i) for i in range(ends)]),
        ],
        axis=dim,
    )


def from_partner(value, axis, apart):
    mask = 2**apart
    pairs = [(source, source ^ mask) for source in range(lax.axis_size(axis))]
    return lax.ppermute(value, axis, pairs)


def gather_rows(block, axis):
    count = lax.axis_size(axis)
    return lax.all_to_all(jnp.tile(block, (count,) + (1,) * (block.ndim - 1)), axis, 0, 0, tiled=True)


STEP_GROUPS = 4


def forward_kernel(pad_ref, w_ref, up_ref, out_ref):
    length = out_ref.shape[1]
    chans = pad_ref.shape[2]
    for g in range(out_ref.shape[0]):
        acc = None
        for k in range(KERNEL):
            x = pad_ref[g, k : k + length, :].astype(jnp.bfloat16)
            w = w_ref[g, :, k * chans : (k + 1) * chans]
            term = lax.dot_general(x, w, (((1,), (1,)), ((), ())), preferred_element_type=jnp.float32)
            acc = term if acc is None else acc + term
        sig = 1.0 / (1.0 + jnp.exp(-acc))
        out_ref[g] = (up_ref[g] * sig * (1.0 + acc * (1.0 - sig))).astype(out_ref.dtype)


def backward_kernel(pad_ref, w_ref, out_ref):
    length = out_ref.shape[1]
    chans = out_ref.shape[2]
    half = KERNEL // 2
    for g in range(out_ref.shape[0]):
        acc = None
        for k in range(KERNEL):
            x = pad_ref[g, 2 * half - k : 2 * half - k + length, :].astype(jnp.bfloat16)
            w = w_ref[g, :, k * chans : (k + 1) * chans]
            term = jnp.dot(x, w, preferred_element_type=jnp.float32)
            acc = term if acc is None else acc + term
        out_ref[g] = acc


def conv_dconv(padded, weights, up):
    groups, rows, chans = padded.shape
    length = up.shape[1]
    step = STEP_GROUPS if groups % STEP_GROUPS == 0 else 1
    flops = 2 * groups * length * chans * weights.shape[1] * KERNEL
    return pl.pallas_call(
        forward_kernel,
        grid=(groups // step,),
        in_specs=[
            pl.BlockSpec((step, rows, chans), lambda i: (i, 0, 0)),
            pl.BlockSpec((step, weights.shape[1], weights.shape[2]), lambda i: (i, 0, 0)),
            pl.BlockSpec((step, length, up.shape[2]), lambda i: (i, 0, 0)),
        ],
        out_specs=pl.BlockSpec((step, length, up.shape[2]), lambda i: (i, 0, 0)),
        out_shape=jax.ShapeDtypeStruct(up.shape, jnp.bfloat16),
        cost_estimate=pl.CostEstimate(
            flops=flops,
            transcendentals=up.size,
            bytes_accessed=padded.size * 4 + weights.size * 2 + up.size * 6,
        ),
    )(padded, weights, up)


def conv_transpose(dpad, weights, length):
    groups, rows, outs = dpad.shape
    chans = weights.shape[2] // KERNEL
    step = STEP_GROUPS if groups % STEP_GROUPS == 0 else 1
    return pl.pallas_call(
        backward_kernel,
        grid=(groups // step,),
        in_specs=[
            pl.BlockSpec((step, rows, outs), lambda i: (i, 0, 0)),
            pl.BlockSpec((step, weights.shape[1], weights.shape[2]), lambda i: (i, 0, 0)),
        ],
        out_specs=pl.BlockSpec((step, length, chans), lambda i: (i, 0, 0)),
        out_shape=jax.ShapeDtypeStruct((groups, length, chans), jnp.float32),
        cost_estimate=pl.CostEstimate(
            flops=2 * groups * length * chans * outs * KERNEL,
            transcendentals=0,
            bytes_accessed=dpad.size * 4 + weights.size * 2 + groups * length * chans * 4,
        ),
    )(dpad, weights)


def spread_groups(normed, dflat, chans):
    normed_slice = lax.all_to_all(normed, "seq", 1, 0, tiled=True)
    dconv_slice = lax.all_to_all(dflat, "seq", 1, 0, tiled=True)
    whole, slice_width = normed_slice.shape
    spread = chans // slice_width
    position = lax.axis_index("seq")
    group_rows = normed_slice
    for bit in range(spread.bit_length() - 1):
        partner = from_partner(group_rows, "seq", bit)
        lower = position >> bit & 1 == 0
        group_rows = jnp.where(
            lower,
            jnp.concatenate([group_rows, partner], axis=1),
            jnp.concatenate([partner, group_rows], axis=1),
        )
    return group_rows.reshape(1, whole, chans), dconv_slice.reshape(1, whole, slice_width)


def sum_rows(block, axis):
    count = lax.axis_size(axis)
    parts = block.reshape(count, block.shape[0] // count, *block.shape[1:])
    return lax.all_to_all(parts, axis, 0, 0, tiled=True).sum(axis=0)


def psum_rows(block, axis):
    return gather_rows(sum_rows(block, axis), axis)


def table_and_gain(input_grad, ids, gain_term, types, scale):
    every = ("fsdp", "seq")
    count = lax.axis_size("fsdp") * lax.axis_size("seq")
    length, width = input_grad.shape
    narrow = width // count
    id_rows = -(-length // narrow)
    ids_wide = jnp.zeros((id_rows * narrow,), jnp.bfloat16).at[:length].set(ids.astype(jnp.bfloat16))
    send = jnp.concatenate(
        [
            input_grad.reshape(length, count, narrow).transpose(1, 0, 2),
            jnp.broadcast_to(ids_wide.reshape(1, id_rows, narrow), (count, id_rows, narrow)),
        ],
        axis=1,
    )
    got = lax.all_to_all(send, every, 0, 0, tiled=True)
    rows_all = got[:, :length].reshape(count * length, narrow)
    ids_all = got[:, length:].reshape(count, id_rows * narrow)[:, :length].reshape(-1).astype(jnp.int32)
    onehot = (ids_all[:, None] == jnp.arange(types, dtype=jnp.int32)[None, :]).astype(jnp.bfloat16)
    columns = lax.dot_general(onehot, rows_all, (((0,), (0,)), ((), ())), preferred_element_type=jnp.float32)
    columns = columns * scale
    per = types // count
    back = jnp.concatenate(
        [columns.reshape(count, per, narrow), gain_term.reshape(count, 1, narrow)], axis=1
    )
    back = lax.all_to_all(back, every, 0, 0, tiled=True)
    table_grad = back[:, :per].transpose(1, 0, 2).reshape(per, width)
    gain_grad = back[:, per].sum(axis=0)
    return table_grad, gain_grad


def gather_by_halves(block, gather):
    core = lax.axis_index("seq") % 2
    half_rows = block.shape[0] // 2
    mine = gather(lax.dynamic_slice_in_dim(block, core * half_rows, half_rows, axis=0))
    other = from_partner(mine, "seq", 0)
    lower = jnp.where(core == 0, mine, other)
    upper = jnp.where(core == 0, other, mine)
    return jnp.stack([lower, upper], axis=1).reshape(-1, block.shape[1])


def body(events, type_ids, type_table, norm_gain, kernel, upstream):
    length = events.shape[1]
    width = events.shape[2]
    chans = width // GROUPS
    half = KERNEL // 2
    fsdp = lax.axis_size("fsdp")
    seq_count = lax.axis_size("seq")
    total = length * seq_count * fsdp
    scale = 1.0 / jnp.sqrt(jnp.float32(total))
    fsdp_parts = lambda part: gather_rows(part, "fsdp").reshape(fsdp, *part.shape)
    table = gather_by_halves(type_table, fsdp_parts)
    types = table.shape[0]
    onehot = (type_ids[0][:, None] == jnp.arange(types, dtype=jnp.int32)[None, :]).astype(jnp.bfloat16)
    mixed = events[0].astype(jnp.float32) + jnp.dot(onehot, table, preferred_element_type=jnp.float32)
    inv = lax.rsqrt(jnp.mean(mixed * mixed, axis=-1, keepdims=True) + 1e-06)
    normed = (mixed * inv * norm_gain).astype(jnp.bfloat16)
    normed_g = normed.reshape(length, GROUPS, chans).transpose(1, 0, 2)
    padded = with_halo(normed_g, "seq", 1, half)
    weights = gather_by_halves(kernel, lambda part: lax.all_gather(part, "fsdp", axis=0))
    weights = weights.reshape(GROUPS, chans, KERNEL * chans)
    up_float = upstream[0].astype(jnp.float32)
    up_g = up_float.reshape(length, GROUPS, chans).transpose(1, 0, 2)
    dconv = conv_dconv(padded.astype(jnp.float32), weights, up_g)
    dpad = with_halo(dconv, "seq", 1, half)
    dnormed = conv_transpose(dpad.astype(jnp.float32), weights, length)
    if seq_count <= GROUPS:
        group_in = lax.all_to_all(normed_g, "seq", 0, 1, tiled=True)
        group_out = lax.all_to_all(dconv, "seq", 0, 1, tiled=True)
    else:
        group_in, group_out = spread_groups(normed, dconv.transpose(1, 0, 2).reshape(length, width), chans)
    local_groups = group_in.shape[0]
    whole = group_in.shape[1]
    group_pad = jnp.pad(group_in, ((0, 0), (half, half), (0, 0)))
    kterms = [
        jnp.einsum("gto,gtc->goc", group_out, group_pad[:, k : k + whole], preferred_element_type=jnp.float32)
        for k in range(KERNEL)
    ]
    kernel_part = jnp.concatenate(kterms, axis=-1).reshape(-1, KERNEL * chans) * scale
    dnormed = dnormed.transpose(1, 0, 2).reshape(length, width)
    gain_term = jnp.sum(dnormed * mixed * inv, axis=0) * scale
    scaled = norm_gain * dnormed
    dmixed = inv * scaled - mixed * inv * inv * inv * jnp.mean(scaled * mixed, axis=-1, keepdims=True)
    input_grad = (up_float + dmixed).astype(jnp.bfloat16)
    kernel_grad = lax.psum(kernel_part, "fsdp")
    table_grad, gain_grad = table_and_gain(input_grad, type_ids[0], gain_term, types, scale)
    return (input_grad[None], table_grad, gain_grad, kernel_grad)


def solution(mesh):
    return jax.shard_map(
        body,
        mesh=mesh,
        in_specs=(
            P("fsdp", "seq", None),
            P("fsdp", "seq"),
            P("fsdp", None),
            P(),
            P("fsdp", None),
            P("fsdp", "seq", None),
        ),
        out_specs=(
            P("fsdp", "seq", None),
            P(("fsdp", "seq"), None),
            P(("fsdp", "seq")),
            P("seq", None),
        ),
        check_vma=False,
    )
```

```python
import jax
import jax.numpy as jnp
from jax import lax
from jax.experimental import pallas as pl
from jax.experimental.pallas import tpu as pltpu
from jax.sharding import PartitionSpec as P

GROUPS = 16
KERNEL = 9


def with_halo(cells, axis, dim, width):
    count = lax.axis_size(axis)
    ends = count - 1
    head = lax.slice_in_dim(cells, 0, width, axis=dim)
    tail = lax.slice_in_dim(cells, cells.shape[dim] - width, cells.shape[dim], axis=dim)
    return jnp.concatenate(
        [
            lax.ppermute(tail, axis, [(i, (i + 1) % count) for i in range(ends)]),
            cells,
            lax.ppermute(head, axis, [((i + 1) % count, i) for i in range(ends)]),
        ],
        axis=dim,
    )


def from_partner(value, axis, apart):
    mask = 2**apart
    pairs = [(source, source ^ mask) for source in range(lax.axis_size(axis))]
    return lax.ppermute(value, axis, pairs)


def gather_rows(block, axis):
    count = lax.axis_size(axis)
    return lax.all_to_all(jnp.tile(block, (count,) + (1,) * (block.ndim - 1)), axis, 0, 0, tiled=True)


STEP_GROUPS = 4


def forward_kernel(pad_ref, w_ref, up_ref, out_ref):
    length = out_ref.shape[1]
    chans = pad_ref.shape[2]
    for g in range(out_ref.shape[0]):
        acc = None
        for k in range(KERNEL):
            x = pad_ref[g, k : k + length, :].astype(jnp.bfloat16)
            w = w_ref[g, :, k * chans : (k + 1) * chans]
            term = lax.dot_general(x, w, (((1,), (1,)), ((), ())), preferred_element_type=jnp.float32)
            acc = term if acc is None else acc + term
        sig = 1.0 / (1.0 + jnp.exp(-acc))
        out_ref[g] = (up_ref[g] * sig * (1.0 + acc * (1.0 - sig))).astype(out_ref.dtype)


def backward_kernel(pad_ref, w_ref, out_ref):
    length = out_ref.shape[1]
    chans = out_ref.shape[2]
    half = KERNEL // 2
    for g in range(out_ref.shape[0]):
        acc = None
        for k in range(KERNEL):
            x = pad_ref[g, 2 * half - k : 2 * half - k + length, :].astype(jnp.bfloat16)
            w = w_ref[g, :, k * chans : (k + 1) * chans]
            term = jnp.dot(x, w, preferred_element_type=jnp.float32)
            acc = term if acc is None else acc + term
        out_ref[g] = acc


def conv_dconv(padded, weights, up):
    groups, rows, chans = padded.shape
    length = up.shape[1]
    step = STEP_GROUPS if groups % STEP_GROUPS == 0 else 1
    flops = 2 * groups * length * chans * weights.shape[1] * KERNEL
    return pl.pallas_call(
        forward_kernel,
        grid=(groups // step,),
        in_specs=[
            pl.BlockSpec((step, rows, chans), lambda i: (i, 0, 0)),
            pl.BlockSpec((step, weights.shape[1], weights.shape[2]), lambda i: (i, 0, 0)),
            pl.BlockSpec((step, length, up.shape[2]), lambda i: (i, 0, 0)),
        ],
        out_specs=pl.BlockSpec((step, length, up.shape[2]), lambda i: (i, 0, 0)),
        out_shape=jax.ShapeDtypeStruct(up.shape, jnp.bfloat16),
        cost_estimate=pl.CostEstimate(
            flops=flops,
            transcendentals=up.size,
            bytes_accessed=padded.size * 4 + weights.size * 2 + up.size * 6,
        ),
    )(padded, weights, up)


def conv_transpose(dpad, weights, length):
    groups, rows, outs = dpad.shape
    chans = weights.shape[2] // KERNEL
    step = STEP_GROUPS if groups % STEP_GROUPS == 0 else 1
    return pl.pallas_call(
        backward_kernel,
        grid=(groups // step,),
        in_specs=[
            pl.BlockSpec((step, rows, outs), lambda i: (i, 0, 0)),
            pl.BlockSpec((step, weights.shape[1], weights.shape[2]), lambda i: (i, 0, 0)),
        ],
        out_specs=pl.BlockSpec((step, length, chans), lambda i: (i, 0, 0)),
        out_shape=jax.ShapeDtypeStruct((groups, length, chans), jnp.float32),
        cost_estimate=pl.CostEstimate(
            flops=2 * groups * length * chans * outs * KERNEL,
            transcendentals=0,
            bytes_accessed=dpad.size * 4 + weights.size * 2 + groups * length * chans * 4,
        ),
    )(dpad, weights)


def spread_groups(normed, dflat, chans):
    normed_slice = lax.all_to_all(normed, "seq", 1, 0, tiled=True)
    dconv_slice = lax.all_to_all(dflat, "seq", 1, 0, tiled=True)
    whole, slice_width = normed_slice.shape
    spread = chans // slice_width
    position = lax.axis_index("seq")
    group_rows = normed_slice
    for bit in range(spread.bit_length() - 1):
        partner = from_partner(group_rows, "seq", bit)
        lower = position >> bit & 1 == 0
        group_rows = jnp.where(
            lower,
            jnp.concatenate([group_rows, partner], axis=1),
            jnp.concatenate([partner, group_rows], axis=1),
        )
    return group_rows.reshape(1, whole, chans), dconv_slice.reshape(1, whole, slice_width)


def sum_rows(block, axis):
    count = lax.axis_size(axis)
    parts = block.reshape(count, block.shape[0] // count, *block.shape[1:])
    return lax.all_to_all(parts, axis, 0, 0, tiled=True).sum(axis=0)


def psum_rows(block, axis):
    return gather_rows(sum_rows(block, axis), axis)


def table_and_gain(input_grad, ids, gain_term, types, scale):
    every = ("fsdp", "seq")
    count = lax.axis_size("fsdp") * lax.axis_size("seq")
    length, width = input_grad.shape
    narrow = width // count
    id_rows = -(-length // narrow)
    ids_wide = jnp.zeros((id_rows * narrow,), jnp.bfloat16).at[:length].set(ids.astype(jnp.bfloat16))
    send = jnp.concatenate(
        [
            input_grad.reshape(length, count, narrow).transpose(1, 0, 2),
            jnp.broadcast_to(ids_wide.reshape(1, id_rows, narrow), (count, id_rows, narrow)),
        ],
        axis=1,
    )
    got = lax.all_to_all(send, every, 0, 0, tiled=True)
    rows_all = got[:, :length].reshape(count * length, narrow)
    ids_all = got[:, length:].reshape(count, id_rows * narrow)[:, :length].reshape(-1).astype(jnp.int32)
    onehot = (ids_all[:, None] == jnp.arange(types, dtype=jnp.int32)[None, :]).astype(jnp.bfloat16)
    columns = lax.dot_general(onehot, rows_all, (((0,), (0,)), ((), ())), preferred_element_type=jnp.float32)
    columns = columns * scale
    per = types // count
    back = jnp.concatenate(
        [columns.reshape(count, per, narrow), gain_term.reshape(count, 1, narrow)], axis=1
    )
    back = lax.all_to_all(back, every, 0, 0, tiled=True)
    table_grad = back[:, :per].transpose(1, 0, 2).reshape(per, width)
    gain_grad = back[:, per].sum(axis=0)
    return table_grad, gain_grad


def body(events, type_ids, type_table, norm_gain, kernel, upstream):
    length = events.shape[1]
    width = events.shape[2]
    chans = width // GROUPS
    half = KERNEL // 2
    fsdp = lax.axis_size("fsdp")
    seq_count = lax.axis_size("seq")
    total = length * seq_count * fsdp
    scale = 1.0 / jnp.sqrt(jnp.float32(total))
    table = gather_rows(type_table, "fsdp")
    types = table.shape[0]
    onehot = (type_ids[0][:, None] == jnp.arange(types, dtype=jnp.int32)[None, :]).astype(jnp.bfloat16)
    mixed = events[0].astype(jnp.float32) + jnp.dot(onehot, table, preferred_element_type=jnp.float32)
    inv = lax.rsqrt(jnp.mean(mixed * mixed, axis=-1, keepdims=True) + 1e-06)
    normed = (mixed * inv * norm_gain).astype(jnp.bfloat16)
    normed_g = normed.reshape(length, GROUPS, chans).transpose(1, 0, 2)
    padded = with_halo(normed_g, "seq", 1, half)
    weights = lax.all_gather(kernel, "fsdp", axis=0, tiled=True).reshape(GROUPS, chans, KERNEL * chans)
    up_float = upstream[0].astype(jnp.float32)
    up_g = up_float.reshape(length, GROUPS, chans).transpose(1, 0, 2)
    dconv = conv_dconv(padded.astype(jnp.float32), weights, up_g)
    dpad = with_halo(dconv, "seq", 1, half)
    dnormed = conv_transpose(dpad.astype(jnp.float32), weights, length)
    if seq_count <= GROUPS:
        group_in = lax.all_to_all(normed_g, "seq", 0, 1, tiled=True)
        group_out = lax.all_to_all(dconv, "seq", 0, 1, tiled=True)
    else:
        group_in, group_out = spread_groups(normed, dconv.transpose(1, 0, 2).reshape(length, width), chans)
    local_groups, whole, outs = group_out.shape
    splits = fsdp // local_groups
    share = outs // splits
    send_out = group_out.reshape(local_groups, whole, splits, share).transpose(0, 2, 1, 3).reshape(fsdp, whole, share)
    send_in = jnp.stack([group_in[part // splits] for part in range(fsdp)])
    streams_out = lax.all_to_all(send_out, "fsdp", 0, 0, tiled=True)
    streams_in = lax.all_to_all(send_in, "fsdp", 0, 0, tiled=True)
    streams_pad = jnp.pad(streams_in, ((0, 0), (half, half), (0, 0)))
    kterms = [
        jnp.einsum("sto,stc->oc", streams_out, streams_pad[:, k : k + whole], preferred_element_type=jnp.float32)
        for k in range(KERNEL)
    ]
    kernel_rows = jnp.concatenate(kterms, axis=-1) * scale
    kernel_grad = lax.all_gather(kernel_rows, "fsdp", axis=0, tiled=True)
    dnormed = dnormed.transpose(1, 0, 2).reshape(length, width)
    gain_term = jnp.sum(dnormed * mixed * inv, axis=0) * scale
    scaled = norm_gain * dnormed
    dmixed = inv * scaled - mixed * inv * inv * inv * jnp.mean(scaled * mixed, axis=-1, keepdims=True)
    input_grad = (up_float + dmixed).astype(jnp.bfloat16)
    table_grad, gain_grad = table_and_gain(input_grad, type_ids[0], gain_term, types, scale)
    return (input_grad[None], table_grad, gain_grad, kernel_grad)


def solution(mesh):
    return jax.shard_map(
        body,
        mesh=mesh,
        in_specs=(
            P("fsdp", "seq", None),
            P("fsdp", "seq"),
            P("fsdp", None),
            P(),
            P("fsdp", None),
            P("fsdp", "seq", None),
        ),
        out_specs=(
            P("fsdp", "seq", None),
            P(("fsdp", "seq"), None),
            P(("fsdp", "seq")),
            P("seq", None),
        ),
        check_vma=False,
    )
```

```python
import jax
import jax.numpy as jnp
from jax import lax
from jax.experimental import pallas as pl
from jax.experimental.pallas import tpu as pltpu
from jax.sharding import PartitionSpec as P

GROUPS = 16
KERNEL = 9


def with_halo(cells, axis, dim, width):
    count = lax.axis_size(axis)
    ends = count - 1
    head = lax.slice_in_dim(cells, 0, width, axis=dim)
    tail = lax.slice_in_dim(cells, cells.shape[dim] - width, cells.shape[dim], axis=dim)
    return jnp.concatenate(
        [
            lax.ppermute(tail, axis, [(i, (i + 1) % count) for i in range(ends)]),
            cells,
            lax.ppermute(head, axis, [((i + 1) % count, i) for i in range(ends)]),
        ],
        axis=dim,
    )


def from_partner(value, axis, apart):
    mask = 2**apart
    pairs = [(source, source ^ mask) for source in range(lax.axis_size(axis))]
    return lax.ppermute(value, axis, pairs)


def gather_rows(block, axis):
    count = lax.axis_size(axis)
    return lax.all_to_all(jnp.tile(block, (count,) + (1,) * (block.ndim - 1)), axis, 0, 0, tiled=True)


STEP_GROUPS = 4


def forward_kernel(pad_ref, w_ref, up_ref, out_ref):
    length = out_ref.shape[1]
    chans = pad_ref.shape[2]
    for g in range(out_ref.shape[0]):
        acc = None
        for k in range(KERNEL):
            x = pad_ref[g, k : k + length, :].astype(jnp.bfloat16)
            w = w_ref[g, :, k * chans : (k + 1) * chans]
            term = lax.dot_general(x, w, (((1,), (1,)), ((), ())), preferred_element_type=jnp.float32)
            acc = term if acc is None else acc + term
        sig = 1.0 / (1.0 + jnp.exp(-acc))
        out_ref[g] = (up_ref[g] * sig * (1.0 + acc * (1.0 - sig))).astype(out_ref.dtype)


def backward_kernel(pad_ref, w_ref, out_ref):
    length = out_ref.shape[1]
    chans = out_ref.shape[2]
    half = KERNEL // 2
    for g in range(out_ref.shape[0]):
        acc = None
        for k in range(KERNEL):
            x = pad_ref[g, 2 * half - k : 2 * half - k + length, :].astype(jnp.bfloat16)
            w = w_ref[g, :, k * chans : (k + 1) * chans]
            term = jnp.dot(x, w, preferred_element_type=jnp.float32)
            acc = term if acc is None else acc + term
        out_ref[g] = acc


def conv_dconv(padded, weights, up):
    groups, rows, chans = padded.shape
    length = up.shape[1]
    step = STEP_GROUPS if groups % STEP_GROUPS == 0 else 1
    flops = 2 * groups * length * chans * weights.shape[1] * KERNEL
    return pl.pallas_call(
        forward_kernel,
        grid=(groups // step,),
        in_specs=[
            pl.BlockSpec((step, rows, chans), lambda i: (i, 0, 0)),
            pl.BlockSpec((step, weights.shape[1], weights.shape[2]), lambda i: (i, 0, 0)),
            pl.BlockSpec((step, length, up.shape[2]), lambda i: (i, 0, 0)),
        ],
        out_specs=pl.BlockSpec((step, length, up.shape[2]), lambda i: (i, 0, 0)),
        out_shape=jax.ShapeDtypeStruct(up.shape, jnp.bfloat16),
        cost_estimate=pl.CostEstimate(
            flops=flops,
            transcendentals=up.size,
            bytes_accessed=padded.size * 4 + weights.size * 2 + up.size * 6,
        ),
    )(padded, weights, up)


def conv_transpose(dpad, weights, length):
    groups, rows, outs = dpad.shape
    chans = weights.shape[2] // KERNEL
    step = STEP_GROUPS if groups % STEP_GROUPS == 0 else 1
    return pl.pallas_call(
        backward_kernel,
        grid=(groups // step,),
        in_specs=[
            pl.BlockSpec((step, rows, outs), lambda i: (i, 0, 0)),
            pl.BlockSpec((step, weights.shape[1], weights.shape[2]), lambda i: (i, 0, 0)),
        ],
        out_specs=pl.BlockSpec((step, length, chans), lambda i: (i, 0, 0)),
        out_shape=jax.ShapeDtypeStruct((groups, length, chans), jnp.float32),
        cost_estimate=pl.CostEstimate(
            flops=2 * groups * length * chans * outs * KERNEL,
            transcendentals=0,
            bytes_accessed=dpad.size * 4 + weights.size * 2 + groups * length * chans * 4,
        ),
    )(dpad, weights)


def spread_groups(normed, dflat, chans):
    normed_slice = lax.all_to_all(normed, "seq", 1, 0, tiled=True)
    dconv_slice = lax.all_to_all(dflat, "seq", 1, 0, tiled=True)
    whole, slice_width = normed_slice.shape
    spread = chans // slice_width
    position = lax.axis_index("seq")
    group_rows = normed_slice
    for bit in range(spread.bit_length() - 1):
        partner = from_partner(group_rows, "seq", bit)
        lower = position >> bit & 1 == 0
        group_rows = jnp.where(
            lower,
            jnp.concatenate([group_rows, partner], axis=1),
            jnp.concatenate([partner, group_rows], axis=1),
        )
    return group_rows.reshape(1, whole, chans), dconv_slice.reshape(1, whole, slice_width)


def sum_rows(block, axis):
    count = lax.axis_size(axis)
    parts = block.reshape(count, block.shape[0] // count, *block.shape[1:])
    return lax.all_to_all(parts, axis, 0, 0, tiled=True).sum(axis=0)


def psum_rows(block, axis):
    return gather_rows(sum_rows(block, axis), axis)


def table_and_gain(input_grad, ids, gain_term, types, scale):
    every = ("fsdp", "seq")
    count = lax.axis_size("fsdp") * lax.axis_size("seq")
    length, width = input_grad.shape
    narrow = width // count
    id_rows = -(-length // narrow)
    ids_wide = jnp.zeros((id_rows * narrow,), jnp.bfloat16).at[:length].set(ids.astype(jnp.bfloat16))
    send = jnp.concatenate(
        [
            input_grad.reshape(length, count, narrow).transpose(1, 0, 2),
            jnp.broadcast_to(ids_wide.reshape(1, id_rows, narrow), (count, id_rows, narrow)),
        ],
        axis=1,
    )
    got = lax.all_to_all(send, every, 0, 0, tiled=True)
    rows_all = got[:, :length].reshape(count * length, narrow)
    ids_all = got[:, length:].reshape(count, id_rows * narrow)[:, :length].reshape(-1).astype(jnp.int32)
    onehot = (ids_all[:, None] == jnp.arange(types, dtype=jnp.int32)[None, :]).astype(jnp.bfloat16)
    columns = lax.dot_general(onehot, rows_all, (((0,), (0,)), ((), ())), preferred_element_type=jnp.float32)
    columns = columns * scale
    per = types // count
    back = jnp.concatenate(
        [columns.reshape(count, per, narrow), gain_term.reshape(count, 1, narrow)], axis=1
    )
    back = lax.all_to_all(back, every, 0, 0, tiled=True)
    table_grad = back[:, :per].transpose(1, 0, 2).reshape(per, width)
    gain_grad = back[:, per].sum(axis=0)
    return table_grad, gain_grad


def psum_by_permutes(block, axis):
    count = lax.axis_size(axis)
    if count & (count - 1):
        return lax.psum(block, axis)
    me = lax.axis_index(axis)
    rows = block.shape[0] // count
    chunk = lambda index: lax.dynamic_slice_in_dim(block, index * rows, rows, axis=0)
    total = chunk(me)
    for apart in range(1, count):
        pairs = [(source, source ^ apart) for source in range(count)]
        total = total + lax.ppermute(chunk(me ^ apart), axis, pairs)
    pieces = [total]
    for apart in range(1, count):
        pairs = [(source, source ^ apart) for source in range(count)]
        pieces.append(lax.ppermute(total, axis, pairs))
    stacked = jnp.stack(pieces)
    return jnp.concatenate(
        [lax.dynamic_index_in_dim(stacked, index ^ me, keepdims=False) for index in range(count)], axis=0
    )


def body(events, type_ids, type_table, norm_gain, kernel, upstream):
    length = events.shape[1]
    width = events.shape[2]
    chans = width // GROUPS
    half = KERNEL // 2
    fsdp = lax.axis_size("fsdp")
    seq_count = lax.axis_size("seq")
    total = length * seq_count * fsdp
    scale = 1.0 / jnp.sqrt(jnp.float32(total))
    table = gather_rows(type_table, "fsdp")
    types = table.shape[0]
    onehot = (type_ids[0][:, None] == jnp.arange(types, dtype=jnp.int32)[None, :]).astype(jnp.bfloat16)
    mixed = events[0].astype(jnp.float32) + jnp.dot(onehot, table, preferred_element_type=jnp.float32)
    inv = lax.rsqrt(jnp.mean(mixed * mixed, axis=-1, keepdims=True) + 1e-06)
    normed = (mixed * inv * norm_gain).astype(jnp.bfloat16)
    normed_g = normed.reshape(length, GROUPS, chans).transpose(1, 0, 2)
    padded = with_halo(normed_g, "seq", 1, half)
    weights = lax.all_gather(kernel, "fsdp", axis=0, tiled=True).reshape(GROUPS, chans, KERNEL * chans)
    up_float = upstream[0].astype(jnp.float32)
    up_g = up_float.reshape(length, GROUPS, chans).transpose(1, 0, 2)
    dconv = conv_dconv(padded.astype(jnp.float32), weights, up_g)
    dpad = with_halo(dconv, "seq", 1, half)
    dnormed = conv_transpose(dpad.astype(jnp.float32), weights, length)
    if seq_count <= GROUPS:
        group_in = lax.all_to_all(normed_g, "seq", 0, 1, tiled=True)
        group_out = lax.all_to_all(dconv, "seq", 0, 1, tiled=True)
    else:
        group_in, group_out = spread_groups(normed, dconv.transpose(1, 0, 2).reshape(length, width), chans)
    local_groups = group_in.shape[0]
    whole = group_in.shape[1]
    group_pad = jnp.pad(group_in, ((0, 0), (half, half), (0, 0)))
    kterms = [
        jnp.einsum("gto,gtc->goc", group_out, group_pad[:, k : k + whole], preferred_element_type=jnp.float32)
        for k in range(KERNEL)
    ]
    kernel_part = jnp.concatenate(kterms, axis=-1).reshape(-1, KERNEL * chans) * scale
    dnormed = dnormed.transpose(1, 0, 2).reshape(length, width)
    gain_term = jnp.sum(dnormed * mixed * inv, axis=0) * scale
    scaled = norm_gain * dnormed
    dmixed = inv * scaled - mixed * inv * inv * inv * jnp.mean(scaled * mixed, axis=-1, keepdims=True)
    input_grad = (up_float + dmixed).astype(jnp.bfloat16)
    kernel_grad = psum_by_permutes(kernel_part, "fsdp")
    table_grad, gain_grad = table_and_gain(input_grad, type_ids[0], gain_term, types, scale)
    return (input_grad[None], table_grad, gain_grad, kernel_grad)


def solution(mesh):
    return jax.shard_map(
        body,
        mesh=mesh,
        in_specs=(
            P("fsdp", "seq", None),
            P("fsdp", "seq"),
            P("fsdp", None),
            P(),
            P("fsdp", None),
            P("fsdp", "seq", None),
        ),
        out_specs=(
            P("fsdp", "seq", None),
            P(("fsdp", "seq"), None),
            P(("fsdp", "seq")),
            P("seq", None),
        ),
        check_vma=False,
    )
```

```python
import jax
import jax.numpy as jnp
from jax import lax
from jax.experimental import pallas as pl
from jax.experimental.pallas import tpu as pltpu
from jax.sharding import PartitionSpec as P

GROUPS = 16
KERNEL = 9


def with_halo(cells, axis, dim, width):
    count = lax.axis_size(axis)
    ends = count - 1
    head = lax.slice_in_dim(cells, 0, width, axis=dim)
    tail = lax.slice_in_dim(cells, cells.shape[dim] - width, cells.shape[dim], axis=dim)
    return jnp.concatenate(
        [
            lax.ppermute(tail, axis, [(i, (i + 1) % count) for i in range(ends)]),
            cells,
            lax.ppermute(head, axis, [((i + 1) % count, i) for i in range(ends)]),
        ],
        axis=dim,
    )


def from_partner(value, axis, apart):
    mask = 2**apart
    pairs = [(source, source ^ mask) for source in range(lax.axis_size(axis))]
    return lax.ppermute(value, axis, pairs)


def gather_rows(block, axis):
    count = lax.axis_size(axis)
    return lax.all_to_all(jnp.tile(block, (count,) + (1,) * (block.ndim - 1)), axis, 0, 0, tiled=True)


STEP_GROUPS = 4


def forward_kernel(pad_ref, w_ref, up_ref, out_ref):
    length = out_ref.shape[1]
    chans = pad_ref.shape[2]
    for g in range(out_ref.shape[0]):
        acc = None
        for k in range(KERNEL):
            x = pad_ref[g, k : k + length, :].astype(jnp.bfloat16)
            w = w_ref[g, :, k * chans : (k + 1) * chans]
            term = lax.dot_general(x, w, (((1,), (1,)), ((), ())), preferred_element_type=jnp.float32)
            acc = term if acc is None else acc + term
        sig = 1.0 / (1.0 + jnp.exp(-acc))
        out_ref[g] = (up_ref[g] * sig * (1.0 + acc * (1.0 - sig))).astype(out_ref.dtype)


def backward_kernel(pad_ref, w_ref, out_ref):
    length = out_ref.shape[1]
    chans = out_ref.shape[2]
    half = KERNEL // 2
    for g in range(out_ref.shape[0]):
        acc = None
        for k in range(KERNEL):
            x = pad_ref[g, 2 * half - k : 2 * half - k + length, :].astype(jnp.bfloat16)
            w = w_ref[g, :, k * chans : (k + 1) * chans]
            term = jnp.dot(x, w, preferred_element_type=jnp.float32)
            acc = term if acc is None else acc + term
        out_ref[g] = acc


def conv_dconv(padded, weights, up):
    groups, rows, chans = padded.shape
    length = up.shape[1]
    step = STEP_GROUPS if groups % STEP_GROUPS == 0 else 1
    flops = 2 * groups * length * chans * weights.shape[1] * KERNEL
    return pl.pallas_call(
        forward_kernel,
        grid=(groups // step,),
        in_specs=[
            pl.BlockSpec((step, rows, chans), lambda i: (i, 0, 0)),
            pl.BlockSpec((step, weights.shape[1], weights.shape[2]), lambda i: (i, 0, 0)),
            pl.BlockSpec((step, length, up.shape[2]), lambda i: (i, 0, 0)),
        ],
        out_specs=pl.BlockSpec((step, length, up.shape[2]), lambda i: (i, 0, 0)),
        out_shape=jax.ShapeDtypeStruct(up.shape, jnp.bfloat16),
        cost_estimate=pl.CostEstimate(
            flops=flops,
            transcendentals=up.size,
            bytes_accessed=padded.size * 4 + weights.size * 2 + up.size * 6,
        ),
    )(padded, weights, up)


def conv_transpose(dpad, weights, length):
    groups, rows, outs = dpad.shape
    chans = weights.shape[2] // KERNEL
    step = STEP_GROUPS if groups % STEP_GROUPS == 0 else 1
    return pl.pallas_call(
        backward_kernel,
        grid=(groups // step,),
        in_specs=[
            pl.BlockSpec((step, rows, outs), lambda i: (i, 0, 0)),
            pl.BlockSpec((step, weights.shape[1], weights.shape[2]), lambda i: (i, 0, 0)),
        ],
        out_specs=pl.BlockSpec((step, length, chans), lambda i: (i, 0, 0)),
        out_shape=jax.ShapeDtypeStruct((groups, length, chans), jnp.float32),
        cost_estimate=pl.CostEstimate(
            flops=2 * groups * length * chans * outs * KERNEL,
            transcendentals=0,
            bytes_accessed=dpad.size * 4 + weights.size * 2 + groups * length * chans * 4,
        ),
    )(dpad, weights)


def spread_groups(normed, dflat, chans):
    normed_slice = lax.all_to_all(normed, "seq", 1, 0, tiled=True)
    dconv_slice = lax.all_to_all(dflat, "seq", 1, 0, tiled=True)
    whole, slice_width = normed_slice.shape
    spread = chans // slice_width
    position = lax.axis_index("seq")
    group_rows = normed_slice
    for bit in range(spread.bit_length() - 1):
        partner = from_partner(group_rows, "seq", bit)
        lower = position >> bit & 1 == 0
        group_rows = jnp.where(
            lower,
            jnp.concatenate([group_rows, partner], axis=1),
            jnp.concatenate([partner, group_rows], axis=1),
        )
    return group_rows.reshape(1, whole, chans), dconv_slice.reshape(1, whole, slice_width)


def sum_rows(block, axis):
    count = lax.axis_size(axis)
    parts = block.reshape(count, block.shape[0] // count, *block.shape[1:])
    return lax.all_to_all(parts, axis, 0, 0, tiled=True).sum(axis=0)


def psum_rows(block, axis):
    return gather_rows(sum_rows(block, axis), axis)


def table_and_gain(input_grad, ids, gain_term, types, scale, tied):
    every = ("fsdp", "seq")
    count = lax.axis_size("fsdp") * lax.axis_size("seq")
    length, width = input_grad.shape
    narrow = width // count
    id_rows = -(-length // narrow)
    ids_wide = jnp.zeros((id_rows * narrow,), jnp.bfloat16).at[:length].set(ids.astype(jnp.bfloat16))
    send = jnp.concatenate(
        [
            input_grad.reshape(length, count, narrow).transpose(1, 0, 2),
            jnp.broadcast_to(ids_wide.reshape(1, id_rows, narrow), (count, id_rows, narrow)),
        ],
        axis=1,
    )
    got = lax.all_to_all(send, every, 0, 0, tiled=True)
    rows_all = got[:, :length].reshape(count * length, narrow)
    ids_all = got[:, length:].reshape(count, id_rows * narrow)[:, :length].reshape(-1).astype(jnp.int32)
    onehot = (ids_all[:, None] == jnp.arange(types, dtype=jnp.int32)[None, :]).astype(jnp.bfloat16)
    columns = lax.dot_general(onehot, rows_all, (((0,), (0,)), ((), ())), preferred_element_type=jnp.float32)
    columns = columns * scale
    per = types // count
    back = jnp.concatenate(
        [columns.reshape(count, per, narrow), gain_term.reshape(count, 1, narrow)], axis=1
    )
    back, tied = lax.optimization_barrier((back, tied))
    back = lax.all_to_all(back, every, 0, 0, tiled=True)
    table_grad = back[:, :per].transpose(1, 0, 2).reshape(per, width)
    gain_grad = back[:, per].sum(axis=0)
    return table_grad, gain_grad, tied


def scatter_by_permutes(block, axis):
    count = lax.axis_size(axis)
    me = lax.axis_index(axis)
    rows = block.shape[0] // count
    chunk = lambda index: lax.dynamic_slice_in_dim(block, index * rows, rows, axis=0)
    total = chunk(me)
    for apart in range(1, count):
        pairs = [(source, source ^ apart) for source in range(count)]
        total = total + lax.ppermute(chunk(me ^ apart), axis, pairs)
    return total


def gather_by_permutes(total, axis):
    count = lax.axis_size(axis)
    me = lax.axis_index(axis)
    pieces = [total]
    for apart in range(1, count):
        pairs = [(source, source ^ apart) for source in range(count)]
        pieces.append(lax.ppermute(total, axis, pairs))
    stacked = jnp.stack(pieces)
    return jnp.concatenate(
        [lax.dynamic_index_in_dim(stacked, index ^ me, keepdims=False) for index in range(count)], axis=0
    )


def body(events, type_ids, type_table, norm_gain, kernel, upstream):
    length = events.shape[1]
    width = events.shape[2]
    chans = width // GROUPS
    half = KERNEL // 2
    fsdp = lax.axis_size("fsdp")
    seq_count = lax.axis_size("seq")
    total = length * seq_count * fsdp
    scale = 1.0 / jnp.sqrt(jnp.float32(total))
    table = gather_rows(type_table, "fsdp")
    types = table.shape[0]
    onehot = (type_ids[0][:, None] == jnp.arange(types, dtype=jnp.int32)[None, :]).astype(jnp.bfloat16)
    mixed = events[0].astype(jnp.float32) + jnp.dot(onehot, table, preferred_element_type=jnp.float32)
    inv = lax.rsqrt(jnp.mean(mixed * mixed, axis=-1, keepdims=True) + 1e-06)
    normed = (mixed * inv * norm_gain).astype(jnp.bfloat16)
    normed_g = normed.reshape(length, GROUPS, chans).transpose(1, 0, 2)
    padded = with_halo(normed_g, "seq", 1, half)
    weights = lax.all_gather(kernel, "fsdp", axis=0, tiled=True).reshape(GROUPS, chans, KERNEL * chans)
    up_float = upstream[0].astype(jnp.float32)
    up_g = up_float.reshape(length, GROUPS, chans).transpose(1, 0, 2)
    dconv = conv_dconv(padded.astype(jnp.float32), weights, up_g)
    dpad = with_halo(dconv, "seq", 1, half)
    dnormed = conv_transpose(dpad.astype(jnp.float32), weights, length)
    if seq_count <= GROUPS:
        group_in = lax.all_to_all(normed_g, "seq", 0, 1, tiled=True)
        group_out = lax.all_to_all(dconv, "seq", 0, 1, tiled=True)
    else:
        group_in, group_out = spread_groups(normed, dconv.transpose(1, 0, 2).reshape(length, width), chans)
    local_groups = group_in.shape[0]
    whole = group_in.shape[1]
    group_pad = jnp.pad(group_in, ((0, 0), (half, half), (0, 0)))
    kterms = [
        jnp.einsum("gto,gtc->goc", group_out, group_pad[:, k : k + whole], preferred_element_type=jnp.float32)
        for k in range(KERNEL)
    ]
    kernel_part = jnp.concatenate(kterms, axis=-1).reshape(-1, KERNEL * chans) * scale
    dnormed = dnormed.transpose(1, 0, 2).reshape(length, width)
    gain_term = jnp.sum(dnormed * mixed * inv, axis=0) * scale
    scaled = norm_gain * dnormed
    dmixed = inv * scaled - mixed * inv * inv * inv * jnp.mean(scaled * mixed, axis=-1, keepdims=True)
    input_grad = (up_float + dmixed).astype(jnp.bfloat16)
    if fsdp & (fsdp - 1):
        raise ValueError("fsdp not pow2")
    kernel_sum = scatter_by_permutes(kernel_part, "fsdp")
    table_grad, gain_grad, kernel_sum = table_and_gain(input_grad, type_ids[0], gain_term, types, scale, kernel_sum)
    kernel_grad = gather_by_permutes(kernel_sum, "fsdp")
    return (input_grad[None], table_grad, gain_grad, kernel_grad)


def solution(mesh):
    return jax.shard_map(
        body,
        mesh=mesh,
        in_specs=(
            P("fsdp", "seq", None),
            P("fsdp", "seq"),
            P("fsdp", None),
            P(),
            P("fsdp", None),
            P("fsdp", "seq", None),
        ),
        out_specs=(
            P("fsdp", "seq", None),
            P(("fsdp", "seq"), None),
            P(("fsdp", "seq")),
            P("seq", None),
        ),
        check_vma=False,
    )
```

```python
import jax
import jax.numpy as jnp
from jax import lax
from jax.experimental import pallas as pl
from jax.experimental.pallas import tpu as pltpu
from jax.sharding import PartitionSpec as P

GROUPS = 16
KERNEL = 9


def with_halo(cells, axis, dim, width):
    count = lax.axis_size(axis)
    ends = count - 1
    head = lax.slice_in_dim(cells, 0, width, axis=dim)
    tail = lax.slice_in_dim(cells, cells.shape[dim] - width, cells.shape[dim], axis=dim)
    return jnp.concatenate(
        [
            lax.ppermute(tail, axis, [(i, (i + 1) % count) for i in range(ends)]),
            cells,
            lax.ppermute(head, axis, [((i + 1) % count, i) for i in range(ends)]),
        ],
        axis=dim,
    )


def from_partner(value, axis, apart):
    mask = 2**apart
    pairs = [(source, source ^ mask) for source in range(lax.axis_size(axis))]
    return lax.ppermute(value, axis, pairs)


def gather_rows(block, axis):
    count = lax.axis_size(axis)
    return lax.all_to_all(jnp.tile(block, (count,) + (1,) * (block.ndim - 1)), axis, 0, 0, tiled=True)


STEP_GROUPS = 4


def forward_kernel(pad_ref, w_ref, up_ref, out_ref):
    length = out_ref.shape[1]
    chans = pad_ref.shape[2]
    for g in range(out_ref.shape[0]):
        acc = None
        for k in range(KERNEL):
            x = pad_ref[g, k : k + length, :].astype(jnp.bfloat16)
            w = w_ref[g, :, k * chans : (k + 1) * chans]
            term = lax.dot_general(x, w, (((1,), (1,)), ((), ())), preferred_element_type=jnp.float32)
            acc = term if acc is None else acc + term
        sig = 1.0 / (1.0 + jnp.exp(-acc))
        out_ref[g] = (up_ref[g] * sig * (1.0 + acc * (1.0 - sig))).astype(out_ref.dtype)


def backward_kernel(pad_ref, w_ref, out_ref):
    length = out_ref.shape[1]
    chans = out_ref.shape[2]
    half = KERNEL // 2
    for g in range(out_ref.shape[0]):
        acc = None
        for k in range(KERNEL):
            x = pad_ref[g, 2 * half - k : 2 * half - k + length, :].astype(jnp.bfloat16)
            w = w_ref[g, :, k * chans : (k + 1) * chans]
            term = jnp.dot(x, w, preferred_element_type=jnp.float32)
            acc = term if acc is None else acc + term
        out_ref[g] = acc


def conv_dconv(padded, weights, up):
    groups, rows, chans = padded.shape
    length = up.shape[1]
    step = STEP_GROUPS if groups % STEP_GROUPS == 0 else 1
    flops = 2 * groups * length * chans * weights.shape[1] * KERNEL
    return pl.pallas_call(
        forward_kernel,
        grid=(groups // step,),
        in_specs=[
            pl.BlockSpec((step, rows, chans), lambda i: (i, 0, 0)),
            pl.BlockSpec((step, weights.shape[1], weights.shape[2]), lambda i: (i, 0, 0)),
            pl.BlockSpec((step, length, up.shape[2]), lambda i: (i, 0, 0)),
        ],
        out_specs=pl.BlockSpec((step, length, up.shape[2]), lambda i: (i, 0, 0)),
        out_shape=jax.ShapeDtypeStruct(up.shape, jnp.bfloat16),
        cost_estimate=pl.CostEstimate(
            flops=flops,
            transcendentals=up.size,
            bytes_accessed=padded.size * 4 + weights.size * 2 + up.size * 6,
        ),
    )(padded, weights, up)


def conv_transpose(dpad, weights, length):
    groups, rows, outs = dpad.shape
    chans = weights.shape[2] // KERNEL
    step = STEP_GROUPS if groups % STEP_GROUPS == 0 else 1
    return pl.pallas_call(
        backward_kernel,
        grid=(groups // step,),
        in_specs=[
            pl.BlockSpec((step, rows, outs), lambda i: (i, 0, 0)),
            pl.BlockSpec((step, weights.shape[1], weights.shape[2]), lambda i: (i, 0, 0)),
        ],
        out_specs=pl.BlockSpec((step, length, chans), lambda i: (i, 0, 0)),
        out_shape=jax.ShapeDtypeStruct((groups, length, chans), jnp.float32),
        cost_estimate=pl.CostEstimate(
            flops=2 * groups * length * chans * outs * KERNEL,
            transcendentals=0,
            bytes_accessed=dpad.size * 4 + weights.size * 2 + groups * length * chans * 4,
        ),
    )(dpad, weights)


def spread_groups(normed, dflat, chans):
    normed_slice = lax.all_to_all(normed, "seq", 1, 0, tiled=True)
    dconv_slice = lax.all_to_all(dflat, "seq", 1, 0, tiled=True)
    whole, slice_width = normed_slice.shape
    spread = chans // slice_width
    position = lax.axis_index("seq")
    group_rows = normed_slice
    for bit in range(spread.bit_length() - 1):
        partner = from_partner(group_rows, "seq", bit)
        lower = position >> bit & 1 == 0
        group_rows = jnp.where(
            lower,
            jnp.concatenate([group_rows, partner], axis=1),
            jnp.concatenate([partner, group_rows], axis=1),
        )
    return group_rows.reshape(1, whole, chans), dconv_slice.reshape(1, whole, slice_width)


def sum_rows(block, axis):
    count = lax.axis_size(axis)
    parts = block.reshape(count, block.shape[0] // count, *block.shape[1:])
    return lax.all_to_all(parts, axis, 0, 0, tiled=True).sum(axis=0)


def psum_rows(block, axis):
    return gather_rows(sum_rows(block, axis), axis)


def table_and_gain(input_grad, ids, gain_term, types, scale, tied):
    every = ("fsdp", "seq")
    count = lax.axis_size("fsdp") * lax.axis_size("seq")
    length, width = input_grad.shape
    narrow = width // count
    id_rows = -(-length // narrow)
    ids_wide = jnp.zeros((id_rows * narrow,), jnp.bfloat16).at[:length].set(ids.astype(jnp.bfloat16))
    send = jnp.concatenate(
        [
            input_grad.reshape(length, count, narrow).transpose(1, 0, 2),
            jnp.broadcast_to(ids_wide.reshape(1, id_rows, narrow), (count, id_rows, narrow)),
        ],
        axis=1,
    )
    got = lax.all_to_all(send, every, 0, 0, tiled=True)
    rows_all = got[:, :length].reshape(count * length, narrow)
    ids_all = got[:, length:].reshape(count, id_rows * narrow)[:, :length].reshape(-1).astype(jnp.int32)
    onehot = (ids_all[:, None] == jnp.arange(types, dtype=jnp.int32)[None, :]).astype(jnp.bfloat16)
    columns = lax.dot_general(onehot, rows_all, (((0,), (0,)), ((), ())), preferred_element_type=jnp.float32)
    columns = columns * scale
    per = types // count
    back = jnp.concatenate(
        [columns.reshape(count, per, narrow), gain_term.reshape(count, 1, narrow)], axis=1
    )
    back, tied = lax.optimization_barrier((back, tied))
    back = lax.all_to_all(back, every, 0, 0, tiled=True)
    table_grad = back[:, :per].transpose(1, 0, 2).reshape(per, width)
    gain_grad = back[:, per].sum(axis=0)
    return table_grad, gain_grad, tied


def scatter_by_permutes(block, axis):
    count = lax.axis_size(axis)
    me = lax.axis_index(axis)
    rows = block.shape[0] // count
    chunk = lambda index: lax.dynamic_slice_in_dim(block, index * rows, rows, axis=0)
    total = chunk(me)
    for apart in range(1, count):
        pairs = [(source, source ^ apart) for source in range(count)]
        total = total + lax.ppermute(chunk(me ^ apart), axis, pairs)
    return total


def gather_by_permutes(total, axis):
    count = lax.axis_size(axis)
    me = lax.axis_index(axis)
    pieces = [total]
    for apart in range(1, count):
        pairs = [(source, source ^ apart) for source in range(count)]
        pieces.append(lax.ppermute(total, axis, pairs))
    stacked = jnp.stack(pieces)
    return jnp.concatenate(
        [lax.dynamic_index_in_dim(stacked, index ^ me, keepdims=False) for index in range(count)], axis=0
    )


def gather_shards(block, axis):
    count = lax.axis_size(axis)
    me = lax.axis_index(axis)
    core = lax.axis_index("seq") % 2
    half_rows = block.shape[0] // 2
    mine = lax.dynamic_slice_in_dim(block, core * half_rows, half_rows, axis=0)
    blocks = [block]
    for apart in range(1, count):
        fetched = lax.ppermute(mine, axis, [(source, source ^ apart) for source in range(count)])
        swapped = from_partner(fetched, "seq", 0)
        lower = jnp.where(core == 0, fetched, swapped)
        upper = jnp.where(core == 0, swapped, fetched)
        blocks.append(jnp.concatenate([lower, upper], axis=0))
    stacked = jnp.stack(blocks)
    return jnp.concatenate(
        [lax.dynamic_index_in_dim(stacked, index ^ me, keepdims=False) for index in range(count)], axis=0
    )


def body(events, type_ids, type_table, norm_gain, kernel, upstream):
    length = events.shape[1]
    width = events.shape[2]
    chans = width // GROUPS
    half = KERNEL // 2
    fsdp = lax.axis_size("fsdp")
    seq_count = lax.axis_size("seq")
    total = length * seq_count * fsdp
    scale = 1.0 / jnp.sqrt(jnp.float32(total))
    if fsdp & (fsdp - 1):
        raise ValueError("fsdp not pow2")
    table = gather_shards(type_table, "fsdp")
    types = table.shape[0]
    onehot = (type_ids[0][:, None] == jnp.arange(types, dtype=jnp.int32)[None, :]).astype(jnp.bfloat16)
    mixed = events[0].astype(jnp.float32) + jnp.dot(onehot, table, preferred_element_type=jnp.float32)
    inv = lax.rsqrt(jnp.mean(mixed * mixed, axis=-1, keepdims=True) + 1e-06)
    normed = (mixed * inv * norm_gain).astype(jnp.bfloat16)
    normed_g = normed.reshape(length, GROUPS, chans).transpose(1, 0, 2)
    padded = with_halo(normed_g, "seq", 1, half)
    weights = gather_shards(kernel, "fsdp").reshape(GROUPS, chans, KERNEL * chans)
    up_float = upstream[0].astype(jnp.float32)
    up_g = up_float.reshape(length, GROUPS, chans).transpose(1, 0, 2)
    dconv = conv_dconv(padded.astype(jnp.float32), weights, up_g)
    dpad = with_halo(dconv, "seq", 1, half)
    dnormed = conv_transpose(dpad.astype(jnp.float32), weights, length)
    if seq_count <= GROUPS:
        group_in = lax.all_to_all(normed_g, "seq", 0, 1, tiled=True)
        group_out = lax.all_to_all(dconv, "seq", 0, 1, tiled=True)
    else:
        group_in, group_out = spread_groups(normed, dconv.transpose(1, 0, 2).reshape(length, width), chans)
    local_groups = group_in.shape[0]
    whole = group_in.shape[1]
    group_pad = jnp.pad(group_in, ((0, 0), (half, half), (0, 0)))
    kterms = [
        jnp.einsum("gto,gtc->goc", group_out, group_pad[:, k : k + whole], preferred_element_type=jnp.float32)
        for k in range(KERNEL)
    ]
    kernel_part = jnp.concatenate(kterms, axis=-1).reshape(-1, KERNEL * chans) * scale
    dnormed = dnormed.transpose(1, 0, 2).reshape(length, width)
    gain_term = jnp.sum(dnormed * mixed * inv, axis=0) * scale
    scaled = norm_gain * dnormed
    dmixed = inv * scaled - mixed * inv * inv * inv * jnp.mean(scaled * mixed, axis=-1, keepdims=True)
    input_grad = (up_float + dmixed).astype(jnp.bfloat16)
    kernel_sum = scatter_by_permutes(kernel_part, "fsdp")
    table_grad, gain_grad, kernel_sum = table_and_gain(input_grad, type_ids[0], gain_term, types, scale, kernel_sum)
    kernel_grad = gather_by_permutes(kernel_sum, "fsdp")
    return (input_grad[None], table_grad, gain_grad, kernel_grad)


def solution(mesh):
    return jax.shard_map(
        body,
        mesh=mesh,
        in_specs=(
            P("fsdp", "seq", None),
            P("fsdp", "seq"),
            P("fsdp", None),
            P(),
            P("fsdp", None),
            P("fsdp", "seq", None),
        ),
        out_specs=(
            P("fsdp", "seq", None),
            P(("fsdp", "seq"), None),
            P(("fsdp", "seq")),
            P("seq", None),
        ),
        check_vma=False,
    )
```

```python
import jax
import jax.numpy as jnp
from jax import lax
from jax.experimental import pallas as pl
from jax.experimental.pallas import tpu as pltpu
from jax.sharding import PartitionSpec as P

GROUPS = 16
KERNEL = 9


def with_halo(cells, axis, dim, width):
    count = lax.axis_size(axis)
    ends = count - 1
    head = lax.slice_in_dim(cells, 0, width, axis=dim)
    tail = lax.slice_in_dim(cells, cells.shape[dim] - width, cells.shape[dim], axis=dim)
    return jnp.concatenate(
        [
            lax.ppermute(tail, axis, [(i, (i + 1) % count) for i in range(ends)]),
            cells,
            lax.ppermute(head, axis, [((i + 1) % count, i) for i in range(ends)]),
        ],
        axis=dim,
    )


def from_partner(value, axis, apart):
    mask = 2**apart
    pairs = [(source, source ^ mask) for source in range(lax.axis_size(axis))]
    return lax.ppermute(value, axis, pairs)


def gather_rows(block, axis):
    count = lax.axis_size(axis)
    return lax.all_to_all(jnp.tile(block, (count,) + (1,) * (block.ndim - 1)), axis, 0, 0, tiled=True)


STEP_GROUPS = 4


def forward_kernel(pad_ref, w_ref, up_ref, out_ref):
    length = out_ref.shape[1]
    chans = pad_ref.shape[2]
    for g in range(out_ref.shape[0]):
        acc = None
        for k in range(KERNEL):
            x = pad_ref[g, k : k + length, :].astype(jnp.bfloat16)
            w = w_ref[g, :, k * chans : (k + 1) * chans]
            term = lax.dot_general(x, w, (((1,), (1,)), ((), ())), preferred_element_type=jnp.float32)
            acc = term if acc is None else acc + term
        sig = 1.0 / (1.0 + jnp.exp(-acc))
        out_ref[g] = (up_ref[g] * sig * (1.0 + acc * (1.0 - sig))).astype(out_ref.dtype)


def backward_kernel(pad_ref, w_ref, out_ref):
    length = out_ref.shape[1]
    chans = out_ref.shape[2]
    half = KERNEL // 2
    for g in range(out_ref.shape[0]):
        acc = None
        for k in range(KERNEL):
            x = pad_ref[g, 2 * half - k : 2 * half - k + length, :].astype(jnp.bfloat16)
            w = w_ref[g, :, k * chans : (k + 1) * chans]
            term = jnp.dot(x, w, preferred_element_type=jnp.float32)
            acc = term if acc is None else acc + term
        out_ref[g] = acc


def conv_dconv(padded, weights, up):
    groups, rows, chans = padded.shape
    length = up.shape[1]
    step = STEP_GROUPS if groups % STEP_GROUPS == 0 else 1
    flops = 2 * groups * length * chans * weights.shape[1] * KERNEL
    return pl.pallas_call(
        forward_kernel,
        grid=(groups // step,),
        in_specs=[
            pl.BlockSpec((step, rows, chans), lambda i: (i, 0, 0)),
            pl.BlockSpec((step, weights.shape[1], weights.shape[2]), lambda i: (i, 0, 0)),
            pl.BlockSpec((step, length, up.shape[2]), lambda i: (i, 0, 0)),
        ],
        out_specs=pl.BlockSpec((step, length, up.shape[2]), lambda i: (i, 0, 0)),
        out_shape=jax.ShapeDtypeStruct(up.shape, jnp.bfloat16),
        cost_estimate=pl.CostEstimate(
            flops=flops,
            transcendentals=up.size,
            bytes_accessed=padded.size * 4 + weights.size * 2 + up.size * 6,
        ),
    )(padded, weights, up)


def conv_transpose(dpad, weights, length):
    groups, rows, outs = dpad.shape
    chans = weights.shape[2] // KERNEL
    step = STEP_GROUPS if groups % STEP_GROUPS == 0 else 1
    return pl.pallas_call(
        backward_kernel,
        grid=(groups // step,),
        in_specs=[
            pl.BlockSpec((step, rows, outs), lambda i: (i, 0, 0)),
            pl.BlockSpec((step, weights.shape[1], weights.shape[2]), lambda i: (i, 0, 0)),
        ],
        out_specs=pl.BlockSpec((step, length, chans), lambda i: (i, 0, 0)),
        out_shape=jax.ShapeDtypeStruct((groups, length, chans), jnp.float32),
        cost_estimate=pl.CostEstimate(
            flops=2 * groups * length * chans * outs * KERNEL,
            transcendentals=0,
            bytes_accessed=dpad.size * 4 + weights.size * 2 + groups * length * chans * 4,
        ),
    )(dpad, weights)


def spread_groups(normed, dflat, chans):
    normed_slice = lax.all_to_all(normed, "seq", 1, 0, tiled=True)
    dconv_slice = lax.all_to_all(dflat, "seq", 1, 0, tiled=True)
    whole, slice_width = normed_slice.shape
    spread = chans // slice_width
    position = lax.axis_index("seq")
    group_rows = normed_slice
    for bit in range(spread.bit_length() - 1):
        partner = from_partner(group_rows, "seq", bit)
        lower = position >> bit & 1 == 0
        group_rows = jnp.where(
            lower,
            jnp.concatenate([group_rows, partner], axis=1),
            jnp.concatenate([partner, group_rows], axis=1),
        )
    return group_rows.reshape(1, whole, chans), dconv_slice.reshape(1, whole, slice_width)


def sum_rows(block, axis):
    count = lax.axis_size(axis)
    parts = block.reshape(count, block.shape[0] // count, *block.shape[1:])
    return lax.all_to_all(parts, axis, 0, 0, tiled=True).sum(axis=0)


def psum_rows(block, axis):
    return gather_rows(sum_rows(block, axis), axis)


def table_and_gain(input_grad, ids, gain_term, types, scale, tied):
    every = ("fsdp", "seq")
    count = lax.axis_size("fsdp") * lax.axis_size("seq")
    length, width = input_grad.shape
    narrow = width // count
    id_rows = -(-length // narrow)
    ids_wide = jnp.zeros((id_rows * narrow,), jnp.bfloat16).at[:length].set(ids.astype(jnp.bfloat16))
    send = jnp.concatenate(
        [
            input_grad.reshape(length, count, narrow).transpose(1, 0, 2),
            jnp.broadcast_to(ids_wide.reshape(1, id_rows, narrow), (count, id_rows, narrow)),
        ],
        axis=1,
    )
    got = lax.all_to_all(send, every, 0, 0, tiled=True)
    rows_all = got[:, :length].reshape(count * length, narrow)
    ids_all = got[:, length:].reshape(count, id_rows * narrow)[:, :length].reshape(-1).astype(jnp.int32)
    onehot = (ids_all[:, None] == jnp.arange(types, dtype=jnp.int32)[None, :]).astype(jnp.bfloat16)
    columns = lax.dot_general(onehot, rows_all, (((0,), (0,)), ((), ())), preferred_element_type=jnp.float32)
    columns = columns * scale
    per = types // count
    back = jnp.concatenate(
        [columns.reshape(count, per, narrow), gain_term.reshape(count, 1, narrow)], axis=1
    )
    back, tied = lax.optimization_barrier((back, tied))
    back = lax.all_to_all(back, every, 0, 0, tiled=True)
    table_grad = back[:, :per].transpose(1, 0, 2).reshape(per, width)
    gain_grad = back[:, per].sum(axis=0)
    return table_grad, gain_grad, tied


def scatter_by_permutes(block, axis):
    count = lax.axis_size(axis)
    me = lax.axis_index(axis)
    rows = block.shape[0] // count
    chunk = lambda index: lax.dynamic_slice_in_dim(block, index * rows, rows, axis=0)
    total = chunk(me)
    for apart in range(1, count):
        pairs = [(source, source ^ apart) for source in range(count)]
        total = total + lax.ppermute(chunk(me ^ apart), axis, pairs)
    return total


def gather_by_permutes(total, axis):
    count = lax.axis_size(axis)
    me = lax.axis_index(axis)
    pieces = [total]
    for apart in range(1, count):
        pairs = [(source, source ^ apart) for source in range(count)]
        pieces.append(lax.ppermute(total, axis, pairs))
    stacked = jnp.stack(pieces)
    return jnp.concatenate(
        [lax.dynamic_index_in_dim(stacked, index ^ me, keepdims=False) for index in range(count)], axis=0
    )


def fetch_halves(block, axis):
    count = lax.axis_size(axis)
    core = lax.axis_index("seq") % 2
    half_rows = block.shape[0] // 2
    mine = lax.dynamic_slice_in_dim(block, core * half_rows, half_rows, axis=0)
    return {
        apart: lax.ppermute(mine, axis, [(source, source ^ apart) for source in range(count)])
        for apart in range(count - 1, 0, -1)
    }


def swap_halves(fetched):
    return {apart: from_partner(piece, "seq", 0) for apart, piece in fetched.items()}


def assemble_shards(block, axis, fetched, swapped):
    count = lax.axis_size(axis)
    me = lax.axis_index(axis)
    core = lax.axis_index("seq") % 2
    blocks = [block]
    for apart in range(1, count):
        lower = jnp.where(core == 0, fetched[apart], swapped[apart])
        upper = jnp.where(core == 0, swapped[apart], fetched[apart])
        blocks.append(jnp.concatenate([lower, upper], axis=0))
    stacked = jnp.stack(blocks)
    return jnp.concatenate(
        [lax.dynamic_index_in_dim(stacked, index ^ me, keepdims=False) for index in range(count)], axis=0
    )


def gather_shards(block, axis):
    fetched = fetch_halves(block, axis)
    return assemble_shards(block, axis, fetched, swap_halves(fetched))


def body(events, type_ids, type_table, norm_gain, kernel, upstream):
    length = events.shape[1]
    width = events.shape[2]
    chans = width // GROUPS
    half = KERNEL // 2
    fsdp = lax.axis_size("fsdp")
    seq_count = lax.axis_size("seq")
    total = length * seq_count * fsdp
    scale = 1.0 / jnp.sqrt(jnp.float32(total))
    if fsdp & (fsdp - 1):
        raise ValueError("fsdp not pow2")
    table = gather_shards(type_table, "fsdp")
    kernel_fetched = fetch_halves(kernel, "fsdp")
    far = fsdp - 1
    types = table.shape[0]
    onehot = (type_ids[0][:, None] == jnp.arange(types, dtype=jnp.int32)[None, :]).astype(jnp.bfloat16)
    mixed = events[0].astype(jnp.float32) + jnp.dot(onehot, table, preferred_element_type=jnp.float32)
    near = {apart: piece for apart, piece in kernel_fetched.items() if apart != far}
    near_swapped = swap_halves(near)
    near, near_swapped, mixed = lax.optimization_barrier((near, near_swapped, mixed))
    inv = lax.rsqrt(jnp.mean(mixed * mixed, axis=-1, keepdims=True) + 1e-06)
    normed = (mixed * inv * norm_gain).astype(jnp.bfloat16)
    normed_g = normed.reshape(length, GROUPS, chans).transpose(1, 0, 2)
    padded = with_halo(normed_g, "seq", 1, half)
    far_piece, padded = lax.optimization_barrier((kernel_fetched[far], padded))
    kernel_fetched = {**near, far: far_piece}
    kernel_swapped = {**near_swapped, **swap_halves({far: far_piece})}
    weights = assemble_shards(kernel, "fsdp", kernel_fetched, kernel_swapped).reshape(GROUPS, chans, KERNEL * chans)
    up_float = upstream[0].astype(jnp.float32)
    up_g = up_float.reshape(length, GROUPS, chans).transpose(1, 0, 2)
    dconv = conv_dconv(padded.astype(jnp.float32), weights, up_g)
    dpad = with_halo(dconv, "seq", 1, half)
    dnormed = conv_transpose(dpad.astype(jnp.float32), weights, length)
    if seq_count <= GROUPS:
        group_in = lax.all_to_all(normed_g, "seq", 0, 1, tiled=True)
        group_out = lax.all_to_all(dconv, "seq", 0, 1, tiled=True)
    else:
        group_in, group_out = spread_groups(normed, dconv.transpose(1, 0, 2).reshape(length, width), chans)
    local_groups = group_in.shape[0]
    whole = group_in.shape[1]
    group_pad = jnp.pad(group_in, ((0, 0), (half, half), (0, 0)))
    kterms = [
        jnp.einsum("gto,gtc->goc", group_out, group_pad[:, k : k + whole], preferred_element_type=jnp.float32)
        for k in range(KERNEL)
    ]
    kernel_part = jnp.concatenate(kterms, axis=-1).reshape(-1, KERNEL * chans) * scale
    dnormed = dnormed.transpose(1, 0, 2).reshape(length, width)
    gain_term = jnp.sum(dnormed * mixed * inv, axis=0) * scale
    scaled = norm_gain * dnormed
    dmixed = inv * scaled - mixed * inv * inv * inv * jnp.mean(scaled * mixed, axis=-1, keepdims=True)
    input_grad = (up_float + dmixed).astype(jnp.bfloat16)
    kernel_sum = scatter_by_permutes(kernel_part, "fsdp")
    table_grad, gain_grad, kernel_sum = table_and_gain(input_grad, type_ids[0], gain_term, types, scale, kernel_sum)
    kernel_grad = gather_by_permutes(kernel_sum, "fsdp")
    return (input_grad[None], table_grad, gain_grad, kernel_grad)


def solution(mesh):
    return jax.shard_map(
        body,
        mesh=mesh,
        in_specs=(
            P("fsdp", "seq", None),
            P("fsdp", "seq"),
            P("fsdp", None),
            P(),
            P("fsdp", None),
            P("fsdp", "seq", None),
        ),
        out_specs=(
            P("fsdp", "seq", None),
            P(("fsdp", "seq"), None),
            P(("fsdp", "seq")),
            P("seq", None),
        ),
        check_vma=False,
    )
```

```python
import jax
import jax.numpy as jnp
from jax import lax
from jax.experimental import pallas as pl
from jax.experimental.pallas import tpu as pltpu
from jax.sharding import PartitionSpec as P

GROUPS = 16
KERNEL = 9


def with_halo(cells, axis, dim, width):
    count = lax.axis_size(axis)
    ends = count - 1
    head = lax.slice_in_dim(cells, 0, width, axis=dim)
    tail = lax.slice_in_dim(cells, cells.shape[dim] - width, cells.shape[dim], axis=dim)
    return jnp.concatenate(
        [
            lax.ppermute(tail, axis, [(i, (i + 1) % count) for i in range(ends)]),
            cells,
            lax.ppermute(head, axis, [((i + 1) % count, i) for i in range(ends)]),
        ],
        axis=dim,
    )


def from_partner(value, axis, apart):
    mask = 2**apart
    pairs = [(source, source ^ mask) for source in range(lax.axis_size(axis))]
    return lax.ppermute(value, axis, pairs)


def gather_rows(block, axis):
    count = lax.axis_size(axis)
    return lax.all_to_all(jnp.tile(block, (count,) + (1,) * (block.ndim - 1)), axis, 0, 0, tiled=True)


STEP_GROUPS = 4


def forward_kernel(pad_ref, w_ref, up_ref, out_ref):
    length = out_ref.shape[1]
    chans = pad_ref.shape[2]
    for g in range(out_ref.shape[0]):
        acc = None
        for k in range(KERNEL):
            x = pad_ref[g, k : k + length, :].astype(jnp.bfloat16)
            w = w_ref[g, :, k * chans : (k + 1) * chans]
            term = lax.dot_general(x, w, (((1,), (1,)), ((), ())), preferred_element_type=jnp.float32)
            acc = term if acc is None else acc + term
        sig = 1.0 / (1.0 + jnp.exp(-acc))
        out_ref[g] = (up_ref[g] * sig * (1.0 + acc * (1.0 - sig))).astype(out_ref.dtype)


def backward_kernel(pad_ref, w_ref, out_ref):
    length = out_ref.shape[1]
    chans = out_ref.shape[2]
    half = KERNEL // 2
    for g in range(out_ref.shape[0]):
        acc = None
        for k in range(KERNEL):
            x = pad_ref[g, 2 * half - k : 2 * half - k + length, :].astype(jnp.bfloat16)
            w = w_ref[g, :, k * chans : (k + 1) * chans]
            term = jnp.dot(x, w, preferred_element_type=jnp.float32)
            acc = term if acc is None else acc + term
        out_ref[g] = acc


def conv_dconv(padded, weights, up):
    groups, rows, chans = padded.shape
    length = up.shape[1]
    step = STEP_GROUPS if groups % STEP_GROUPS == 0 else 1
    flops = 2 * groups * length * chans * weights.shape[1] * KERNEL
    return pl.pallas_call(
        forward_kernel,
        grid=(groups // step,),
        in_specs=[
            pl.BlockSpec((step, rows, chans), lambda i: (i, 0, 0)),
            pl.BlockSpec((step, weights.shape[1], weights.shape[2]), lambda i: (i, 0, 0)),
            pl.BlockSpec((step, length, up.shape[2]), lambda i: (i, 0, 0)),
        ],
        out_specs=pl.BlockSpec((step, length, up.shape[2]), lambda i: (i, 0, 0)),
        out_shape=jax.ShapeDtypeStruct(up.shape, jnp.bfloat16),
        cost_estimate=pl.CostEstimate(
            flops=flops,
            transcendentals=up.size,
            bytes_accessed=padded.size * 4 + weights.size * 2 + up.size * 6,
        ),
    )(padded, weights, up)


def conv_transpose(dpad, weights, length):
    groups, rows, outs = dpad.shape
    chans = weights.shape[2] // KERNEL
    step = STEP_GROUPS if groups % STEP_GROUPS == 0 else 1
    return pl.pallas_call(
        backward_kernel,
        grid=(groups // step,),
        in_specs=[
            pl.BlockSpec((step, rows, outs), lambda i: (i, 0, 0)),
            pl.BlockSpec((step, weights.shape[1], weights.shape[2]), lambda i: (i, 0, 0)),
        ],
        out_specs=pl.BlockSpec((step, length, chans), lambda i: (i, 0, 0)),
        out_shape=jax.ShapeDtypeStruct((groups, length, chans), jnp.float32),
        cost_estimate=pl.CostEstimate(
            flops=2 * groups * length * chans * outs * KERNEL,
            transcendentals=0,
            bytes_accessed=dpad.size * 4 + weights.size * 2 + groups * length * chans * 4,
        ),
    )(dpad, weights)


def spread_groups(normed, dflat, chans):
    normed_slice = lax.all_to_all(normed, "seq", 1, 0, tiled=True)
    dconv_slice = lax.all_to_all(dflat, "seq", 1, 0, tiled=True)
    whole, slice_width = normed_slice.shape
    spread = chans // slice_width
    position = lax.axis_index("seq")
    group_rows = normed_slice
    for bit in range(spread.bit_length() - 1):
        partner = from_partner(group_rows, "seq", bit)
        lower = position >> bit & 1 == 0
        group_rows = jnp.where(
            lower,
            jnp.concatenate([group_rows, partner], axis=1),
            jnp.concatenate([partner, group_rows], axis=1),
        )
    return group_rows.reshape(1, whole, chans), dconv_slice.reshape(1, whole, slice_width)


def sum_rows(block, axis):
    count = lax.axis_size(axis)
    parts = block.reshape(count, block.shape[0] // count, *block.shape[1:])
    return lax.all_to_all(parts, axis, 0, 0, tiled=True).sum(axis=0)


def psum_rows(block, axis):
    return gather_rows(sum_rows(block, axis), axis)


def table_and_gain(input_grad, ids, gain_term, types, scale, tied):
    every = ("fsdp", "seq")
    count = lax.axis_size("fsdp") * lax.axis_size("seq")
    length, width = input_grad.shape
    narrow = width // count
    id_rows = -(-length // narrow)
    ids_wide = jnp.zeros((id_rows * narrow,), jnp.bfloat16).at[:length].set(ids.astype(jnp.bfloat16))
    send = jnp.concatenate(
        [
            input_grad.reshape(length, count, narrow).transpose(1, 0, 2),
            jnp.broadcast_to(ids_wide.reshape(1, id_rows, narrow), (count, id_rows, narrow)),
        ],
        axis=1,
    )
    got = lax.all_to_all(send, every, 0, 0, tiled=True)
    rows_all = got[:, :length].reshape(count * length, narrow)
    ids_all = got[:, length:].reshape(count, id_rows * narrow)[:, :length].reshape(-1).astype(jnp.int32)
    onehot = (ids_all[:, None] == jnp.arange(types, dtype=jnp.int32)[None, :]).astype(jnp.bfloat16)
    columns = lax.dot_general(onehot, rows_all, (((0,), (0,)), ((), ())), preferred_element_type=jnp.float32)
    columns = columns * scale
    per = types // count
    back = jnp.concatenate(
        [columns.reshape(count, per, narrow), gain_term.reshape(count, 1, narrow)], axis=1
    )
    back, tied = lax.optimization_barrier((back, tied))
    back = lax.all_to_all(back, every, 0, 0, tiled=True)
    table_grad = back[:, :per].transpose(1, 0, 2).reshape(per, width)
    gain_grad = back[:, per].sum(axis=0)
    return table_grad, gain_grad, tied


def scatter_by_permutes(block, axis):
    count = lax.axis_size(axis)
    me = lax.axis_index(axis)
    rows = block.shape[0] // count
    chunk = lambda index: lax.dynamic_slice_in_dim(block, index * rows, rows, axis=0)
    total = chunk(me)
    for apart in range(1, count):
        pairs = [(source, source ^ apart) for source in range(count)]
        total = total + lax.ppermute(chunk(me ^ apart), axis, pairs)
    return total


def gather_by_permutes(total, axis):
    count = lax.axis_size(axis)
    me = lax.axis_index(axis)
    pieces = [total]
    for apart in range(1, count):
        pairs = [(source, source ^ apart) for source in range(count)]
        pieces.append(lax.ppermute(total, axis, pairs))
    stacked = jnp.stack(pieces)
    return jnp.concatenate(
        [lax.dynamic_index_in_dim(stacked, index ^ me, keepdims=False) for index in range(count)], axis=0
    )


def fetch_halves(block, axis):
    count = lax.axis_size(axis)
    core = lax.axis_index("seq") % 2
    half_rows = block.shape[0] // 2
    mine = lax.dynamic_slice_in_dim(block, core * half_rows, half_rows, axis=0)
    return {
        apart: lax.ppermute(mine, axis, [(source, source ^ apart) for source in range(count)])
        for apart in range(count - 1, 0, -1)
    }


def swap_halves(fetched):
    return {apart: from_partner(piece, "seq", 0) for apart, piece in fetched.items()}


def assemble_shards(block, axis, fetched, swapped):
    count = lax.axis_size(axis)
    me = lax.axis_index(axis)
    core = lax.axis_index("seq") % 2
    blocks = [block]
    for apart in range(1, count):
        lower = jnp.where(core == 0, fetched[apart], swapped[apart])
        upper = jnp.where(core == 0, swapped[apart], fetched[apart])
        blocks.append(jnp.concatenate([lower, upper], axis=0))
    stacked = jnp.stack(blocks)
    return jnp.concatenate(
        [lax.dynamic_index_in_dim(stacked, index ^ me, keepdims=False) for index in range(count)], axis=0
    )


def gather_shards(block, axis):
    fetched = fetch_halves(block, axis)
    return assemble_shards(block, axis, fetched, swap_halves(fetched))


def body(events, type_ids, type_table, norm_gain, kernel, upstream):
    length = events.shape[1]
    width = events.shape[2]
    chans = width // GROUPS
    half = KERNEL // 2
    fsdp = lax.axis_size("fsdp")
    seq_count = lax.axis_size("seq")
    total = length * seq_count * fsdp
    scale = 1.0 / jnp.sqrt(jnp.float32(total))
    if fsdp & (fsdp - 1):
        raise ValueError("fsdp not pow2")
    table = gather_shards(type_table, "fsdp")
    kernel_fetched = fetch_halves(kernel, "fsdp")
    far = fsdp - 1
    types = table.shape[0]
    onehot = (type_ids[0][:, None] == jnp.arange(types, dtype=jnp.int32)[None, :]).astype(jnp.bfloat16)
    mixed = events[0].astype(jnp.float32) + jnp.dot(onehot, table, preferred_element_type=jnp.float32)
    near = {apart: piece for apart, piece in kernel_fetched.items() if apart != far}
    near_swapped = swap_halves(near)
    inv = lax.rsqrt(jnp.mean(mixed * mixed, axis=-1, keepdims=True) + 1e-06)
    normed = (mixed * inv * norm_gain).astype(jnp.bfloat16)
    normed_g = normed.reshape(length, GROUPS, chans).transpose(1, 0, 2)
    padded = with_halo(normed_g, "seq", 1, half)
    far_piece, padded = lax.optimization_barrier((kernel_fetched[far], padded))
    kernel_fetched = {**near, far: far_piece}
    kernel_swapped = {**near_swapped, **swap_halves({far: far_piece})}
    weights = assemble_shards(kernel, "fsdp", kernel_fetched, kernel_swapped).reshape(GROUPS, chans, KERNEL * chans)
    up_float = upstream[0].astype(jnp.float32)
    up_g = up_float.reshape(length, GROUPS, chans).transpose(1, 0, 2)
    dconv = conv_dconv(padded.astype(jnp.float32), weights, up_g)
    dpad = with_halo(dconv, "seq", 1, half)
    dnormed = conv_transpose(dpad.astype(jnp.float32), weights, length)
    if seq_count <= GROUPS:
        group_in = lax.all_to_all(normed_g, "seq", 0, 1, tiled=True)
        group_out = lax.all_to_all(dconv, "seq", 0, 1, tiled=True)
    else:
        group_in, group_out = spread_groups(normed, dconv.transpose(1, 0, 2).reshape(length, width), chans)
    local_groups = group_in.shape[0]
    whole = group_in.shape[1]
    group_pad = jnp.pad(group_in, ((0, 0), (half, half), (0, 0)))
    kterms = [
        jnp.einsum("gto,gtc->goc", group_out, group_pad[:, k : k + whole], preferred_element_type=jnp.float32)
        for k in range(KERNEL)
    ]
    kernel_part = jnp.concatenate(kterms, axis=-1).reshape(-1, KERNEL * chans) * scale
    dnormed = dnormed.transpose(1, 0, 2).reshape(length, width)
    gain_term = jnp.sum(dnormed * mixed * inv, axis=0) * scale
    scaled = norm_gain * dnormed
    dmixed = inv * scaled - mixed * inv * inv * inv * jnp.mean(scaled * mixed, axis=-1, keepdims=True)
    input_grad = (up_float + dmixed).astype(jnp.bfloat16)
    kernel_sum = scatter_by_permutes(kernel_part, "fsdp")
    table_grad, gain_grad, kernel_sum = table_and_gain(input_grad, type_ids[0], gain_term, types, scale, kernel_sum)
    kernel_grad = gather_by_permutes(kernel_sum, "fsdp")
    return (input_grad[None], table_grad, gain_grad, kernel_grad)


def solution(mesh):
    return jax.shard_map(
        body,
        mesh=mesh,
        in_specs=(
            P("fsdp", "seq", None),
            P("fsdp", "seq"),
            P("fsdp", None),
            P(),
            P("fsdp", None),
            P("fsdp", "seq", None),
        ),
        out_specs=(
            P("fsdp", "seq", None),
            P(("fsdp", "seq"), None),
            P(("fsdp", "seq")),
            P("seq", None),
        ),
        check_vma=False,
    )
```

```python
import jax
import jax.numpy as jnp
from jax import lax
from jax.experimental import pallas as pl
from jax.experimental.pallas import tpu as pltpu
from jax.sharding import PartitionSpec as P

GROUPS = 16
KERNEL = 9


def with_halo(cells, axis, dim, width):
    count = lax.axis_size(axis)
    ends = count - 1
    head = lax.slice_in_dim(cells, 0, width, axis=dim)
    tail = lax.slice_in_dim(cells, cells.shape[dim] - width, cells.shape[dim], axis=dim)
    return jnp.concatenate(
        [
            lax.ppermute(tail, axis, [(i, (i + 1) % count) for i in range(ends)]),
            cells,
            lax.ppermute(head, axis, [((i + 1) % count, i) for i in range(ends)]),
        ],
        axis=dim,
    )


def from_partner(value, axis, apart):
    mask = 2**apart
    pairs = [(source, source ^ mask) for source in range(lax.axis_size(axis))]
    return lax.ppermute(value, axis, pairs)


def gather_rows(block, axis):
    count = lax.axis_size(axis)
    return lax.all_to_all(jnp.tile(block, (count,) + (1,) * (block.ndim - 1)), axis, 0, 0, tiled=True)


STEP_GROUPS = 4


def forward_kernel(pad_ref, w_ref, up_ref, out_ref):
    length = out_ref.shape[1]
    for g in range(out_ref.shape[0]):
        x = jnp.concatenate(
            [pad_ref[g, k : k + length, :].astype(jnp.bfloat16) for k in range(KERNEL)], axis=1
        )
        acc = lax.dot_general(x, w_ref[g], (((1,), (1,)), ((), ())), preferred_element_type=jnp.float32)
        sig = 1.0 / (1.0 + jnp.exp(-acc))
        out_ref[g] = (up_ref[g] * sig * (1.0 + acc * (1.0 - sig))).astype(out_ref.dtype)


def backward_kernel(pad_ref, w_ref, out_ref):
    length = out_ref.shape[1]
    chans = out_ref.shape[2]
    half = KERNEL // 2
    for g in range(out_ref.shape[0]):
        x = jnp.concatenate(
            [pad_ref[g, 2 * half - k : 2 * half - k + length, :].astype(jnp.bfloat16) for k in range(KERNEL)], axis=1
        )
        w = jnp.concatenate([w_ref[g, :, k * chans : (k + 1) * chans] for k in range(KERNEL)], axis=0)
        out_ref[g] = jnp.dot(x, w, preferred_element_type=jnp.float32)


def conv_dconv(padded, weights, up):
    groups, rows, chans = padded.shape
    length = up.shape[1]
    step = STEP_GROUPS if groups % STEP_GROUPS == 0 else 1
    flops = 2 * groups * length * chans * weights.shape[1] * KERNEL
    return pl.pallas_call(
        forward_kernel,
        grid=(groups // step,),
        in_specs=[
            pl.BlockSpec((step, rows, chans), lambda i: (i, 0, 0)),
            pl.BlockSpec((step, weights.shape[1], weights.shape[2]), lambda i: (i, 0, 0)),
            pl.BlockSpec((step, length, up.shape[2]), lambda i: (i, 0, 0)),
        ],
        out_specs=pl.BlockSpec((step, length, up.shape[2]), lambda i: (i, 0, 0)),
        out_shape=jax.ShapeDtypeStruct(up.shape, jnp.bfloat16),
        cost_estimate=pl.CostEstimate(
            flops=flops,
            transcendentals=up.size,
            bytes_accessed=padded.size * 4 + weights.size * 2 + up.size * 6,
        ),
    )(padded, weights, up)


def conv_transpose(dpad, weights, length):
    groups, rows, outs = dpad.shape
    chans = weights.shape[2] // KERNEL
    step = STEP_GROUPS if groups % STEP_GROUPS == 0 else 1
    return pl.pallas_call(
        backward_kernel,
        grid=(groups // step,),
        in_specs=[
            pl.BlockSpec((step, rows, outs), lambda i: (i, 0, 0)),
            pl.BlockSpec((step, weights.shape[1], weights.shape[2]), lambda i: (i, 0, 0)),
        ],
        out_specs=pl.BlockSpec((step, length, chans), lambda i: (i, 0, 0)),
        out_shape=jax.ShapeDtypeStruct((groups, length, chans), jnp.float32),
        cost_estimate=pl.CostEstimate(
            flops=2 * groups * length * chans * outs * KERNEL,
            transcendentals=0,
            bytes_accessed=dpad.size * 4 + weights.size * 2 + groups * length * chans * 4,
        ),
    )(dpad, weights)


def spread_groups(normed, dflat, chans):
    normed_slice = lax.all_to_all(normed, "seq", 1, 0, tiled=True)
    dconv_slice = lax.all_to_all(dflat, "seq", 1, 0, tiled=True)
    whole, slice_width = normed_slice.shape
    spread = chans // slice_width
    position = lax.axis_index("seq")
    group_rows = normed_slice
    for bit in range(spread.bit_length() - 1):
        partner = from_partner(group_rows, "seq", bit)
        lower = position >> bit & 1 == 0
        group_rows = jnp.where(
            lower,
            jnp.concatenate([group_rows, partner], axis=1),
            jnp.concatenate([partner, group_rows], axis=1),
        )
    return group_rows.reshape(1, whole, chans), dconv_slice.reshape(1, whole, slice_width)


def sum_rows(block, axis):
    count = lax.axis_size(axis)
    parts = block.reshape(count, block.shape[0] // count, *block.shape[1:])
    return lax.all_to_all(parts, axis, 0, 0, tiled=True).sum(axis=0)


def psum_rows(block, axis):
    return gather_rows(sum_rows(block, axis), axis)


def table_and_gain(input_grad, ids, gain_term, types, scale, tied):
    every = ("fsdp", "seq")
    count = lax.axis_size("fsdp") * lax.axis_size("seq")
    length, width = input_grad.shape
    narrow = width // count
    id_rows = -(-length // narrow)
    ids_wide = jnp.zeros((id_rows * narrow,), jnp.bfloat16).at[:length].set(ids.astype(jnp.bfloat16))
    send = jnp.concatenate(
        [
            input_grad.reshape(length, count, narrow).transpose(1, 0, 2),
            jnp.broadcast_to(ids_wide.reshape(1, id_rows, narrow), (count, id_rows, narrow)),
        ],
        axis=1,
    )
    got = lax.all_to_all(send, every, 0, 0, tiled=True)
    rows_all = got[:, :length].reshape(count * length, narrow)
    ids_all = got[:, length:].reshape(count, id_rows * narrow)[:, :length].reshape(-1).astype(jnp.int32)
    onehot = (ids_all[:, None] == jnp.arange(types, dtype=jnp.int32)[None, :]).astype(jnp.bfloat16)
    columns = lax.dot_general(onehot, rows_all, (((0,), (0,)), ((), ())), preferred_element_type=jnp.float32)
    columns = columns * scale
    per = types // count
    back = jnp.concatenate(
        [columns.reshape(count, per, narrow), gain_term.reshape(count, 1, narrow)], axis=1
    )
    back, tied = lax.optimization_barrier((back, tied))
    back = lax.all_to_all(back, every, 0, 0, tiled=True)
    table_grad = back[:, :per].transpose(1, 0, 2).reshape(per, width)
    gain_grad = back[:, per].sum(axis=0)
    return table_grad, gain_grad, tied


def scatter_by_permutes(block, axis):
    count = lax.axis_size(axis)
    me = lax.axis_index(axis)
    rows = block.shape[0] // count
    chunk = lambda index: lax.dynamic_slice_in_dim(block, index * rows, rows, axis=0)
    total = chunk(me)
    for apart in range(1, count):
        pairs = [(source, source ^ apart) for source in range(count)]
        total = total + lax.ppermute(chunk(me ^ apart), axis, pairs)
    return total


def gather_by_permutes(total, axis):
    count = lax.axis_size(axis)
    me = lax.axis_index(axis)
    pieces = [total]
    for apart in range(1, count):
        pairs = [(source, source ^ apart) for source in range(count)]
        pieces.append(lax.ppermute(total, axis, pairs))
    stacked = jnp.stack(pieces)
    return jnp.concatenate(
        [lax.dynamic_index_in_dim(stacked, index ^ me, keepdims=False) for index in range(count)], axis=0
    )


def fetch_halves(block, axis):
    count = lax.axis_size(axis)
    core = lax.axis_index("seq") % 2
    half_rows = block.shape[0] // 2
    mine = lax.dynamic_slice_in_dim(block, core * half_rows, half_rows, axis=0)
    return {
        apart: lax.ppermute(mine, axis, [(source, source ^ apart) for source in range(count)])
        for apart in range(count - 1, 0, -1)
    }


def swap_halves(fetched):
    return {apart: from_partner(piece, "seq", 0) for apart, piece in fetched.items()}


def assemble_shards(block, axis, fetched, swapped):
    count = lax.axis_size(axis)
    me = lax.axis_index(axis)
    core = lax.axis_index("seq") % 2
    blocks = [block]
    for apart in range(1, count):
        lower = jnp.where(core == 0, fetched[apart], swapped[apart])
        upper = jnp.where(core == 0, swapped[apart], fetched[apart])
        blocks.append(jnp.concatenate([lower, upper], axis=0))
    stacked = jnp.stack(blocks)
    return jnp.concatenate(
        [lax.dynamic_index_in_dim(stacked, index ^ me, keepdims=False) for index in range(count)], axis=0
    )


def gather_shards(block, axis):
    fetched = fetch_halves(block, axis)
    return assemble_shards(block, axis, fetched, swap_halves(fetched))


def body(events, type_ids, type_table, norm_gain, kernel, upstream):
    length = events.shape[1]
    width = events.shape[2]
    chans = width // GROUPS
    half = KERNEL // 2
    fsdp = lax.axis_size("fsdp")
    seq_count = lax.axis_size("seq")
    total = length * seq_count * fsdp
    scale = 1.0 / jnp.sqrt(jnp.float32(total))
    if fsdp & (fsdp - 1):
        raise ValueError("fsdp not pow2")
    table = gather_shards(type_table, "fsdp")
    kernel_fetched = fetch_halves(kernel, "fsdp")
    far = fsdp - 1
    types = table.shape[0]
    onehot = (type_ids[0][:, None] == jnp.arange(types, dtype=jnp.int32)[None, :]).astype(jnp.bfloat16)
    mixed = events[0].astype(jnp.float32) + jnp.dot(onehot, table, preferred_element_type=jnp.float32)
    near = {apart: piece for apart, piece in kernel_fetched.items() if apart != far}
    near_swapped = swap_halves(near)
    inv = lax.rsqrt(jnp.mean(mixed * mixed, axis=-1, keepdims=True) + 1e-06)
    normed = (mixed * inv * norm_gain).astype(jnp.bfloat16)
    normed_g = normed.reshape(length, GROUPS, chans).transpose(1, 0, 2)
    padded = with_halo(normed_g, "seq", 1, half)
    far_piece, padded = lax.optimization_barrier((kernel_fetched[far], padded))
    kernel_fetched = {**near, far: far_piece}
    kernel_swapped = {**near_swapped, **swap_halves({far: far_piece})}
    weights = assemble_shards(kernel, "fsdp", kernel_fetched, kernel_swapped).reshape(GROUPS, chans, KERNEL * chans)
    up_float = upstream[0].astype(jnp.float32)
    up_g = up_float.reshape(length, GROUPS, chans).transpose(1, 0, 2)
    dconv = conv_dconv(padded.astype(jnp.float32), weights, up_g)
    dpad = with_halo(dconv, "seq", 1, half)
    dnormed = conv_transpose(dpad.astype(jnp.float32), weights, length)
    if seq_count <= GROUPS:
        group_in = lax.all_to_all(normed_g, "seq", 0, 1, tiled=True)
        group_out = lax.all_to_all(dconv, "seq", 0, 1, tiled=True)
    else:
        group_in, group_out = spread_groups(normed, dconv.transpose(1, 0, 2).reshape(length, width), chans)
    local_groups = group_in.shape[0]
    whole = group_in.shape[1]
    group_pad = jnp.pad(group_in, ((0, 0), (half, half), (0, 0)))
    kterms = [
        jnp.einsum("gto,gtc->goc", group_out, group_pad[:, k : k + whole], preferred_element_type=jnp.float32)
        for k in range(KERNEL)
    ]
    kernel_part = jnp.concatenate(kterms, axis=-1).reshape(-1, KERNEL * chans) * scale
    dnormed = dnormed.transpose(1, 0, 2).reshape(length, width)
    gain_term = jnp.sum(dnormed * mixed * inv, axis=0) * scale
    scaled = norm_gain * dnormed
    dmixed = inv * scaled - mixed * inv * inv * inv * jnp.mean(scaled * mixed, axis=-1, keepdims=True)
    input_grad = (up_float + dmixed).astype(jnp.bfloat16)
    kernel_sum = scatter_by_permutes(kernel_part, "fsdp")
    table_grad, gain_grad, kernel_sum = table_and_gain(input_grad, type_ids[0], gain_term, types, scale, kernel_sum)
    kernel_grad = gather_by_permutes(kernel_sum, "fsdp")
    return (input_grad[None], table_grad, gain_grad, kernel_grad)


def solution(mesh):
    return jax.shard_map(
        body,
        mesh=mesh,
        in_specs=(
            P("fsdp", "seq", None),
            P("fsdp", "seq"),
            P("fsdp", None),
            P(),
            P("fsdp", None),
            P("fsdp", "seq", None),
        ),
        out_specs=(
            P("fsdp", "seq", None),
            P(("fsdp", "seq"), None),
            P(("fsdp", "seq")),
            P("seq", None),
        ),
        check_vma=False,
    )
```

```python
import jax
import jax.numpy as jnp
from jax import lax
from jax.experimental import pallas as pl
from jax.experimental.pallas import tpu as pltpu
from jax.sharding import PartitionSpec as P

GROUPS = 16
KERNEL = 9


def with_halo(cells, axis, dim, width):
    count = lax.axis_size(axis)
    ends = count - 1
    head = lax.slice_in_dim(cells, 0, width, axis=dim)
    tail = lax.slice_in_dim(cells, cells.shape[dim] - width, cells.shape[dim], axis=dim)
    return jnp.concatenate(
        [
            lax.ppermute(tail, axis, [(i, (i + 1) % count) for i in range(ends)]),
            cells,
            lax.ppermute(head, axis, [((i + 1) % count, i) for i in range(ends)]),
        ],
        axis=dim,
    )


def from_partner(value, axis, apart):
    mask = 2**apart
    pairs = [(source, source ^ mask) for source in range(lax.axis_size(axis))]
    return lax.ppermute(value, axis, pairs)


def gather_rows(block, axis):
    count = lax.axis_size(axis)
    return lax.all_to_all(jnp.tile(block, (count,) + (1,) * (block.ndim - 1)), axis, 0, 0, tiled=True)


STEP_GROUPS = 4


def forward_kernel(pad_ref, w_ref, up_ref, out_ref):
    length = out_ref.shape[1]
    for g in range(out_ref.shape[0]):
        x = jnp.concatenate(
            [pad_ref[g, k : k + length, :].astype(jnp.bfloat16) for k in range(KERNEL)], axis=1
        )
        acc = lax.dot_general(x, w_ref[g], (((1,), (1,)), ((), ())), preferred_element_type=jnp.float32)
        sig = 1.0 / (1.0 + jnp.exp(-acc))
        out_ref[g] = (up_ref[g] * sig * (1.0 + acc * (1.0 - sig))).astype(out_ref.dtype)


def backward_kernel(pad_ref, w_ref, out_ref):
    length = out_ref.shape[1]
    chans = out_ref.shape[2]
    half = KERNEL // 2
    for g in range(out_ref.shape[0]):
        x = jnp.concatenate(
            [pad_ref[g, 2 * half - k : 2 * half - k + length, :].astype(jnp.bfloat16) for k in range(KERNEL)], axis=1
        )
        w = jnp.concatenate([w_ref[g, :, k * chans : (k + 1) * chans] for k in range(KERNEL)], axis=0)
        out_ref[g] = jnp.dot(x, w, preferred_element_type=jnp.float32)


def conv_dconv(padded, weights, up):
    groups, rows, chans = padded.shape
    length = up.shape[1]
    step = STEP_GROUPS if groups % STEP_GROUPS == 0 else 1
    flops = 2 * groups * length * chans * weights.shape[1] * KERNEL
    return pl.pallas_call(
        forward_kernel,
        grid=(groups // step,),
        in_specs=[
            pl.BlockSpec((step, rows, chans), lambda i: (i, 0, 0)),
            pl.BlockSpec((step, weights.shape[1], weights.shape[2]), lambda i: (i, 0, 0)),
            pl.BlockSpec((step, length, up.shape[2]), lambda i: (i, 0, 0)),
        ],
        out_specs=pl.BlockSpec((step, length, up.shape[2]), lambda i: (i, 0, 0)),
        out_shape=jax.ShapeDtypeStruct(up.shape, jnp.bfloat16),
        cost_estimate=pl.CostEstimate(
            flops=flops,
            transcendentals=up.size,
            bytes_accessed=padded.size * 4 + weights.size * 2 + up.size * 6,
        ),
    )(padded, weights, up)


def conv_transpose(dpad, weights, length):
    groups, rows, outs = dpad.shape
    chans = weights.shape[2] // KERNEL
    step = STEP_GROUPS if groups % STEP_GROUPS == 0 else 1
    return pl.pallas_call(
        backward_kernel,
        grid=(groups // step,),
        in_specs=[
            pl.BlockSpec((step, rows, outs), lambda i: (i, 0, 0)),
            pl.BlockSpec((step, weights.shape[1], weights.shape[2]), lambda i: (i, 0, 0)),
        ],
        out_specs=pl.BlockSpec((step, length, chans), lambda i: (i, 0, 0)),
        out_shape=jax.ShapeDtypeStruct((groups, length, chans), jnp.float32),
        cost_estimate=pl.CostEstimate(
            flops=2 * groups * length * chans * outs * KERNEL,
            transcendentals=0,
            bytes_accessed=dpad.size * 4 + weights.size * 2 + groups * length * chans * 4,
        ),
    )(dpad, weights)


def spread_groups(normed, dflat, chans):
    normed_slice = lax.all_to_all(normed, "seq", 1, 0, tiled=True)
    dconv_slice = lax.all_to_all(dflat, "seq", 1, 0, tiled=True)
    whole, slice_width = normed_slice.shape
    spread = chans // slice_width
    position = lax.axis_index("seq")
    group_rows = normed_slice
    for bit in range(spread.bit_length() - 1):
        partner = from_partner(group_rows, "seq", bit)
        lower = position >> bit & 1 == 0
        group_rows = jnp.where(
            lower,
            jnp.concatenate([group_rows, partner], axis=1),
            jnp.concatenate([partner, group_rows], axis=1),
        )
    return group_rows.reshape(1, whole, chans), dconv_slice.reshape(1, whole, slice_width)


def sum_rows(block, axis):
    count = lax.axis_size(axis)
    parts = block.reshape(count, block.shape[0] // count, *block.shape[1:])
    return lax.all_to_all(parts, axis, 0, 0, tiled=True).sum(axis=0)


def psum_rows(block, axis):
    return gather_rows(sum_rows(block, axis), axis)


def table_and_gain(input_grad, ids, gain_term, types, scale, tied):
    every = ("fsdp", "seq")
    count = lax.axis_size("fsdp") * lax.axis_size("seq")
    length, width = input_grad.shape
    narrow = width // count
    id_rows = -(-length // narrow)
    ids_wide = jnp.zeros((id_rows * narrow,), jnp.bfloat16).at[:length].set(ids.astype(jnp.bfloat16))
    send = jnp.concatenate(
        [
            input_grad.reshape(length, count, narrow).transpose(1, 0, 2),
            jnp.broadcast_to(ids_wide.reshape(1, id_rows, narrow), (count, id_rows, narrow)),
        ],
        axis=1,
    )
    got = lax.all_to_all(send, every, 0, 0, tiled=True)
    rows_all = got[:, :length].reshape(count * length, narrow)
    ids_all = got[:, length:].reshape(count, id_rows * narrow)[:, :length].reshape(-1).astype(jnp.int32)
    onehot = (ids_all[:, None] == jnp.arange(types, dtype=jnp.int32)[None, :]).astype(jnp.bfloat16)
    columns = lax.dot_general(onehot, rows_all, (((0,), (0,)), ((), ())), preferred_element_type=jnp.float32)
    columns = columns * scale
    per = types // count
    back = jnp.concatenate(
        [columns.reshape(count, per, narrow), gain_term.reshape(count, 1, narrow)], axis=1
    )
    back, tied = lax.optimization_barrier((back, tied))
    back = lax.all_to_all(back, every, 0, 0, tiled=True)
    table_grad = back[:, :per].transpose(1, 0, 2).reshape(per, width)
    gain_grad = back[:, per].sum(axis=0)
    return table_grad, gain_grad, tied


def scatter_by_permutes(block, axis):
    count = lax.axis_size(axis)
    me = lax.axis_index(axis)
    rows = block.shape[0] // count
    chunk = lambda index: lax.dynamic_slice_in_dim(block, index * rows, rows, axis=0)
    total = chunk(me)
    for apart in range(1, count):
        pairs = [(source, source ^ apart) for source in range(count)]
        total = total + lax.ppermute(chunk(me ^ apart), axis, pairs)
    return total


def gather_by_permutes(total, axis):
    count = lax.axis_size(axis)
    me = lax.axis_index(axis)
    pieces = [total]
    for apart in range(1, count):
        pairs = [(source, source ^ apart) for source in range(count)]
        pieces.append(lax.ppermute(total, axis, pairs))
    stacked = jnp.stack(pieces)
    return jnp.concatenate(
        [lax.dynamic_index_in_dim(stacked, index ^ me, keepdims=False) for index in range(count)], axis=0
    )


def fetch_halves(block, axis):
    count = lax.axis_size(axis)
    core = lax.axis_index("seq") % 2
    half_rows = block.shape[0] // 2
    mine = lax.dynamic_slice_in_dim(block, core * half_rows, half_rows, axis=0)
    return {
        apart: lax.ppermute(mine, axis, [(source, source ^ apart) for source in range(count)])
        for apart in range(count - 1, 0, -1)
    }


def swap_halves(fetched):
    return {apart: from_partner(piece, "seq", 0) for apart, piece in fetched.items()}


def assemble_shards(block, axis, fetched, swapped):
    count = lax.axis_size(axis)
    me = lax.axis_index(axis)
    core = lax.axis_index("seq") % 2
    rows = block.shape[0]
    half_rows = rows // 2
    whole = jnp.zeros((count * rows,) + block.shape[1:], block.dtype)
    whole = lax.dynamic_update_slice_in_dim(whole, block, me * rows, axis=0)
    for apart in range(1, count):
        base = (me ^ apart) * rows
        whole = lax.dynamic_update_slice_in_dim(whole, fetched[apart], base + core * half_rows, axis=0)
        whole = lax.dynamic_update_slice_in_dim(whole, swapped[apart], base + (1 - core) * half_rows, axis=0)
    return whole


def gather_shards(block, axis):
    fetched = fetch_halves(block, axis)
    return assemble_shards(block, axis, fetched, swap_halves(fetched))


def body(events, type_ids, type_table, norm_gain, kernel, upstream):
    length = events.shape[1]
    width = events.shape[2]
    chans = width // GROUPS
    half = KERNEL // 2
    fsdp = lax.axis_size("fsdp")
    seq_count = lax.axis_size("seq")
    total = length * seq_count * fsdp
    scale = 1.0 / jnp.sqrt(jnp.float32(total))
    if fsdp & (fsdp - 1):
        raise ValueError("fsdp not pow2")
    table = gather_shards(type_table, "fsdp")
    kernel_fetched = fetch_halves(kernel, "fsdp")
    far = fsdp - 1
    types = table.shape[0]
    onehot = (type_ids[0][:, None] == jnp.arange(types, dtype=jnp.int32)[None, :]).astype(jnp.bfloat16)
    mixed = events[0].astype(jnp.float32) + jnp.dot(onehot, table, preferred_element_type=jnp.float32)
    near = {apart: piece for apart, piece in kernel_fetched.items() if apart != far}
    near_swapped = swap_halves(near)
    inv = lax.rsqrt(jnp.mean(mixed * mixed, axis=-1, keepdims=True) + 1e-06)
    normed = (mixed * inv * norm_gain).astype(jnp.bfloat16)
    normed_g = normed.reshape(length, GROUPS, chans).transpose(1, 0, 2)
    padded = with_halo(normed_g, "seq", 1, half)
    far_piece, padded = lax.optimization_barrier((kernel_fetched[far], padded))
    kernel_fetched = {**near, far: far_piece}
    kernel_swapped = {**near_swapped, **swap_halves({far: far_piece})}
    weights = assemble_shards(kernel, "fsdp", kernel_fetched, kernel_swapped).reshape(GROUPS, chans, KERNEL * chans)
    up_float = upstream[0].astype(jnp.float32)
    up_g = up_float.reshape(length, GROUPS, chans).transpose(1, 0, 2)
    dconv = conv_dconv(padded.astype(jnp.float32), weights, up_g)
    dpad = with_halo(dconv, "seq", 1, half)
    dnormed = conv_transpose(dpad.astype(jnp.float32), weights, length)
    if seq_count <= GROUPS:
        group_in = lax.all_to_all(normed_g, "seq", 0, 1, tiled=True)
        group_out = lax.all_to_all(dconv, "seq", 0, 1, tiled=True)
    else:
        group_in, group_out = spread_groups(normed, dconv.transpose(1, 0, 2).reshape(length, width), chans)
    local_groups = group_in.shape[0]
    whole = group_in.shape[1]
    group_pad = jnp.pad(group_in, ((0, 0), (half, half), (0, 0)))
    kterms = [
        jnp.einsum("gto,gtc->goc", group_out, group_pad[:, k : k + whole], preferred_element_type=jnp.float32)
        for k in range(KERNEL)
    ]
    kernel_part = jnp.concatenate(kterms, axis=-1).reshape(-1, KERNEL * chans) * scale
    dnormed = dnormed.transpose(1, 0, 2).reshape(length, width)
    gain_term = jnp.sum(dnormed * mixed * inv, axis=0) * scale
    scaled = norm_gain * dnormed
    dmixed = inv * scaled - mixed * inv * inv * inv * jnp.mean(scaled * mixed, axis=-1, keepdims=True)
    input_grad = (up_float + dmixed).astype(jnp.bfloat16)
    kernel_sum = scatter_by_permutes(kernel_part, "fsdp")
    table_grad, gain_grad, kernel_sum = table_and_gain(input_grad, type_ids[0], gain_term, types, scale, kernel_sum)
    kernel_grad = gather_by_permutes(kernel_sum, "fsdp")
    return (input_grad[None], table_grad, gain_grad, kernel_grad)


def solution(mesh):
    return jax.shard_map(
        body,
        mesh=mesh,
        in_specs=(
            P("fsdp", "seq", None),
            P("fsdp", "seq"),
            P("fsdp", None),
            P(),
            P("fsdp", None),
            P("fsdp", "seq", None),
        ),
        out_specs=(
            P("fsdp", "seq", None),
            P(("fsdp", "seq"), None),
            P(("fsdp", "seq")),
            P("seq", None),
        ),
        check_vma=False,
    )
```

```python
import jax
import jax.numpy as jnp
from jax import lax
from jax.experimental import pallas as pl
from jax.experimental.pallas import tpu as pltpu
from jax.sharding import PartitionSpec as P

GROUPS = 16
KERNEL = 9


def with_halo(cells, axis, dim, width):
    count = lax.axis_size(axis)
    ends = count - 1
    head = lax.slice_in_dim(cells, 0, width, axis=dim)
    tail = lax.slice_in_dim(cells, cells.shape[dim] - width, cells.shape[dim], axis=dim)
    return jnp.concatenate(
        [
            lax.ppermute(tail, axis, [(i, (i + 1) % count) for i in range(ends)]),
            cells,
            lax.ppermute(head, axis, [((i + 1) % count, i) for i in range(ends)]),
        ],
        axis=dim,
    )


def from_partner(value, axis, apart):
    mask = 2**apart
    pairs = [(source, source ^ mask) for source in range(lax.axis_size(axis))]
    return lax.ppermute(value, axis, pairs)


def gather_rows(block, axis):
    count = lax.axis_size(axis)
    return lax.all_to_all(jnp.tile(block, (count,) + (1,) * (block.ndim - 1)), axis, 0, 0, tiled=True)


STEP_GROUPS = 4


def forward_kernel(pad_ref, w_ref, up_ref, out_ref):
    length = out_ref.shape[1]
    for g in range(out_ref.shape[0]):
        rows = pad_ref[g].astype(jnp.float32)
        x = jnp.concatenate([rows[k : k + length].astype(jnp.bfloat16) for k in range(KERNEL)], axis=1)
        acc = lax.dot_general(x, w_ref[g], (((1,), (1,)), ((), ())), preferred_element_type=jnp.float32)
        sig = 1.0 / (1.0 + jnp.exp(-acc))
        out_ref[g] = (up_ref[g] * sig * (1.0 + acc * (1.0 - sig))).astype(out_ref.dtype)


def backward_kernel(pad_ref, w_ref, out_ref):
    length = out_ref.shape[1]
    chans = out_ref.shape[2]
    half = KERNEL // 2
    for g in range(out_ref.shape[0]):
        rows = pad_ref[g].astype(jnp.float32)
        x = jnp.concatenate(
            [rows[2 * half - k : 2 * half - k + length].astype(jnp.bfloat16) for k in range(KERNEL)], axis=1
        )
        w = jnp.concatenate([w_ref[g, :, k * chans : (k + 1) * chans] for k in range(KERNEL)], axis=0)
        out_ref[g] = jnp.dot(x, w, preferred_element_type=jnp.float32)


def conv_dconv(padded, weights, up):
    groups, rows, chans = padded.shape
    length = up.shape[1]
    step = STEP_GROUPS if groups % STEP_GROUPS == 0 else 1
    flops = 2 * groups * length * chans * weights.shape[1] * KERNEL
    return pl.pallas_call(
        forward_kernel,
        grid=(groups // step,),
        in_specs=[
            pl.BlockSpec((step, rows, chans), lambda i: (i, 0, 0)),
            pl.BlockSpec((step, weights.shape[1], weights.shape[2]), lambda i: (i, 0, 0)),
            pl.BlockSpec((step, length, up.shape[2]), lambda i: (i, 0, 0)),
        ],
        out_specs=pl.BlockSpec((step, length, up.shape[2]), lambda i: (i, 0, 0)),
        out_shape=jax.ShapeDtypeStruct(up.shape, jnp.bfloat16),
        cost_estimate=pl.CostEstimate(
            flops=flops,
            transcendentals=up.size,
            bytes_accessed=padded.size * 2 + weights.size * 2 + up.size * 6,
        ),
    )(padded, weights, up)


def conv_transpose(dpad, weights, length):
    groups, rows, outs = dpad.shape
    chans = weights.shape[2] // KERNEL
    step = STEP_GROUPS if groups % STEP_GROUPS == 0 else 1
    return pl.pallas_call(
        backward_kernel,
        grid=(groups // step,),
        in_specs=[
            pl.BlockSpec((step, rows, outs), lambda i: (i, 0, 0)),
            pl.BlockSpec((step, weights.shape[1], weights.shape[2]), lambda i: (i, 0, 0)),
        ],
        out_specs=pl.BlockSpec((step, length, chans), lambda i: (i, 0, 0)),
        out_shape=jax.ShapeDtypeStruct((groups, length, chans), jnp.float32),
        cost_estimate=pl.CostEstimate(
            flops=2 * groups * length * chans * outs * KERNEL,
            transcendentals=0,
            bytes_accessed=dpad.size * 2 + weights.size * 2 + groups * length * chans * 4,
        ),
    )(dpad, weights)


def spread_groups(normed, dflat, chans):
    normed_slice = lax.all_to_all(normed, "seq", 1, 0, tiled=True)
    dconv_slice = lax.all_to_all(dflat, "seq", 1, 0, tiled=True)
    whole, slice_width = normed_slice.shape
    spread = chans // slice_width
    position = lax.axis_index("seq")
    group_rows = normed_slice
    for bit in range(spread.bit_length() - 1):
        partner = from_partner(group_rows, "seq", bit)
        lower = position >> bit & 1 == 0
        group_rows = jnp.where(
            lower,
            jnp.concatenate([group_rows, partner], axis=1),
            jnp.concatenate([partner, group_rows], axis=1),
        )
    return group_rows.reshape(1, whole, chans), dconv_slice.reshape(1, whole, slice_width)


def sum_rows(block, axis):
    count = lax.axis_size(axis)
    parts = block.reshape(count, block.shape[0] // count, *block.shape[1:])
    return lax.all_to_all(parts, axis, 0, 0, tiled=True).sum(axis=0)


def psum_rows(block, axis):
    return gather_rows(sum_rows(block, axis), axis)


def table_and_gain(input_grad, ids, gain_term, types, scale, tied):
    every = ("fsdp", "seq")
    count = lax.axis_size("fsdp") * lax.axis_size("seq")
    length, width = input_grad.shape
    narrow = width // count
    id_rows = -(-length // narrow)
    ids_wide = jnp.zeros((id_rows * narrow,), jnp.bfloat16).at[:length].set(ids.astype(jnp.bfloat16))
    send = jnp.concatenate(
        [
            input_grad.reshape(length, count, narrow).transpose(1, 0, 2),
            jnp.broadcast_to(ids_wide.reshape(1, id_rows, narrow), (count, id_rows, narrow)),
        ],
        axis=1,
    )
    got = lax.all_to_all(send, every, 0, 0, tiled=True)
    rows_all = got[:, :length].reshape(count * length, narrow)
    ids_all = got[:, length:].reshape(count, id_rows * narrow)[:, :length].reshape(-1).astype(jnp.int32)
    onehot = (ids_all[:, None] == jnp.arange(types, dtype=jnp.int32)[None, :]).astype(jnp.bfloat16)
    columns = lax.dot_general(onehot, rows_all, (((0,), (0,)), ((), ())), preferred_element_type=jnp.float32)
    columns = columns * scale
    per = types // count
    back = jnp.concatenate(
        [columns.reshape(count, per, narrow), gain_term.reshape(count, 1, narrow)], axis=1
    )
    back, tied = lax.optimization_barrier((back, tied))
    back = lax.all_to_all(back, every, 0, 0, tiled=True)
    table_grad = back[:, :per].transpose(1, 0, 2).reshape(per, width)
    gain_grad = back[:, per].sum(axis=0)
    return table_grad, gain_grad, tied


def scatter_by_permutes(block, axis):
    count = lax.axis_size(axis)
    me = lax.axis_index(axis)
    rows = block.shape[0] // count
    chunk = lambda index: lax.dynamic_slice_in_dim(block, index * rows, rows, axis=0)
    total = chunk(me)
    for apart in range(1, count):
        pairs = [(source, source ^ apart) for source in range(count)]
        total = total + lax.ppermute(chunk(me ^ apart), axis, pairs)
    return total


def gather_by_permutes(total, axis):
    count = lax.axis_size(axis)
    me = lax.axis_index(axis)
    pieces = [total]
    for apart in range(1, count):
        pairs = [(source, source ^ apart) for source in range(count)]
        pieces.append(lax.ppermute(total, axis, pairs))
    stacked = jnp.stack(pieces)
    return jnp.concatenate(
        [lax.dynamic_index_in_dim(stacked, index ^ me, keepdims=False) for index in range(count)], axis=0
    )


def fetch_halves(block, axis):
    count = lax.axis_size(axis)
    core = lax.axis_index("seq") % 2
    half_rows = block.shape[0] // 2
    mine = lax.dynamic_slice_in_dim(block, core * half_rows, half_rows, axis=0)
    return {
        apart: lax.ppermute(mine, axis, [(source, source ^ apart) for source in range(count)])
        for apart in range(count - 1, 0, -1)
    }


def swap_halves(fetched):
    return {apart: from_partner(piece, "seq", 0) for apart, piece in fetched.items()}


def assemble_shards(block, axis, fetched, swapped):
    count = lax.axis_size(axis)
    me = lax.axis_index(axis)
    core = lax.axis_index("seq") % 2
    blocks = [block]
    for apart in range(1, count):
        lower = jnp.where(core == 0, fetched[apart], swapped[apart])
        upper = jnp.where(core == 0, swapped[apart], fetched[apart])
        blocks.append(jnp.concatenate([lower, upper], axis=0))
    stacked = jnp.stack(blocks)
    return jnp.concatenate(
        [lax.dynamic_index_in_dim(stacked, index ^ me, keepdims=False) for index in range(count)], axis=0
    )


def gather_shards(block, axis):
    fetched = fetch_halves(block, axis)
    return assemble_shards(block, axis, fetched, swap_halves(fetched))


def body(events, type_ids, type_table, norm_gain, kernel, upstream):
    length = events.shape[1]
    width = events.shape[2]
    chans = width // GROUPS
    half = KERNEL // 2
    fsdp = lax.axis_size("fsdp")
    seq_count = lax.axis_size("seq")
    total = length * seq_count * fsdp
    scale = 1.0 / jnp.sqrt(jnp.float32(total))
    if fsdp & (fsdp - 1):
        raise ValueError("fsdp not pow2")
    table = gather_shards(type_table, "fsdp")
    kernel_fetched = fetch_halves(kernel, "fsdp")
    far = fsdp - 1
    types = table.shape[0]
    onehot = (type_ids[0][:, None] == jnp.arange(types, dtype=jnp.int32)[None, :]).astype(jnp.bfloat16)
    mixed = events[0].astype(jnp.float32) + jnp.dot(onehot, table, preferred_element_type=jnp.float32)
    near = {apart: piece for apart, piece in kernel_fetched.items() if apart != far}
    near_swapped = swap_halves(near)
    inv = lax.rsqrt(jnp.mean(mixed * mixed, axis=-1, keepdims=True) + 1e-06)
    normed = (mixed * inv * norm_gain).astype(jnp.bfloat16)
    normed_g = normed.reshape(length, GROUPS, chans).transpose(1, 0, 2)
    padded = with_halo(normed_g, "seq", 1, half)
    far_piece, padded = lax.optimization_barrier((kernel_fetched[far], padded))
    kernel_fetched = {**near, far: far_piece}
    kernel_swapped = {**near_swapped, **swap_halves({far: far_piece})}
    weights = assemble_shards(kernel, "fsdp", kernel_fetched, kernel_swapped).reshape(GROUPS, chans, KERNEL * chans)
    up_float = upstream[0].astype(jnp.float32)
    up_g = up_float.reshape(length, GROUPS, chans).transpose(1, 0, 2)
    dconv = conv_dconv(padded, weights, up_g)
    dpad = with_halo(dconv, "seq", 1, half)
    dnormed = conv_transpose(dpad, weights, length)
    if seq_count <= GROUPS:
        group_in = lax.all_to_all(normed_g, "seq", 0, 1, tiled=True)
        group_out = lax.all_to_all(dconv, "seq", 0, 1, tiled=True)
    else:
        group_in, group_out = spread_groups(normed, dconv.transpose(1, 0, 2).reshape(length, width), chans)
    local_groups = group_in.shape[0]
    whole = group_in.shape[1]
    group_pad = jnp.pad(group_in, ((0, 0), (half, half), (0, 0)))
    kterms = [
        jnp.einsum("gto,gtc->goc", group_out, group_pad[:, k : k + whole], preferred_element_type=jnp.float32)
        for k in range(KERNEL)
    ]
    kernel_part = jnp.concatenate(kterms, axis=-1).reshape(-1, KERNEL * chans) * scale
    dnormed = dnormed.transpose(1, 0, 2).reshape(length, width)
    gain_term = jnp.sum(dnormed * mixed * inv, axis=0) * scale
    scaled = norm_gain * dnormed
    dmixed = inv * scaled - mixed * inv * inv * inv * jnp.mean(scaled * mixed, axis=-1, keepdims=True)
    input_grad = (up_float + dmixed).astype(jnp.bfloat16)
    kernel_sum = scatter_by_permutes(kernel_part, "fsdp")
    table_grad, gain_grad, kernel_sum = table_and_gain(input_grad, type_ids[0], gain_term, types, scale, kernel_sum)
    kernel_grad = gather_by_permutes(kernel_sum, "fsdp")
    return (input_grad[None], table_grad, gain_grad, kernel_grad)


def solution(mesh):
    return jax.shard_map(
        body,
        mesh=mesh,
        in_specs=(
            P("fsdp", "seq", None),
            P("fsdp", "seq"),
            P("fsdp", None),
            P(),
            P("fsdp", None),
            P("fsdp", "seq", None),
        ),
        out_specs=(
            P("fsdp", "seq", None),
            P(("fsdp", "seq"), None),
            P(("fsdp", "seq")),
            P("seq", None),
        ),
        check_vma=False,
    )
```

```python
import jax
import jax.numpy as jnp
from jax import lax
from jax.experimental import pallas as pl
from jax.experimental.pallas import tpu as pltpu
from jax.sharding import PartitionSpec as P

GROUPS = 16
KERNEL = 9


def with_halo(cells, axis, dim, width):
    count = lax.axis_size(axis)
    ends = count - 1
    head = lax.slice_in_dim(cells, 0, width, axis=dim)
    tail = lax.slice_in_dim(cells, cells.shape[dim] - width, cells.shape[dim], axis=dim)
    return jnp.concatenate(
        [
            lax.ppermute(tail, axis, [(i, (i + 1) % count) for i in range(ends)]),
            cells,
            lax.ppermute(head, axis, [((i + 1) % count, i) for i in range(ends)]),
        ],
        axis=dim,
    )


def from_partner(value, axis, apart):
    mask = 2**apart
    pairs = [(source, source ^ mask) for source in range(lax.axis_size(axis))]
    return lax.ppermute(value, axis, pairs)


def gather_rows(block, axis):
    count = lax.axis_size(axis)
    return lax.all_to_all(jnp.tile(block, (count,) + (1,) * (block.ndim - 1)), axis, 0, 0, tiled=True)


STEP_GROUPS = 4


def forward_kernel(pad_ref, w_ref, up_ref, out_ref):
    length = out_ref.shape[1]
    for g in range(out_ref.shape[0]):
        rows = pad_ref[g].astype(jnp.float32)
        x = jnp.concatenate([rows[k : k + length].astype(jnp.bfloat16) for k in range(KERNEL)], axis=1)
        acc = lax.dot_general(x, w_ref[g], (((1,), (1,)), ((), ())), preferred_element_type=jnp.float32)
        sig = 1.0 / (1.0 + jnp.exp(-acc))
        out_ref[g] = (up_ref[g] * sig * (1.0 + acc * (1.0 - sig))).astype(out_ref.dtype)


def backward_kernel(pad_ref, w_ref, out_ref):
    length = out_ref.shape[1]
    chans = out_ref.shape[2]
    half = KERNEL // 2
    for g in range(out_ref.shape[0]):
        rows = pad_ref[g].astype(jnp.float32)
        x = jnp.concatenate(
            [rows[2 * half - k : 2 * half - k + length].astype(jnp.bfloat16) for k in range(KERNEL)], axis=1
        )
        w = jnp.concatenate([w_ref[g, :, k * chans : (k + 1) * chans] for k in range(KERNEL)], axis=0)
        out_ref[g] = jnp.dot(x, w, preferred_element_type=jnp.float32)


def conv_dconv(padded, weights, up):
    groups, rows, chans = padded.shape
    length = up.shape[1]
    step = STEP_GROUPS if groups % STEP_GROUPS == 0 else 1
    flops = 2 * groups * length * chans * weights.shape[1] * KERNEL
    return pl.pallas_call(
        forward_kernel,
        grid=(groups // step,),
        in_specs=[
            pl.BlockSpec((step, rows, chans), lambda i: (i, 0, 0)),
            pl.BlockSpec((step, weights.shape[1], weights.shape[2]), lambda i: (i, 0, 0)),
            pl.BlockSpec((step, length, up.shape[2]), lambda i: (i, 0, 0)),
        ],
        out_specs=pl.BlockSpec((step, length, up.shape[2]), lambda i: (i, 0, 0)),
        out_shape=jax.ShapeDtypeStruct(up.shape, jnp.bfloat16),
        cost_estimate=pl.CostEstimate(
            flops=flops,
            transcendentals=up.size,
            bytes_accessed=padded.size * 2 + weights.size * 2 + up.size * 6,
        ),
    )(padded, weights, up)


def conv_transpose(dpad, weights, length):
    groups, rows, outs = dpad.shape
    chans = weights.shape[2] // KERNEL
    step = STEP_GROUPS if groups % STEP_GROUPS == 0 else 1
    return pl.pallas_call(
        backward_kernel,
        grid=(groups // step,),
        in_specs=[
            pl.BlockSpec((step, rows, outs), lambda i: (i, 0, 0)),
            pl.BlockSpec((step, weights.shape[1], weights.shape[2]), lambda i: (i, 0, 0)),
        ],
        out_specs=pl.BlockSpec((step, length, chans), lambda i: (i, 0, 0)),
        out_shape=jax.ShapeDtypeStruct((groups, length, chans), jnp.float32),
        cost_estimate=pl.CostEstimate(
            flops=2 * groups * length * chans * outs * KERNEL,
            transcendentals=0,
            bytes_accessed=dpad.size * 2 + weights.size * 2 + groups * length * chans * 4,
        ),
    )(dpad, weights)


def spread_groups(normed, dflat, chans):
    normed_slice = lax.all_to_all(normed, "seq", 1, 0, tiled=True)
    dconv_slice = lax.all_to_all(dflat, "seq", 1, 0, tiled=True)
    whole, slice_width = normed_slice.shape
    spread = chans // slice_width
    position = lax.axis_index("seq")
    group_rows = normed_slice
    for bit in range(spread.bit_length() - 1):
        partner = from_partner(group_rows, "seq", bit)
        lower = position >> bit & 1 == 0
        group_rows = jnp.where(
            lower,
            jnp.concatenate([group_rows, partner], axis=1),
            jnp.concatenate([partner, group_rows], axis=1),
        )
    return group_rows.reshape(1, whole, chans), dconv_slice.reshape(1, whole, slice_width)


def sum_rows(block, axis):
    count = lax.axis_size(axis)
    parts = block.reshape(count, block.shape[0] // count, *block.shape[1:])
    return lax.all_to_all(parts, axis, 0, 0, tiled=True).sum(axis=0)


def psum_rows(block, axis):
    return gather_rows(sum_rows(block, axis), axis)


def table_and_gain(input_grad, ids, gain_term, types, scale, tied):
    every = ("fsdp", "seq")
    count = lax.axis_size("fsdp") * lax.axis_size("seq")
    length, width = input_grad.shape
    narrow = width // count
    id_rows = -(-length // narrow)
    ids_wide = jnp.zeros((id_rows * narrow,), jnp.bfloat16).at[:length].set(ids.astype(jnp.bfloat16))
    send = jnp.concatenate(
        [
            input_grad.reshape(length, count, narrow).transpose(1, 0, 2),
            jnp.broadcast_to(ids_wide.reshape(1, id_rows, narrow), (count, id_rows, narrow)),
        ],
        axis=1,
    )
    got = lax.all_to_all(send, every, 0, 0, tiled=True)
    rows_all = got[:, :length].reshape(count * length, narrow)
    ids_all = got[:, length:].reshape(count, id_rows * narrow)[:, :length].reshape(-1).astype(jnp.int32)
    onehot = (ids_all[:, None] == jnp.arange(types, dtype=jnp.int32)[None, :]).astype(jnp.bfloat16)
    columns = lax.dot_general(onehot, rows_all, (((0,), (0,)), ((), ())), preferred_element_type=jnp.float32)
    columns = columns * scale
    per = types // count
    back = jnp.concatenate(
        [columns.reshape(count, per, narrow), gain_term.reshape(count, 1, narrow)], axis=1
    )
    back, tied = lax.optimization_barrier((back, tied))
    back = lax.all_to_all(back, every, 0, 0, tiled=True)
    table_grad = back[:, :per].transpose(1, 0, 2).reshape(per, width)
    gain_grad = back[:, per].sum(axis=0)
    return table_grad, gain_grad, tied


def scatter_by_permutes(block, axis):
    count = lax.axis_size(axis)
    me = lax.axis_index(axis)
    rows = block.shape[0] // count
    chunk = lambda index: lax.dynamic_slice_in_dim(block, index * rows, rows, axis=0)
    total = chunk(me)
    for apart in range(1, count):
        pairs = [(source, source ^ apart) for source in range(count)]
        total = total + lax.ppermute(chunk(me ^ apart), axis, pairs)
    return total


def gather_by_permutes(total, axis):
    count = lax.axis_size(axis)
    me = lax.axis_index(axis)
    pieces = [total]
    for apart in range(1, count):
        pairs = [(source, source ^ apart) for source in range(count)]
        pieces.append(lax.ppermute(total, axis, pairs))
    stacked = jnp.stack(pieces)
    return jnp.concatenate(
        [lax.dynamic_index_in_dim(stacked, index ^ me, keepdims=False) for index in range(count)], axis=0
    )


def fetch_halves(block, axis):
    count = lax.axis_size(axis)
    core = lax.axis_index("seq") % 2
    half_rows = block.shape[0] // 2
    mine = lax.dynamic_slice_in_dim(block, core * half_rows, half_rows, axis=0)
    return {
        apart: lax.ppermute(mine, axis, [(source, source ^ apart) for source in range(count)])
        for apart in range(count - 1, 0, -1)
    }


def swap_halves(fetched):
    return {apart: from_partner(piece, "seq", 0) for apart, piece in fetched.items()}


def assemble_shards(block, axis, fetched, swapped):
    count = lax.axis_size(axis)
    me = lax.axis_index(axis)
    core = lax.axis_index("seq") % 2
    blocks = [block]
    for apart in range(1, count):
        lower = jnp.where(core == 0, fetched[apart], swapped[apart])
        upper = jnp.where(core == 0, swapped[apart], fetched[apart])
        blocks.append(jnp.concatenate([lower, upper], axis=0))
    stacked = jnp.stack(blocks)
    return jnp.concatenate(
        [lax.dynamic_index_in_dim(stacked, index ^ me, keepdims=False) for index in range(count)], axis=0
    )


def gather_shards(block, axis):
    fetched = fetch_halves(block, axis)
    return assemble_shards(block, axis, fetched, swap_halves(fetched))


def body(events, type_ids, type_table, norm_gain, kernel, upstream):
    length = events.shape[1]
    width = events.shape[2]
    chans = width // GROUPS
    half = KERNEL // 2
    fsdp = lax.axis_size("fsdp")
    seq_count = lax.axis_size("seq")
    total = length * seq_count * fsdp
    scale = 1.0 / jnp.sqrt(jnp.float32(total))
    if fsdp & (fsdp - 1):
        raise ValueError("fsdp not pow2")
    table = gather_shards(type_table, "fsdp")
    kernel_fetched = fetch_halves(kernel, "fsdp")
    far = fsdp - 1
    types = table.shape[0]
    onehot = (type_ids[0][:, None] == jnp.arange(types, dtype=jnp.int32)[None, :]).astype(jnp.bfloat16)
    mixed = events[0].astype(jnp.float32) + jnp.dot(onehot, table, preferred_element_type=jnp.float32)
    near = {apart: piece for apart, piece in kernel_fetched.items() if apart != far}
    near_swapped = swap_halves(near)
    inv = lax.rsqrt(jnp.mean(mixed * mixed, axis=-1, keepdims=True) + 1e-06)
    normed = (mixed * inv * norm_gain).astype(jnp.bfloat16)
    normed_g = normed.reshape(length, GROUPS, chans).transpose(1, 0, 2)
    padded = with_halo(normed_g, "seq", 1, 2 * half)
    up_pad = with_halo(upstream[0].reshape(length, GROUPS, chans).transpose(1, 0, 2), "seq", 1, half)
    far_piece, padded = lax.optimization_barrier((kernel_fetched[far], padded))
    kernel_fetched = {**near, far: far_piece}
    kernel_swapped = {**near_swapped, **swap_halves({far: far_piece})}
    weights = assemble_shards(kernel, "fsdp", kernel_fetched, kernel_swapped).reshape(GROUPS, chans, KERNEL * chans)
    up_float = upstream[0].astype(jnp.float32)
    up_g = up_float.reshape(length, GROUPS, chans).transpose(1, 0, 2)
    dpad = conv_dconv(padded, weights, up_pad.astype(jnp.float32))
    dconv = dpad[:, half : half + length]
    dnormed = conv_transpose(dpad, weights, length)
    if seq_count <= GROUPS:
        group_in = lax.all_to_all(normed_g, "seq", 0, 1, tiled=True)
        group_out = lax.all_to_all(dconv, "seq", 0, 1, tiled=True)
    else:
        group_in, group_out = spread_groups(normed, dconv.transpose(1, 0, 2).reshape(length, width), chans)
    local_groups = group_in.shape[0]
    whole = group_in.shape[1]
    group_pad = jnp.pad(group_in, ((0, 0), (half, half), (0, 0)))
    kterms = [
        jnp.einsum("gto,gtc->goc", group_out, group_pad[:, k : k + whole], preferred_element_type=jnp.float32)
        for k in range(KERNEL)
    ]
    kernel_part = jnp.concatenate(kterms, axis=-1).reshape(-1, KERNEL * chans) * scale
    dnormed = dnormed.transpose(1, 0, 2).reshape(length, width)
    gain_term = jnp.sum(dnormed * mixed * inv, axis=0) * scale
    scaled = norm_gain * dnormed
    dmixed = inv * scaled - mixed * inv * inv * inv * jnp.mean(scaled * mixed, axis=-1, keepdims=True)
    input_grad = (up_float + dmixed).astype(jnp.bfloat16)
    kernel_sum = scatter_by_permutes(kernel_part, "fsdp")
    table_grad, gain_grad, kernel_sum = table_and_gain(input_grad, type_ids[0], gain_term, types, scale, kernel_sum)
    kernel_grad = gather_by_permutes(kernel_sum, "fsdp")
    return (input_grad[None], table_grad, gain_grad, kernel_grad)


def solution(mesh):
    return jax.shard_map(
        body,
        mesh=mesh,
        in_specs=(
            P("fsdp", "seq", None),
            P("fsdp", "seq"),
            P("fsdp", None),
            P(),
            P("fsdp", None),
            P("fsdp", "seq", None),
        ),
        out_specs=(
            P("fsdp", "seq", None),
            P(("fsdp", "seq"), None),
            P(("fsdp", "seq")),
            P("seq", None),
        ),
        check_vma=False,
    )
```

```python
import jax
import jax.numpy as jnp
from jax import lax
from jax.experimental import pallas as pl
from jax.experimental.pallas import tpu as pltpu
from jax.sharding import PartitionSpec as P

GROUPS = 16
KERNEL = 9


def with_halo(cells, axis, dim, width):
    count = lax.axis_size(axis)
    ends = count - 1
    head = lax.slice_in_dim(cells, 0, width, axis=dim)
    tail = lax.slice_in_dim(cells, cells.shape[dim] - width, cells.shape[dim], axis=dim)
    return jnp.concatenate(
        [
            lax.ppermute(tail, axis, [(i, (i + 1) % count) for i in range(ends)]),
            cells,
            lax.ppermute(head, axis, [((i + 1) % count, i) for i in range(ends)]),
        ],
        axis=dim,
    )


def from_partner(value, axis, apart):
    mask = 2**apart
    pairs = [(source, source ^ mask) for source in range(lax.axis_size(axis))]
    return lax.ppermute(value, axis, pairs)


def gather_rows(block, axis):
    count = lax.axis_size(axis)
    return lax.all_to_all(jnp.tile(block, (count,) + (1,) * (block.ndim - 1)), axis, 0, 0, tiled=True)


STEP_GROUPS = 4


def forward_kernel(pad_ref, w_ref, up_ref, out_ref):
    length = out_ref.shape[1]
    for g in range(out_ref.shape[0]):
        rows = pad_ref[g].astype(jnp.float32)
        x = jnp.concatenate([rows[k : k + length].astype(jnp.bfloat16) for k in range(KERNEL)], axis=1)
        acc = lax.dot_general(x, w_ref[g], (((1,), (1,)), ((), ())), preferred_element_type=jnp.float32)
        sig = 1.0 / (1.0 + jnp.exp(-acc))
        out_ref[g] = (up_ref[g] * sig * (1.0 + acc * (1.0 - sig))).astype(out_ref.dtype)


def backward_kernel(pad_ref, w_ref, out_ref):
    length = out_ref.shape[1]
    chans = out_ref.shape[2]
    half = KERNEL // 2
    for g in range(out_ref.shape[0]):
        rows = pad_ref[g].astype(jnp.float32)
        x = jnp.concatenate(
            [rows[2 * half - k : 2 * half - k + length].astype(jnp.bfloat16) for k in range(KERNEL)], axis=1
        )
        w = jnp.concatenate([w_ref[g, :, k * chans : (k + 1) * chans] for k in range(KERNEL)], axis=0)
        out_ref[g] = jnp.dot(x, w, preferred_element_type=jnp.float32)


def conv_dconv(padded, weights, up):
    groups, rows, chans = padded.shape
    length = up.shape[1]
    step = STEP_GROUPS if groups % STEP_GROUPS == 0 else 1
    flops = 2 * groups * length * chans * weights.shape[1] * KERNEL
    return pl.pallas_call(
        forward_kernel,
        grid=(groups // step,),
        in_specs=[
            pl.BlockSpec((step, rows, chans), lambda i: (i, 0, 0)),
            pl.BlockSpec((step, weights.shape[1], weights.shape[2]), lambda i: (i, 0, 0)),
            pl.BlockSpec((step, length, up.shape[2]), lambda i: (i, 0, 0)),
        ],
        out_specs=pl.BlockSpec((step, length, up.shape[2]), lambda i: (i, 0, 0)),
        out_shape=jax.ShapeDtypeStruct(up.shape, jnp.bfloat16),
        cost_estimate=pl.CostEstimate(
            flops=flops,
            transcendentals=up.size,
            bytes_accessed=padded.size * 2 + weights.size * 2 + up.size * 6,
        ),
    )(padded, weights, up)


def conv_transpose(dpad, weights, length):
    groups, rows, outs = dpad.shape
    chans = weights.shape[2] // KERNEL
    step = STEP_GROUPS if groups % STEP_GROUPS == 0 else 1
    return pl.pallas_call(
        backward_kernel,
        grid=(groups // step,),
        in_specs=[
            pl.BlockSpec((step, rows, outs), lambda i: (i, 0, 0)),
            pl.BlockSpec((step, weights.shape[1], weights.shape[2]), lambda i: (i, 0, 0)),
        ],
        out_specs=pl.BlockSpec((step, length, chans), lambda i: (i, 0, 0)),
        out_shape=jax.ShapeDtypeStruct((groups, length, chans), jnp.float32),
        cost_estimate=pl.CostEstimate(
            flops=2 * groups * length * chans * outs * KERNEL,
            transcendentals=0,
            bytes_accessed=dpad.size * 2 + weights.size * 2 + groups * length * chans * 4,
        ),
    )(dpad, weights)


def spread_groups(normed, dflat, chans):
    normed_slice = lax.all_to_all(normed, "seq", 1, 0, tiled=True)
    dconv_slice = lax.all_to_all(dflat, "seq", 1, 0, tiled=True)
    whole, slice_width = normed_slice.shape
    spread = chans // slice_width
    position = lax.axis_index("seq")
    group_rows = normed_slice
    for bit in range(spread.bit_length() - 1):
        partner = from_partner(group_rows, "seq", bit)
        lower = position >> bit & 1 == 0
        group_rows = jnp.where(
            lower,
            jnp.concatenate([group_rows, partner], axis=1),
            jnp.concatenate([partner, group_rows], axis=1),
        )
    return group_rows.reshape(1, whole, chans), dconv_slice.reshape(1, whole, slice_width)


def sum_rows(block, axis):
    count = lax.axis_size(axis)
    parts = block.reshape(count, block.shape[0] // count, *block.shape[1:])
    return lax.all_to_all(parts, axis, 0, 0, tiled=True).sum(axis=0)


def psum_rows(block, axis):
    return gather_rows(sum_rows(block, axis), axis)


def table_and_gain(input_grad, ids, gain_term, types, scale, tied):
    every = ("fsdp", "seq")
    count = lax.axis_size("fsdp") * lax.axis_size("seq")
    length, width = input_grad.shape
    narrow = width // count
    id_rows = -(-length // narrow)
    ids_wide = jnp.zeros((id_rows * narrow,), jnp.bfloat16).at[:length].set(ids.astype(jnp.bfloat16))
    send = jnp.concatenate(
        [
            input_grad.reshape(length, count, narrow).transpose(1, 0, 2),
            jnp.broadcast_to(ids_wide.reshape(1, id_rows, narrow), (count, id_rows, narrow)),
        ],
        axis=1,
    )
    got = lax.all_to_all(send, every, 0, 0, tiled=True)
    rows_all = got[:, :length].reshape(count * length, narrow)
    ids_all = got[:, length:].reshape(count, id_rows * narrow)[:, :length].reshape(-1).astype(jnp.int32)
    onehot = (ids_all[:, None] == jnp.arange(types, dtype=jnp.int32)[None, :]).astype(jnp.bfloat16)
    columns = lax.dot_general(onehot, rows_all, (((0,), (0,)), ((), ())), preferred_element_type=jnp.float32)
    columns = columns * scale
    per = types // count
    back = jnp.concatenate(
        [columns.reshape(count, per, narrow), gain_term.reshape(count, 1, narrow)], axis=1
    )
    back, tied = lax.optimization_barrier((back, tied))
    back = lax.all_to_all(back, every, 0, 0, tiled=True)
    table_grad = back[:, :per].transpose(1, 0, 2).reshape(per, width)
    gain_grad = back[:, per].sum(axis=0)
    return table_grad, gain_grad, tied


def scatter_by_permutes(block, axis):
    count = lax.axis_size(axis)
    me = lax.axis_index(axis)
    rows = block.shape[0] // count
    chunk = lambda index: lax.dynamic_slice_in_dim(block, index * rows, rows, axis=0)
    total = chunk(me)
    for apart in range(1, count):
        pairs = [(source, source ^ apart) for source in range(count)]
        total = total + lax.ppermute(chunk(me ^ apart), axis, pairs)
    return total


def gather_by_permutes(total, axis):
    count = lax.axis_size(axis)
    me = lax.axis_index(axis)
    pieces = [total]
    for apart in range(1, count):
        pairs = [(source, source ^ apart) for source in range(count)]
        pieces.append(lax.ppermute(total, axis, pairs))
    stacked = jnp.stack(pieces)
    return jnp.concatenate(
        [lax.dynamic_index_in_dim(stacked, index ^ me, keepdims=False) for index in range(count)], axis=0
    )


def fetch_halves(block, axis):
    count = lax.axis_size(axis)
    core = lax.axis_index("seq") % 2
    half_rows = block.shape[0] // 2
    mine = lax.dynamic_slice_in_dim(block, core * half_rows, half_rows, axis=0)
    return {
        apart: lax.ppermute(mine, axis, [(source, source ^ apart) for source in range(count)])
        for apart in range(count - 1, 0, -1)
    }


def swap_halves(fetched):
    return {apart: from_partner(piece, "seq", 0) for apart, piece in fetched.items()}


def assemble_shards(block, axis, fetched, swapped):
    count = lax.axis_size(axis)
    me = lax.axis_index(axis)
    core = lax.axis_index("seq") % 2
    blocks = [block]
    for apart in range(1, count):
        lower = jnp.where(core == 0, fetched[apart], swapped[apart])
        upper = jnp.where(core == 0, swapped[apart], fetched[apart])
        blocks.append(jnp.concatenate([lower, upper], axis=0))
    stacked = jnp.stack(blocks)
    return jnp.concatenate(
        [lax.dynamic_index_in_dim(stacked, index ^ me, keepdims=False) for index in range(count)], axis=0
    )


def gather_shards(block, axis):
    fetched = fetch_halves(block, axis)
    return assemble_shards(block, axis, fetched, swap_halves(fetched))


def body(events, type_ids, type_table, norm_gain, kernel, upstream):
    length = events.shape[1]
    width = events.shape[2]
    chans = width // GROUPS
    half = KERNEL // 2
    fsdp = lax.axis_size("fsdp")
    seq_count = lax.axis_size("seq")
    total = length * seq_count * fsdp
    scale = 1.0 / jnp.sqrt(jnp.float32(total))
    if fsdp & (fsdp - 1):
        raise ValueError("fsdp not pow2")
    table = gather_by_permutes(type_table, "fsdp")
    kernel_fetched = fetch_halves(kernel, "fsdp")
    far = fsdp - 1
    types = table.shape[0]
    onehot = (type_ids[0][:, None] == jnp.arange(types, dtype=jnp.int32)[None, :]).astype(jnp.bfloat16)
    mixed = events[0].astype(jnp.float32) + jnp.dot(onehot, table, preferred_element_type=jnp.float32)
    near = {apart: piece for apart, piece in kernel_fetched.items() if apart != far}
    near_swapped = swap_halves(near)
    inv = lax.rsqrt(jnp.mean(mixed * mixed, axis=-1, keepdims=True) + 1e-06)
    normed = (mixed * inv * norm_gain).astype(jnp.bfloat16)
    normed_g = normed.reshape(length, GROUPS, chans).transpose(1, 0, 2)
    padded = with_halo(normed_g, "seq", 1, half)
    far_piece, padded = lax.optimization_barrier((kernel_fetched[far], padded))
    kernel_fetched = {**near, far: far_piece}
    kernel_swapped = {**near_swapped, **swap_halves({far: far_piece})}
    weights = assemble_shards(kernel, "fsdp", kernel_fetched, kernel_swapped).reshape(GROUPS, chans, KERNEL * chans)
    up_float = upstream[0].astype(jnp.float32)
    up_g = up_float.reshape(length, GROUPS, chans).transpose(1, 0, 2)
    dconv = conv_dconv(padded, weights, up_g)
    dpad = with_halo(dconv, "seq", 1, half)
    dnormed = conv_transpose(dpad, weights, length)
    if seq_count <= GROUPS:
        group_in = lax.all_to_all(normed_g, "seq", 0, 1, tiled=True)
        group_out = lax.all_to_all(dconv, "seq", 0, 1, tiled=True)
    else:
        group_in, group_out = spread_groups(normed, dconv.transpose(1, 0, 2).reshape(length, width), chans)
    local_groups = group_in.shape[0]
    whole = group_in.shape[1]
    group_pad = jnp.pad(group_in, ((0, 0), (half, half), (0, 0)))
    kterms = [
        jnp.einsum("gto,gtc->goc", group_out, group_pad[:, k : k + whole], preferred_element_type=jnp.float32)
        for k in range(KERNEL)
    ]
    kernel_part = jnp.concatenate(kterms, axis=-1).reshape(-1, KERNEL * chans) * scale
    dnormed = dnormed.transpose(1, 0, 2).reshape(length, width)
    gain_term = jnp.sum(dnormed * mixed * inv, axis=0) * scale
    scaled = norm_gain * dnormed
    dmixed = inv * scaled - mixed * inv * inv * inv * jnp.mean(scaled * mixed, axis=-1, keepdims=True)
    input_grad = (up_float + dmixed).astype(jnp.bfloat16)
    kernel_sum = scatter_by_permutes(kernel_part, "fsdp")
    table_grad, gain_grad, kernel_sum = table_and_gain(input_grad, type_ids[0], gain_term, types, scale, kernel_sum)
    kernel_grad = gather_by_permutes(kernel_sum, "fsdp")
    return (input_grad[None], table_grad, gain_grad, kernel_grad)


def solution(mesh):
    return jax.shard_map(
        body,
        mesh=mesh,
        in_specs=(
            P("fsdp", "seq", None),
            P("fsdp", "seq"),
            P("fsdp", None),
            P(),
            P("fsdp", None),
            P("fsdp", "seq", None),
        ),
        out_specs=(
            P("fsdp", "seq", None),
            P(("fsdp", "seq"), None),
            P(("fsdp", "seq")),
            P("seq", None),
        ),
        check_vma=False,
    )
```

```python
import jax
import jax.numpy as jnp
from jax import lax
from jax.experimental import pallas as pl
from jax.experimental.pallas import tpu as pltpu
from jax.sharding import PartitionSpec as P

GROUPS = 16
KERNEL = 9


def with_halo(cells, axis, dim, width):
    count = lax.axis_size(axis)
    ends = count - 1
    head = lax.slice_in_dim(cells, 0, width, axis=dim)
    tail = lax.slice_in_dim(cells, cells.shape[dim] - width, cells.shape[dim], axis=dim)
    return jnp.concatenate(
        [
            lax.ppermute(tail, axis, [(i, (i + 1) % count) for i in range(ends)]),
            cells,
            lax.ppermute(head, axis, [((i + 1) % count, i) for i in range(ends)]),
        ],
        axis=dim,
    )


def from_partner(value, axis, apart):
    mask = 2**apart
    pairs = [(source, source ^ mask) for source in range(lax.axis_size(axis))]
    return lax.ppermute(value, axis, pairs)


def gather_rows(block, axis):
    count = lax.axis_size(axis)
    return lax.all_to_all(jnp.tile(block, (count,) + (1,) * (block.ndim - 1)), axis, 0, 0, tiled=True)


STEP_GROUPS = 8


def forward_kernel(pad_ref, w_ref, up_ref, out_ref):
    length = out_ref.shape[1]
    for g in range(out_ref.shape[0]):
        rows = pad_ref[g].astype(jnp.float32)
        x = jnp.concatenate([rows[k : k + length].astype(jnp.bfloat16) for k in range(KERNEL)], axis=1)
        acc = lax.dot_general(x, w_ref[g], (((1,), (1,)), ((), ())), preferred_element_type=jnp.float32)
        sig = 1.0 / (1.0 + jnp.exp(-acc))
        out_ref[g] = (up_ref[g] * sig * (1.0 + acc * (1.0 - sig))).astype(out_ref.dtype)


def backward_kernel(pad_ref, w_ref, out_ref):
    length = out_ref.shape[1]
    chans = out_ref.shape[2]
    half = KERNEL // 2
    for g in range(out_ref.shape[0]):
        rows = pad_ref[g].astype(jnp.float32)
        x = jnp.concatenate(
            [rows[2 * half - k : 2 * half - k + length].astype(jnp.bfloat16) for k in range(KERNEL)], axis=1
        )
        w = jnp.concatenate([w_ref[g, :, k * chans : (k + 1) * chans] for k in range(KERNEL)], axis=0)
        out_ref[g] = jnp.dot(x, w, preferred_element_type=jnp.float32)


def conv_dconv(padded, weights, up):
    groups, rows, chans = padded.shape
    length = up.shape[1]
    step = STEP_GROUPS if groups % STEP_GROUPS == 0 else 1
    flops = 2 * groups * length * chans * weights.shape[1] * KERNEL
    return pl.pallas_call(
        forward_kernel,
        grid=(groups // step,),
        in_specs=[
            pl.BlockSpec((step, rows, chans), lambda i: (i, 0, 0)),
            pl.BlockSpec((step, weights.shape[1], weights.shape[2]), lambda i: (i, 0, 0)),
            pl.BlockSpec((step, length, up.shape[2]), lambda i: (i, 0, 0)),
        ],
        out_specs=pl.BlockSpec((step, length, up.shape[2]), lambda i: (i, 0, 0)),
        out_shape=jax.ShapeDtypeStruct(up.shape, jnp.bfloat16),
        cost_estimate=pl.CostEstimate(
            flops=flops,
            transcendentals=up.size,
            bytes_accessed=padded.size * 2 + weights.size * 2 + up.size * 6,
        ),
    )(padded, weights, up)


def conv_transpose(dpad, weights, length):
    groups, rows, outs = dpad.shape
    chans = weights.shape[2] // KERNEL
    step = STEP_GROUPS if groups % STEP_GROUPS == 0 else 1
    return pl.pallas_call(
        backward_kernel,
        grid=(groups // step,),
        in_specs=[
            pl.BlockSpec((step, rows, outs), lambda i: (i, 0, 0)),
            pl.BlockSpec((step, weights.shape[1], weights.shape[2]), lambda i: (i, 0, 0)),
        ],
        out_specs=pl.BlockSpec((step, length, chans), lambda i: (i, 0, 0)),
        out_shape=jax.ShapeDtypeStruct((groups, length, chans), jnp.float32),
        cost_estimate=pl.CostEstimate(
            flops=2 * groups * length * chans * outs * KERNEL,
            transcendentals=0,
            bytes_accessed=dpad.size * 2 + weights.size * 2 + groups * length * chans * 4,
        ),
    )(dpad, weights)


def spread_groups(normed, dflat, chans):
    normed_slice = lax.all_to_all(normed, "seq", 1, 0, tiled=True)
    dconv_slice = lax.all_to_all(dflat, "seq", 1, 0, tiled=True)
    whole, slice_width = normed_slice.shape
    spread = chans // slice_width
    position = lax.axis_index("seq")
    group_rows = normed_slice
    for bit in range(spread.bit_length() - 1):
        partner = from_partner(group_rows, "seq", bit)
        lower = position >> bit & 1 == 0
        group_rows = jnp.where(
            lower,
            jnp.concatenate([group_rows, partner], axis=1),
            jnp.concatenate([partner, group_rows], axis=1),
        )
    return group_rows.reshape(1, whole, chans), dconv_slice.reshape(1, whole, slice_width)


def sum_rows(block, axis):
    count = lax.axis_size(axis)
    parts = block.reshape(count, block.shape[0] // count, *block.shape[1:])
    return lax.all_to_all(parts, axis, 0, 0, tiled=True).sum(axis=0)


def psum_rows(block, axis):
    return gather_rows(sum_rows(block, axis), axis)


def table_and_gain(input_grad, ids, gain_term, types, scale, tied):
    every = ("fsdp", "seq")
    count = lax.axis_size("fsdp") * lax.axis_size("seq")
    length, width = input_grad.shape
    narrow = width // count
    id_rows = -(-length // narrow)
    ids_wide = jnp.zeros((id_rows * narrow,), jnp.bfloat16).at[:length].set(ids.astype(jnp.bfloat16))
    send = jnp.concatenate(
        [
            input_grad.reshape(length, count, narrow).transpose(1, 0, 2),
            jnp.broadcast_to(ids_wide.reshape(1, id_rows, narrow), (count, id_rows, narrow)),
        ],
        axis=1,
    )
    got = lax.all_to_all(send, every, 0, 0, tiled=True)
    rows_all = got[:, :length].reshape(count * length, narrow)
    ids_all = got[:, length:].reshape(count, id_rows * narrow)[:, :length].reshape(-1).astype(jnp.int32)
    onehot = (ids_all[:, None] == jnp.arange(types, dtype=jnp.int32)[None, :]).astype(jnp.bfloat16)
    columns = lax.dot_general(onehot, rows_all, (((0,), (0,)), ((), ())), preferred_element_type=jnp.float32)
    columns = columns * scale
    per = types // count
    back = jnp.concatenate(
        [columns.reshape(count, per, narrow), gain_term.reshape(count, 1, narrow)], axis=1
    )
    back, tied = lax.optimization_barrier((back, tied))
    back = lax.all_to_all(back, every, 0, 0, tiled=True)
    table_grad = back[:, :per].transpose(1, 0, 2).reshape(per, width)
    gain_grad = back[:, per].sum(axis=0)
    return table_grad, gain_grad, tied


def scatter_by_permutes(block, axis):
    count = lax.axis_size(axis)
    me = lax.axis_index(axis)
    rows = block.shape[0] // count
    chunk = lambda index: lax.dynamic_slice_in_dim(block, index * rows, rows, axis=0)
    total = chunk(me)
    for apart in range(1, count):
        pairs = [(source, source ^ apart) for source in range(count)]
        total = total + lax.ppermute(chunk(me ^ apart), axis, pairs)
    return total


def gather_by_permutes(total, axis):
    count = lax.axis_size(axis)
    me = lax.axis_index(axis)
    pieces = [total]
    for apart in range(1, count):
        pairs = [(source, source ^ apart) for source in range(count)]
        pieces.append(lax.ppermute(total, axis, pairs))
    stacked = jnp.stack(pieces)
    return jnp.concatenate(
        [lax.dynamic_index_in_dim(stacked, index ^ me, keepdims=False) for index in range(count)], axis=0
    )


def fetch_halves(block, axis):
    count = lax.axis_size(axis)
    core = lax.axis_index("seq") % 2
    half_rows = block.shape[0] // 2
    mine = lax.dynamic_slice_in_dim(block, core * half_rows, half_rows, axis=0)
    return {
        apart: lax.ppermute(mine, axis, [(source, source ^ apart) for source in range(count)])
        for apart in range(count - 1, 0, -1)
    }


def swap_halves(fetched):
    return {apart: from_partner(piece, "seq", 0) for apart, piece in fetched.items()}


def assemble_shards(block, axis, fetched, swapped):
    count = lax.axis_size(axis)
    me = lax.axis_index(axis)
    core = lax.axis_index("seq") % 2
    blocks = [block]
    for apart in range(1, count):
        lower = jnp.where(core == 0, fetched[apart], swapped[apart])
        upper = jnp.where(core == 0, swapped[apart], fetched[apart])
        blocks.append(jnp.concatenate([lower, upper], axis=0))
    stacked = jnp.stack(blocks)
    return jnp.concatenate(
        [lax.dynamic_index_in_dim(stacked, index ^ me, keepdims=False) for index in range(count)], axis=0
    )


def gather_shards(block, axis):
    fetched = fetch_halves(block, axis)
    return assemble_shards(block, axis, fetched, swap_halves(fetched))


def body(events, type_ids, type_table, norm_gain, kernel, upstream):
    length = events.shape[1]
    width = events.shape[2]
    chans = width // GROUPS
    half = KERNEL // 2
    fsdp = lax.axis_size("fsdp")
    seq_count = lax.axis_size("seq")
    total = length * seq_count * fsdp
    scale = 1.0 / jnp.sqrt(jnp.float32(total))
    if fsdp & (fsdp - 1):
        raise ValueError("fsdp not pow2")
    table = gather_shards(type_table, "fsdp")
    kernel_fetched = fetch_halves(kernel, "fsdp")
    far = fsdp - 1
    types = table.shape[0]
    onehot = (type_ids[0][:, None] == jnp.arange(types, dtype=jnp.int32)[None, :]).astype(jnp.bfloat16)
    mixed = events[0].astype(jnp.float32) + jnp.dot(onehot, table, preferred_element_type=jnp.float32)
    near = {apart: piece for apart, piece in kernel_fetched.items() if apart != far}
    near_swapped = swap_halves(near)
    inv = lax.rsqrt(jnp.mean(mixed * mixed, axis=-1, keepdims=True) + 1e-06)
    normed = (mixed * inv * norm_gain).astype(jnp.bfloat16)
    normed_g = normed.reshape(length, GROUPS, chans).transpose(1, 0, 2)
    padded = with_halo(normed_g, "seq", 1, half)
    far_piece, padded = lax.optimization_barrier((kernel_fetched[far], padded))
    kernel_fetched = {**near, far: far_piece}
    kernel_swapped = {**near_swapped, **swap_halves({far: far_piece})}
    weights = assemble_shards(kernel, "fsdp", kernel_fetched, kernel_swapped).reshape(GROUPS, chans, KERNEL * chans)
    up_float = upstream[0].astype(jnp.float32)
    up_g = up_float.reshape(length, GROUPS, chans).transpose(1, 0, 2)
    dconv = conv_dconv(padded, weights, up_g)
    dpad = with_halo(dconv, "seq", 1, half)
    dnormed = conv_transpose(dpad, weights, length)
    if seq_count <= GROUPS:
        group_in = lax.all_to_all(normed_g, "seq", 0, 1, tiled=True)
        group_out = lax.all_to_all(dconv, "seq", 0, 1, tiled=True)
    else:
        group_in, group_out = spread_groups(normed, dconv.transpose(1, 0, 2).reshape(length, width), chans)
    local_groups = group_in.shape[0]
    whole = group_in.shape[1]
    group_pad = jnp.pad(group_in, ((0, 0), (half, half), (0, 0)))
    kterms = [
        jnp.einsum("gto,gtc->goc", group_out, group_pad[:, k : k + whole], preferred_element_type=jnp.float32)
        for k in range(KERNEL)
    ]
    kernel_part = jnp.concatenate(kterms, axis=-1).reshape(-1, KERNEL * chans) * scale
    dnormed = dnormed.transpose(1, 0, 2).reshape(length, width)
    gain_term = jnp.sum(dnormed * mixed * inv, axis=0) * scale
    scaled = norm_gain * dnormed
    dmixed = inv * scaled - mixed * inv * inv * inv * jnp.mean(scaled * mixed, axis=-1, keepdims=True)
    input_grad = (up_float + dmixed).astype(jnp.bfloat16)
    kernel_sum = scatter_by_permutes(kernel_part, "fsdp")
    table_grad, gain_grad, kernel_sum = table_and_gain(input_grad, type_ids[0], gain_term, types, scale, kernel_sum)
    kernel_grad = gather_by_permutes(kernel_sum, "fsdp")
    return (input_grad[None], table_grad, gain_grad, kernel_grad)


def solution(mesh):
    return jax.shard_map(
        body,
        mesh=mesh,
        in_specs=(
            P("fsdp", "seq", None),
            P("fsdp", "seq"),
            P("fsdp", None),
            P(),
            P("fsdp", None),
            P("fsdp", "seq", None),
        ),
        out_specs=(
            P("fsdp", "seq", None),
            P(("fsdp", "seq"), None),
            P(("fsdp", "seq")),
            P("seq", None),
        ),
        check_vma=False,
    )
```

```python
import jax
import jax.numpy as jnp
from jax import lax
from jax.experimental import pallas as pl
from jax.experimental.pallas import tpu as pltpu
from jax.sharding import PartitionSpec as P

GROUPS = 16
KERNEL = 9


def with_halo(cells, axis, dim, width):
    count = lax.axis_size(axis)
    ends = count - 1
    head = lax.slice_in_dim(cells, 0, width, axis=dim)
    tail = lax.slice_in_dim(cells, cells.shape[dim] - width, cells.shape[dim], axis=dim)
    return jnp.concatenate(
        [
            lax.ppermute(tail, axis, [(i, (i + 1) % count) for i in range(ends)]),
            cells,
            lax.ppermute(head, axis, [((i + 1) % count, i) for i in range(ends)]),
        ],
        axis=dim,
    )


def from_partner(value, axis, apart):
    mask = 2**apart
    pairs = [(source, source ^ mask) for source in range(lax.axis_size(axis))]
    return lax.ppermute(value, axis, pairs)


def gather_rows(block, axis):
    count = lax.axis_size(axis)
    return lax.all_to_all(jnp.tile(block, (count,) + (1,) * (block.ndim - 1)), axis, 0, 0, tiled=True)


STEP_GROUPS = 16


def forward_kernel(pad_ref, w_ref, up_ref, out_ref):
    length = out_ref.shape[1]
    for g in range(out_ref.shape[0]):
        rows = pad_ref[g].astype(jnp.float32)
        x = jnp.concatenate([rows[k : k + length].astype(jnp.bfloat16) for k in range(KERNEL)], axis=1)
        acc = lax.dot_general(x, w_ref[g], (((1,), (1,)), ((), ())), preferred_element_type=jnp.float32)
        sig = 1.0 / (1.0 + jnp.exp(-acc))
        out_ref[g] = (up_ref[g] * sig * (1.0 + acc * (1.0 - sig))).astype(out_ref.dtype)


def backward_kernel(pad_ref, w_ref, out_ref):
    length = out_ref.shape[1]
    chans = out_ref.shape[2]
    half = KERNEL // 2
    for g in range(out_ref.shape[0]):
        rows = pad_ref[g].astype(jnp.float32)
        x = jnp.concatenate(
            [rows[2 * half - k : 2 * half - k + length].astype(jnp.bfloat16) for k in range(KERNEL)], axis=1
        )
        w = jnp.concatenate([w_ref[g, :, k * chans : (k + 1) * chans] for k in range(KERNEL)], axis=0)
        out_ref[g] = jnp.dot(x, w, preferred_element_type=jnp.float32)


def conv_dconv(padded, weights, up):
    groups, rows, chans = padded.shape
    length = up.shape[1]
    step = STEP_GROUPS if groups % STEP_GROUPS == 0 else 1
    flops = 2 * groups * length * chans * weights.shape[1] * KERNEL
    return pl.pallas_call(
        forward_kernel,
        grid=(groups // step,),
        in_specs=[
            pl.BlockSpec((step, rows, chans), lambda i: (i, 0, 0)),
            pl.BlockSpec((step, weights.shape[1], weights.shape[2]), lambda i: (i, 0, 0)),
            pl.BlockSpec((step, length, up.shape[2]), lambda i: (i, 0, 0)),
        ],
        out_specs=pl.BlockSpec((step, length, up.shape[2]), lambda i: (i, 0, 0)),
        out_shape=jax.ShapeDtypeStruct(up.shape, jnp.bfloat16),
        cost_estimate=pl.CostEstimate(
            flops=flops,
            transcendentals=up.size,
            bytes_accessed=padded.size * 2 + weights.size * 2 + up.size * 6,
        ),
    )(padded, weights, up)


def conv_transpose(dpad, weights, length):
    groups, rows, outs = dpad.shape
    chans = weights.shape[2] // KERNEL
    step = STEP_GROUPS if groups % STEP_GROUPS == 0 else 1
    return pl.pallas_call(
        backward_kernel,
        grid=(groups // step,),
        in_specs=[
            pl.BlockSpec((step, rows, outs), lambda i: (i, 0, 0)),
            pl.BlockSpec((step, weights.shape[1], weights.shape[2]), lambda i: (i, 0, 0)),
        ],
        out_specs=pl.BlockSpec((step, length, chans), lambda i: (i, 0, 0)),
        out_shape=jax.ShapeDtypeStruct((groups, length, chans), jnp.float32),
        cost_estimate=pl.CostEstimate(
            flops=2 * groups * length * chans * outs * KERNEL,
            transcendentals=0,
            bytes_accessed=dpad.size * 2 + weights.size * 2 + groups * length * chans * 4,
        ),
    )(dpad, weights)


def spread_groups(normed, dflat, chans):
    normed_slice = lax.all_to_all(normed, "seq", 1, 0, tiled=True)
    dconv_slice = lax.all_to_all(dflat, "seq", 1, 0, tiled=True)
    whole, slice_width = normed_slice.shape
    spread = chans // slice_width
    position = lax.axis_index("seq")
    group_rows = normed_slice
    for bit in range(spread.bit_length() - 1):
        partner = from_partner(group_rows, "seq", bit)
        lower = position >> bit & 1 == 0
        group_rows = jnp.where(
            lower,
            jnp.concatenate([group_rows, partner], axis=1),
            jnp.concatenate([partner, group_rows], axis=1),
        )
    return group_rows.reshape(1, whole, chans), dconv_slice.reshape(1, whole, slice_width)


def sum_rows(block, axis):
    count = lax.axis_size(axis)
    parts = block.reshape(count, block.shape[0] // count, *block.shape[1:])
    return lax.all_to_all(parts, axis, 0, 0, tiled=True).sum(axis=0)


def psum_rows(block, axis):
    return gather_rows(sum_rows(block, axis), axis)


def table_and_gain(input_grad, ids, gain_term, types, scale, tied):
    every = ("fsdp", "seq")
    count = lax.axis_size("fsdp") * lax.axis_size("seq")
    length, width = input_grad.shape
    narrow = width // count
    id_rows = -(-length // narrow)
    ids_wide = jnp.zeros((id_rows * narrow,), jnp.bfloat16).at[:length].set(ids.astype(jnp.bfloat16))
    send = jnp.concatenate(
        [
            input_grad.reshape(length, count, narrow).transpose(1, 0, 2),
            jnp.broadcast_to(ids_wide.reshape(1, id_rows, narrow), (count, id_rows, narrow)),
        ],
        axis=1,
    )
    got = lax.all_to_all(send, every, 0, 0, tiled=True)
    rows_all = got[:, :length].reshape(count * length, narrow)
    ids_all = got[:, length:].reshape(count, id_rows * narrow)[:, :length].reshape(-1).astype(jnp.int32)
    onehot = (ids_all[:, None] == jnp.arange(types, dtype=jnp.int32)[None, :]).astype(jnp.bfloat16)
    columns = lax.dot_general(onehot, rows_all, (((0,), (0,)), ((), ())), preferred_element_type=jnp.float32)
    columns = columns * scale
    per = types // count
    back = jnp.concatenate(
        [columns.reshape(count, per, narrow), gain_term.reshape(count, 1, narrow)], axis=1
    )
    back, tied = lax.optimization_barrier((back, tied))
    back = lax.all_to_all(back, every, 0, 0, tiled=True)
    table_grad = back[:, :per].transpose(1, 0, 2).reshape(per, width)
    gain_grad = back[:, per].sum(axis=0)
    return table_grad, gain_grad, tied


def scatter_by_permutes(block, axis):
    count = lax.axis_size(axis)
    me = lax.axis_index(axis)
    rows = block.shape[0] // count
    chunk = lambda index: lax.dynamic_slice_in_dim(block, index * rows, rows, axis=0)
    total = chunk(me)
    for apart in range(1, count):
        pairs = [(source, source ^ apart) for source in range(count)]
        total = total + lax.ppermute(chunk(me ^ apart), axis, pairs)
    return total


def gather_by_permutes(total, axis):
    count = lax.axis_size(axis)
    me = lax.axis_index(axis)
    pieces = [total]
    for apart in range(1, count):
        pairs = [(source, source ^ apart) for source in range(count)]
        pieces.append(lax.ppermute(total, axis, pairs))
    stacked = jnp.stack(pieces)
    return jnp.concatenate(
        [lax.dynamic_index_in_dim(stacked, index ^ me, keepdims=False) for index in range(count)], axis=0
    )


def fetch_halves(block, axis):
    count = lax.axis_size(axis)
    core = lax.axis_index("seq") % 2
    half_rows = block.shape[0] // 2
    mine = lax.dynamic_slice_in_dim(block, core * half_rows, half_rows, axis=0)
    return {
        apart: lax.ppermute(mine, axis, [(source, source ^ apart) for source in range(count)])
        for apart in range(count - 1, 0, -1)
    }


def swap_halves(fetched):
    return {apart: from_partner(piece, "seq", 0) for apart, piece in fetched.items()}


def assemble_shards(block, axis, fetched, swapped):
    count = lax.axis_size(axis)
    me = lax.axis_index(axis)
    core = lax.axis_index("seq") % 2
    blocks = [block]
    for apart in range(1, count):
        lower = jnp.where(core == 0, fetched[apart], swapped[apart])
        upper = jnp.where(core == 0, swapped[apart], fetched[apart])
        blocks.append(jnp.concatenate([lower, upper], axis=0))
    stacked = jnp.stack(blocks)
    return jnp.concatenate(
        [lax.dynamic_index_in_dim(stacked, index ^ me, keepdims=False) for index in range(count)], axis=0
    )


def gather_shards(block, axis):
    fetched = fetch_halves(block, axis)
    return assemble_shards(block, axis, fetched, swap_halves(fetched))


def body(events, type_ids, type_table, norm_gain, kernel, upstream):
    length = events.shape[1]
    width = events.shape[2]
    chans = width // GROUPS
    half = KERNEL // 2
    fsdp = lax.axis_size("fsdp")
    seq_count = lax.axis_size("seq")
    total = length * seq_count * fsdp
    scale = 1.0 / jnp.sqrt(jnp.float32(total))
    if fsdp & (fsdp - 1):
        raise ValueError("fsdp not pow2")
    table = gather_shards(type_table, "fsdp")
    kernel_fetched = fetch_halves(kernel, "fsdp")
    far = fsdp - 1
    types = table.shape[0]
    onehot = (type_ids[0][:, None] == jnp.arange(types, dtype=jnp.int32)[None, :]).astype(jnp.bfloat16)
    mixed = events[0].astype(jnp.float32) + jnp.dot(onehot, table, preferred_element_type=jnp.float32)
    near = {apart: piece for apart, piece in kernel_fetched.items() if apart != far}
    near_swapped = swap_halves(near)
    inv = lax.rsqrt(jnp.mean(mixed * mixed, axis=-1, keepdims=True) + 1e-06)
    normed = (mixed * inv * norm_gain).astype(jnp.bfloat16)
    normed_g = normed.reshape(length, GROUPS, chans).transpose(1, 0, 2)
    padded = with_halo(normed_g, "seq", 1, half)
    far_piece, padded = lax.optimization_barrier((kernel_fetched[far], padded))
    kernel_fetched = {**near, far: far_piece}
    kernel_swapped = {**near_swapped, **swap_halves({far: far_piece})}
    weights = assemble_shards(kernel, "fsdp", kernel_fetched, kernel_swapped).reshape(GROUPS, chans, KERNEL * chans)
    up_float = upstream[0].astype(jnp.float32)
    up_g = up_float.reshape(length, GROUPS, chans).transpose(1, 0, 2)
    dconv = conv_dconv(padded, weights, up_g)
    dpad = with_halo(dconv, "seq", 1, half)
    dnormed = conv_transpose(dpad, weights, length)
    if seq_count <= GROUPS:
        group_in = lax.all_to_all(normed_g, "seq", 0, 1, tiled=True)
        group_out = lax.all_to_all(dconv, "seq", 0, 1, tiled=True)
    else:
        group_in, group_out = spread_groups(normed, dconv.transpose(1, 0, 2).reshape(length, width), chans)
    local_groups = group_in.shape[0]
    whole = group_in.shape[1]
    group_pad = jnp.pad(group_in, ((0, 0), (half, half), (0, 0)))
    kterms = [
        jnp.einsum("gto,gtc->goc", group_out, group_pad[:, k : k + whole], preferred_element_type=jnp.float32)
        for k in range(KERNEL)
    ]
    kernel_part = jnp.concatenate(kterms, axis=-1).reshape(-1, KERNEL * chans) * scale
    dnormed = dnormed.transpose(1, 0, 2).reshape(length, width)
    gain_term = jnp.sum(dnormed * mixed * inv, axis=0) * scale
    scaled = norm_gain * dnormed
    dmixed = inv * scaled - mixed * inv * inv * inv * jnp.mean(scaled * mixed, axis=-1, keepdims=True)
    input_grad = (up_float + dmixed).astype(jnp.bfloat16)
    kernel_sum = scatter_by_permutes(kernel_part, "fsdp")
    table_grad, gain_grad, kernel_sum = table_and_gain(input_grad, type_ids[0], gain_term, types, scale, kernel_sum)
    kernel_grad = gather_by_permutes(kernel_sum, "fsdp")
    return (input_grad[None], table_grad, gain_grad, kernel_grad)


def solution(mesh):
    return jax.shard_map(
        body,
        mesh=mesh,
        in_specs=(
            P("fsdp", "seq", None),
            P("fsdp", "seq"),
            P("fsdp", None),
            P(),
            P("fsdp", None),
            P("fsdp", "seq", None),
        ),
        out_specs=(
            P("fsdp", "seq", None),
            P(("fsdp", "seq"), None),
            P(("fsdp", "seq")),
            P("seq", None),
        ),
        check_vma=False,
    )
```

```python
import jax
import jax.numpy as jnp
from jax import lax
from jax.experimental import pallas as pl
from jax.experimental.pallas import tpu as pltpu
from jax.sharding import PartitionSpec as P

GROUPS = 16
KERNEL = 9


def with_halo(cells, axis, dim, width):
    count = lax.axis_size(axis)
    ends = count - 1
    head = lax.slice_in_dim(cells, 0, width, axis=dim)
    tail = lax.slice_in_dim(cells, cells.shape[dim] - width, cells.shape[dim], axis=dim)
    return jnp.concatenate(
        [
            lax.ppermute(tail, axis, [(i, (i + 1) % count) for i in range(ends)]),
            cells,
            lax.ppermute(head, axis, [((i + 1) % count, i) for i in range(ends)]),
        ],
        axis=dim,
    )


def from_partner(value, axis, apart):
    mask = 2**apart
    pairs = [(source, source ^ mask) for source in range(lax.axis_size(axis))]
    return lax.ppermute(value, axis, pairs)


def gather_rows(block, axis):
    count = lax.axis_size(axis)
    return lax.all_to_all(jnp.tile(block, (count,) + (1,) * (block.ndim - 1)), axis, 0, 0, tiled=True)


STEP_GROUPS = 8


def forward_kernel(pad_ref, w_ref, up_ref, out_ref):
    length = out_ref.shape[1]
    for g in range(out_ref.shape[0]):
        rows = pad_ref[g].astype(jnp.float32)
        x = jnp.concatenate([rows[k : k + length].astype(jnp.bfloat16) for k in range(KERNEL)], axis=1)
        acc = lax.dot_general(x, w_ref[g], (((1,), (1,)), ((), ())), preferred_element_type=jnp.float32)
        sig = 1.0 / (1.0 + jnp.exp(-acc))
        out_ref[g] = (up_ref[g].astype(jnp.float32) * sig * (1.0 + acc * (1.0 - sig))).astype(out_ref.dtype)


def backward_kernel(pad_ref, w_ref, out_ref):
    length = out_ref.shape[1]
    chans = out_ref.shape[2]
    half = KERNEL // 2
    for g in range(out_ref.shape[0]):
        rows = pad_ref[g].astype(jnp.float32)
        x = jnp.concatenate(
            [rows[2 * half - k : 2 * half - k + length].astype(jnp.bfloat16) for k in range(KERNEL)], axis=1
        )
        w = jnp.concatenate([w_ref[g, :, k * chans : (k + 1) * chans] for k in range(KERNEL)], axis=0)
        out_ref[g] = jnp.dot(x, w, preferred_element_type=jnp.float32)


def conv_dconv(padded, weights, up):
    groups, rows, chans = padded.shape
    length = up.shape[1]
    step = STEP_GROUPS if groups % STEP_GROUPS == 0 else 1
    flops = 2 * groups * length * chans * weights.shape[1] * KERNEL
    return pl.pallas_call(
        forward_kernel,
        grid=(groups // step,),
        in_specs=[
            pl.BlockSpec((step, rows, chans), lambda i: (i, 0, 0)),
            pl.BlockSpec((step, weights.shape[1], weights.shape[2]), lambda i: (i, 0, 0)),
            pl.BlockSpec((step, length, up.shape[2]), lambda i: (i, 0, 0)),
        ],
        out_specs=pl.BlockSpec((step, length, up.shape[2]), lambda i: (i, 0, 0)),
        out_shape=jax.ShapeDtypeStruct(up.shape, jnp.bfloat16),
        cost_estimate=pl.CostEstimate(
            flops=flops,
            transcendentals=up.size,
            bytes_accessed=padded.size * 2 + weights.size * 2 + up.size * 4,
        ),
    )(padded, weights, up)


def conv_transpose(dpad, weights, length):
    groups, rows, outs = dpad.shape
    chans = weights.shape[2] // KERNEL
    step = STEP_GROUPS if groups % STEP_GROUPS == 0 else 1
    return pl.pallas_call(
        backward_kernel,
        grid=(groups // step,),
        in_specs=[
            pl.BlockSpec((step, rows, outs), lambda i: (i, 0, 0)),
            pl.BlockSpec((step, weights.shape[1], weights.shape[2]), lambda i: (i, 0, 0)),
        ],
        out_specs=pl.BlockSpec((step, length, chans), lambda i: (i, 0, 0)),
        out_shape=jax.ShapeDtypeStruct((groups, length, chans), jnp.float32),
        cost_estimate=pl.CostEstimate(
            flops=2 * groups * length * chans * outs * KERNEL,
            transcendentals=0,
            bytes_accessed=dpad.size * 2 + weights.size * 2 + groups * length * chans * 4,
        ),
    )(dpad, weights)


def spread_groups(normed, dflat, chans):
    normed_slice = lax.all_to_all(normed, "seq", 1, 0, tiled=True)
    dconv_slice = lax.all_to_all(dflat, "seq", 1, 0, tiled=True)
    whole, slice_width = normed_slice.shape
    spread = chans // slice_width
    position = lax.axis_index("seq")
    group_rows = normed_slice
    for bit in range(spread.bit_length() - 1):
        partner = from_partner(group_rows, "seq", bit)
        lower = position >> bit & 1 == 0
        group_rows = jnp.where(
            lower,
            jnp.concatenate([group_rows, partner], axis=1),
            jnp.concatenate([partner, group_rows], axis=1),
        )
    return group_rows.reshape(1, whole, chans), dconv_slice.reshape(1, whole, slice_width)


def sum_rows(block, axis):
    count = lax.axis_size(axis)
    parts = block.reshape(count, block.shape[0] // count, *block.shape[1:])
    return lax.all_to_all(parts, axis, 0, 0, tiled=True).sum(axis=0)


def psum_rows(block, axis):
    return gather_rows(sum_rows(block, axis), axis)


def table_and_gain(input_grad, ids, gain_term, types, scale, tied):
    every = ("fsdp", "seq")
    count = lax.axis_size("fsdp") * lax.axis_size("seq")
    length, width = input_grad.shape
    narrow = width // count
    id_rows = -(-length // narrow)
    ids_wide = jnp.zeros((id_rows * narrow,), jnp.bfloat16).at[:length].set(ids.astype(jnp.bfloat16))
    send = jnp.concatenate(
        [
            input_grad.reshape(length, count, narrow).transpose(1, 0, 2),
            jnp.broadcast_to(ids_wide.reshape(1, id_rows, narrow), (count, id_rows, narrow)),
        ],
        axis=1,
    )
    got = lax.all_to_all(send, every, 0, 0, tiled=True)
    rows_all = got[:, :length].reshape(count * length, narrow)
    ids_all = got[:, length:].reshape(count, id_rows * narrow)[:, :length].reshape(-1).astype(jnp.int32)
    onehot = (ids_all[:, None] == jnp.arange(types, dtype=jnp.int32)[None, :]).astype(jnp.bfloat16)
    columns = lax.dot_general(onehot, rows_all, (((0,), (0,)), ((), ())), preferred_element_type=jnp.float32)
    columns = columns * scale
    per = types // count
    back = jnp.concatenate(
        [columns.reshape(count, per, narrow), gain_term.reshape(count, 1, narrow)], axis=1
    )
    back, tied = lax.optimization_barrier((back, tied))
    back = lax.all_to_all(back, every, 0, 0, tiled=True)
    table_grad = back[:, :per].transpose(1, 0, 2).reshape(per, width)
    gain_grad = back[:, per].sum(axis=0)
    return table_grad, gain_grad, tied


def scatter_by_permutes(block, axis):
    count = lax.axis_size(axis)
    me = lax.axis_index(axis)
    rows = block.shape[0] // count
    chunk = lambda index: lax.dynamic_slice_in_dim(block, index * rows, rows, axis=0)
    total = chunk(me)
    for apart in range(1, count):
        pairs = [(source, source ^ apart) for source in range(count)]
        total = total + lax.ppermute(chunk(me ^ apart), axis, pairs)
    return total


def gather_by_permutes(total, axis):
    count = lax.axis_size(axis)
    me = lax.axis_index(axis)
    pieces = [total]
    for apart in range(1, count):
        pairs = [(source, source ^ apart) for source in range(count)]
        pieces.append(lax.ppermute(total, axis, pairs))
    stacked = jnp.stack(pieces)
    return jnp.concatenate(
        [lax.dynamic_index_in_dim(stacked, index ^ me, keepdims=False) for index in range(count)], axis=0
    )


def fetch_halves(block, axis):
    count = lax.axis_size(axis)
    core = lax.axis_index("seq") % 2
    half_rows = block.shape[0] // 2
    mine = lax.dynamic_slice_in_dim(block, core * half_rows, half_rows, axis=0)
    return {
        apart: lax.ppermute(mine, axis, [(source, source ^ apart) for source in range(count)])
        for apart in range(count - 1, 0, -1)
    }


def swap_halves(fetched):
    return {apart: from_partner(piece, "seq", 0) for apart, piece in fetched.items()}


def assemble_shards(block, axis, fetched, swapped):
    count = lax.axis_size(axis)
    me = lax.axis_index(axis)
    core = lax.axis_index("seq") % 2
    blocks = [block]
    for apart in range(1, count):
        lower = jnp.where(core == 0, fetched[apart], swapped[apart])
        upper = jnp.where(core == 0, swapped[apart], fetched[apart])
        blocks.append(jnp.concatenate([lower, upper], axis=0))
    stacked = jnp.stack(blocks)
    return jnp.concatenate(
        [lax.dynamic_index_in_dim(stacked, index ^ me, keepdims=False) for index in range(count)], axis=0
    )


def gather_shards(block, axis):
    fetched = fetch_halves(block, axis)
    return assemble_shards(block, axis, fetched, swap_halves(fetched))


def body(events, type_ids, type_table, norm_gain, kernel, upstream):
    length = events.shape[1]
    width = events.shape[2]
    chans = width // GROUPS
    half = KERNEL // 2
    fsdp = lax.axis_size("fsdp")
    seq_count = lax.axis_size("seq")
    total = length * seq_count * fsdp
    scale = 1.0 / jnp.sqrt(jnp.float32(total))
    if fsdp & (fsdp - 1):
        raise ValueError("fsdp not pow2")
    table = gather_shards(type_table, "fsdp")
    kernel_fetched = fetch_halves(kernel, "fsdp")
    far = fsdp - 1
    types = table.shape[0]
    onehot = (type_ids[0][:, None] == jnp.arange(types, dtype=jnp.int32)[None, :]).astype(jnp.bfloat16)
    mixed = events[0].astype(jnp.float32) + jnp.dot(onehot, table, preferred_element_type=jnp.float32)
    near = {apart: piece for apart, piece in kernel_fetched.items() if apart != far}
    near_swapped = swap_halves(near)
    inv = lax.rsqrt(jnp.mean(mixed * mixed, axis=-1, keepdims=True) + 1e-06)
    normed = (mixed * inv * norm_gain).astype(jnp.bfloat16)
    normed_g = normed.reshape(length, GROUPS, chans).transpose(1, 0, 2)
    padded = with_halo(normed_g, "seq", 1, half)
    far_piece, padded = lax.optimization_barrier((kernel_fetched[far], padded))
    kernel_fetched = {**near, far: far_piece}
    kernel_swapped = {**near_swapped, **swap_halves({far: far_piece})}
    weights = assemble_shards(kernel, "fsdp", kernel_fetched, kernel_swapped).reshape(GROUPS, chans, KERNEL * chans)
    up_float = upstream[0].astype(jnp.float32)
    up_g = upstream[0].reshape(length, GROUPS, chans).transpose(1, 0, 2)
    dconv = conv_dconv(padded, weights, up_g)
    dpad = with_halo(dconv, "seq", 1, half)
    dnormed = conv_transpose(dpad, weights, length)
    if seq_count <= GROUPS:
        group_in = lax.all_to_all(normed_g, "seq", 0, 1, tiled=True)
        group_out = lax.all_to_all(dconv, "seq", 0, 1, tiled=True)
    else:
        group_in, group_out = spread_groups(normed, dconv.transpose(1, 0, 2).reshape(length, width), chans)
    local_groups = group_in.shape[0]
    whole = group_in.shape[1]
    group_pad = jnp.pad(group_in, ((0, 0), (half, half), (0, 0)))
    kterms = [
        jnp.einsum("gto,gtc->goc", group_out, group_pad[:, k : k + whole], preferred_element_type=jnp.float32)
        for k in range(KERNEL)
    ]
    kernel_part = jnp.concatenate(kterms, axis=-1).reshape(-1, KERNEL * chans) * scale
    dnormed = dnormed.transpose(1, 0, 2).reshape(length, width)
    gain_term = jnp.sum(dnormed * mixed * inv, axis=0) * scale
    scaled = norm_gain * dnormed
    dmixed = inv * scaled - mixed * inv * inv * inv * jnp.mean(scaled * mixed, axis=-1, keepdims=True)
    input_grad = (up_float + dmixed).astype(jnp.bfloat16)
    kernel_sum = scatter_by_permutes(kernel_part, "fsdp")
    table_grad, gain_grad, kernel_sum = table_and_gain(input_grad, type_ids[0], gain_term, types, scale, kernel_sum)
    kernel_grad = gather_by_permutes(kernel_sum, "fsdp")
    return (input_grad[None], table_grad, gain_grad, kernel_grad)


def solution(mesh):
    return jax.shard_map(
        body,
        mesh=mesh,
        in_specs=(
            P("fsdp", "seq", None),
            P("fsdp", "seq"),
            P("fsdp", None),
            P(),
            P("fsdp", None),
            P("fsdp", "seq", None),
        ),
        out_specs=(
            P("fsdp", "seq", None),
            P(("fsdp", "seq"), None),
            P(("fsdp", "seq")),
            P("seq", None),
        ),
        check_vma=False,
    )
```
